32 devices in a mesh: tile: 16 (over z, x, core), dp: 2 (over y).
Axes of the slice: x: 2, y: 2, z: 4, core: 2. Of those that a mesh axis runs over, the one named last changes fastest.
Arguments:
- fields: bfloat16 [2, 192, 8, 8, 256], P('dp', 'tile'), may hold values from -6 to 6
- weight_one: bfloat16 [9, 256, 256], replicated, may hold values from -0.125 to 0.125
- weight_two: bfloat16 [9, 256, 256], replicated, may hold values from -0.125 to 0.125
- cotangent: bfloat16 [2, 192, 8, 8, 256], P('dp', 'tile'), may hold values from -6 to 6
- face_links: int32 [12, 4, 3], replicated, may hold values from 0 to 11, as said below
- face_order: int32 [12], replicated, may hold values from 0 to 11, each once
Outputs:
- block_output: bfloat16 [2, 192, 8, 8, 256], P('dp', 'tile')
- field_grad: bfloat16 [2, 192, 8, 8, 256], P('dp', 'tile')
- grad_one: float32 [9, 256, 256], replicated
- grad_two: float32 [9, 256, 256], replicated
The draws below stay inside these ranges and needn't reach their ends.
Inputs may be any that keep to these rules, and one draw needn't show every extreme that they name: face_links[f, s, 0] is a face number, and each face appears once among face_links[., s, 0] for every side s; face_links[f, s, 1] and face_links[f, s, 2] are 0 or 1. `face_order`: a permutation of the 12 faces.
All inputs are finite; a program needn't handle non-finite values.
Results may differ from the reference program's by a relative error of at most 0.009.
Values may be sent and summed in bfloat16 or wider, within the bound.
No kernel may reach another device: no remote copies, remote signals or barrier semaphores. Data moves between devices by JAX's collectives and lax.ppermute only.
A program may use at most 128 MiB of HBM per device.

```python
import math
from functools import partial
import jax
import jax.numpy as jnp
from jax import lax

CHANNELS = 256
TILE = 8
GRID = 4
HALVES = 1
FACES_DEV = 12
TILES = 192
NSIDE = 32
SAMPLES = 2


def draw_face_links(key, part):
    streams = jax.random.split(key, 3)
    numbers = jnp.arange(12, dtype=jnp.int32)
    across = jnp.stack([jax.random.permutation(jax.random.fold_in(streams[0], which_side), numbers) for which_side in range(4)], axis=1)
    edge_mode = jax.random.randint(streams[1], (12, 4), 0, 2, dtype=jnp.int32)
    reversed_flag = jax.random.randint(streams[2], (12, 4), 0, 2, dtype=jnp.int32)
    return jnp.stack([across, edge_mode, reversed_flag], axis=2).astype(jnp.int32)


def shard_levels(own_key, shape, shards, least, largest):
    def one(position, blocks):
        steps = jax.random.uniform(jax.random.fold_in(jax.random.fold_in(own_key, 6), position), (blocks,), jnp.float32, least / len(shards), largest / len(shards))
        return jnp.repeat(jnp.exp(steps), shape[position] // blocks).reshape((-1,) + (1,) * (len(shape) - position - 1))

    gain = one(*shards[0])
    for cut in shards[1:]:
        gain = gain * one(*cut)
    return gain


def bell_draw(stream_key, dims, width, reach, cuts=(), kind=jnp.bfloat16):
    factor_of = shard_levels(stream_key, dims, cuts, -0.22, 0.18) if cuts else 1.0
    values = jax.random.normal(stream_key, dims, jnp.float32) * width * factor_of
    return jnp.minimum(jnp.maximum(values, -reach), reach).astype(kind)


def setup_inputs(seed: int = 0) -> dict:
    streams_of = jax.random.split(jax.random.key(seed), 7)
    fields = bell_draw(streams_of[0], (SAMPLES, TILES, TILE, TILE, CHANNELS), 1.0, 6.0, ((0, 2), (1, 16)))
    weight_one = bell_draw(streams_of[1], (9, CHANNELS, CHANNELS), (9 * CHANNELS) ** -0.5, 0.125)
    weight_two = bell_draw(streams_of[2], (9, CHANNELS, CHANNELS), (9 * CHANNELS) ** -0.5, 0.125)
    cotangent = bell_draw(streams_of[3], (SAMPLES, TILES, TILE, TILE, CHANNELS), 1.0, 6.0, ((0, 2), (1, 16)))
    face_links = draw_face_links(jax.random.fold_in(streams_of[6], 71), 0)
    face_order = jax.random.permutation(streams_of[5], 12).astype(jnp.int32)
    return {"fields": fields, "weight_one": weight_one, "weight_two": weight_two, "cotangent": cotangent, "face_links": face_links, "face_order": face_order}


def to_faces(slots, face_order):
    sample_count = slots.shape[0]
    arranged = slots.reshape(sample_count, HALVES, GRID, GRID, FACES_DEV, TILE, TILE, CHANNELS)
    arranged = arranged.transpose(0, 1, 4, 2, 5, 3, 6, 7).reshape(sample_count, 12, NSIDE, NSIDE, CHANNELS)
    lookup = jnp.arange(12, dtype=jnp.int32)
    inverse = lax.optimization_barrier(jnp.sum(lookup[None, :] * (face_order[None, :] == lookup[:, None]).astype(jnp.int32), axis=1)).astype(jnp.int32)
    return jnp.take(arranged, inverse, axis=1)

def from_faces(faces, face_order):
    sample_count = faces.shape[0]
    arranged = jnp.take(faces, face_order, axis=1)
    arranged = arranged.reshape(sample_count, HALVES, FACES_DEV, GRID, TILE, GRID, TILE, CHANNELS)
    return arranged.transpose(0, 1, 3, 5, 2, 4, 6, 7).reshape(sample_count, TILES, TILE, TILE, CHANNELS)

def pad_faces(faces, face_links):
    extent = faces.shape[2]
    edges = [faces[:, :, 0], faces[:, :, extent - 1], faces[:, :, :, 0], faces[:, :, :, extent - 1]]
    opposite = [1, 0, 3, 2]
    strips = []
    for which_side in range(4):
        link_rows = face_links[:, which_side]
        far_edge = jnp.take(edges[opposite[which_side]], link_rows[:, 0], axis=1)
        near_edge = jnp.take(edges[which_side], link_rows[:, 0], axis=1)
        chosen = jnp.where((link_rows[:, 1] == 0)[None, :, None, None], far_edge, near_edge)
        strips.append(jnp.where((link_rows[:, 2] == 1)[None, :, None, None], chosen[:, :, ::-1], chosen))
    widened = jnp.concatenate([strips[2][:, :, :, None], faces, strips[3][:, :, :, None]], axis=3)
    corner_zero = jnp.zeros(faces.shape[:2] + (1, faces.shape[-1]), faces.dtype)
    top_rim = jnp.concatenate([corner_zero, strips[0], corner_zero], axis=2)
    bottom_rim = jnp.concatenate([corner_zero, strips[1], corner_zero], axis=2)
    return jnp.concatenate([top_rim[:, :, None], widened, bottom_rim[:, :, None]], axis=2)

def convolve(padded, weight):
    extent = padded.shape[-2] - 2
    summed = None
    for offset in range(9):
        row_offset, col_offset = (offset // 3, offset % 3)
        window = padded[..., row_offset:row_offset + extent, col_offset:col_offset + extent, :]
        product = jnp.dot(window, weight[offset], preferred_element_type=jnp.float32)
        summed = product if summed is None else summed + product
    return summed

def convolve_back(grad, weight):
    extent = grad.shape[-2]
    result = jnp.zeros(grad.shape[:-3] + (extent + 2, extent + 2, grad.shape[-1]), jnp.float32)
    for offset in range(9):
        row_offset, col_offset = (offset // 3, offset % 3)
        product = lax.dot_general(grad, weight[offset], (((grad.ndim - 1,), (1,)), ((), ())), preferred_element_type=jnp.float32)
        result = result.at[..., row_offset:row_offset + extent, col_offset:col_offset + extent, :].add(product)
    return result

def weight_grad(padded, grad):
    extent = grad.shape[-2]
    channels = grad.shape[-1]
    flat_grad = grad.reshape(-1, channels)
    pieces = []
    for offset in range(9):
        row_offset, col_offset = (offset // 3, offset % 3)
        window = padded[..., row_offset:row_offset + extent, col_offset:col_offset + extent, :].reshape(-1, channels)
        pieces.append(lax.dot_general(window, flat_grad, (((0,), (0,)), ((), ())), preferred_element_type=jnp.float32))
    return jnp.stack(pieces, axis=0)

def reference(fields, weight_one, weight_two, cotangent, face_links, face_order):
    pad_now = partial(pad_faces, face_links=face_links)
    faces_in = to_faces(fields, face_order)
    padded_in = pad_now(faces_in)
    pre_act = convolve(padded_in, weight_one)
    hidden = jax.nn.gelu(pre_act, approximate=True).astype(jnp.bfloat16)
    padded_hidden = pad_now(hidden)
    second = convolve(padded_hidden, weight_two)
    block_output = (faces_in.astype(jnp.float32) + second).astype(jnp.bfloat16)
    grad_out = to_faces(cotangent, face_order)
    grad_scale = 1.0 / math.sqrt(SAMPLES * 12 * NSIDE * NSIDE)
    grad_two = weight_grad(padded_hidden, grad_out) * grad_scale
    rim_two = convolve_back(grad_out, weight_two).astype(jnp.bfloat16)
    rim_two = lax.optimization_barrier(rim_two).astype(jnp.float32)
    zero_faces = jnp.zeros(faces_in.shape, jnp.float32)
    pad_pair = jax.vjp(pad_now, zero_faces)
    pad_adjoint = pad_pair[1]
    grad_hidden = pad_adjoint(rim_two)[0]
    gelu_pair = jax.vjp(partial(jax.nn.gelu, approximate=True), pre_act)
    grad_pre = gelu_pair[1](grad_hidden)[0].astype(jnp.bfloat16)
    grad_one = weight_grad(padded_in, grad_pre) * grad_scale
    rim_one = convolve_back(grad_pre, weight_one).astype(jnp.bfloat16)
    rim_one = lax.optimization_barrier(rim_one).astype(jnp.float32)
    field_grad = (grad_out.astype(jnp.float32) + pad_adjoint(rim_one)[0]).astype(jnp.bfloat16)
    return (from_faces(block_output, face_order), from_faces(field_grad, face_order), grad_one, grad_two)
```

```python
from functools import partial
import math

import jax
import jax.numpy as jnp
from jax import lax
from jax.sharding import PartitionSpec as P


def shortened(shard):
    return jax.tree.map(lambda a: a.astype(jnp.bfloat16) if a.dtype == jnp.float32 else a, shard)


def from_behind(value, axis, steps):
    count = lax.axis_size(axis)
    first, last = (max(0, -steps), min(count, count - steps))
    return lax.ppermute(value, axis, [(source, source + steps) for source in range(first, last)])


def swapped(shard, axis, apart):
    return lax.ppermute(shard, axis, [(i, i ^ 1 << apart) for i in range(lax.axis_size(axis))])


def send_rim(values, offset):
    return jax.tree.map(
        lambda part, own: part.astype(own.dtype),
        from_behind(shortened(values), "tile", offset),
        values,
    )


def swap_rim(values, bit_index):
    return jax.tree.map(
        lambda part, own: part.astype(own.dtype),
        swapped(shortened(values), "tile", bit_index),
        values,
    )


def send_back(values, offset):
    return jax.tree.map(
        lambda part, own: part.astype(own.dtype),
        from_behind(shortened(values), "tile", offset),
        values,
    )


def swap_back(values, bit_index):
    return jax.tree.map(
        lambda part, own: part.astype(own.dtype),
        swapped(shortened(values), "tile", bit_index),
        values,
    )


def link_table(face_order, face_links, my_half, face_count, which_side):
    lookup = jnp.arange(face_order.shape[0], dtype=jnp.int32)
    inverse = jnp.sum(
        lookup[None, :] * (face_order[None, :] == lookup[:, None]).astype(jnp.int32), axis=1
    ).astype(jnp.int32)
    face_ids = lax.dynamic_slice_in_dim(face_order, my_half * face_count, face_count)
    link_rows = jnp.take(face_links, face_ids, axis=0)[:, which_side]
    source = jnp.take(inverse, link_rows[:, 0])
    remote = source // face_count != my_half
    candidate = which_side % 2 * 2 + link_rows[:, 1]
    pick_index = ((link_rows[:, 2] * 4 + candidate) * face_count + source % face_count).astype(
        jnp.int32
    )
    return (pick_index, remote, link_rows[:, 2] == 1)


def make_plan(
    face_order,
    face_links,
    my_half,
    halves,
    face_count,
    grid_side,
    step_size,
    mirror_bits,
    side_pair,
    device_pos,
    along_pos,
    mask_ends,
    half_bit,
):
    plan = {
        "step": step_size,
        "far": (grid_side - 1) * step_size,
        "bits": mirror_bits,
        "half_bit": half_bit,
        "halves": halves,
        "device_pos": device_pos,
        "along_pos": along_pos,
        "grid_side": grid_side,
        "ends": mask_ends,
    }
    for label_name, which_side in (("lower", side_pair[0]), ("upper", side_pair[1])):
        plan[label_name] = link_table(face_order, face_links, my_half, face_count, which_side)
        if halves == 2:
            plan[label_name + "_partner"] = link_table(
                face_order, face_links, 1 - my_half, face_count, which_side
            )
    return plan


def end_mask(plan, length):
    positions = jnp.arange(length)
    along_pos = plan["along_pos"]
    cut_cells = (positions == 0) & (along_pos == 0) | (positions == length - 1) & (
        along_pos == plan["grid_side"] - 1
    )
    return jnp.logical_not(cut_cells)[None, :, None]


def orient(rim_strip, reverse, plan):
    turned = jnp.where(reverse[:, None, None], rim_strip[:, ::-1], rim_strip)
    if plan["ends"]:
        turned = jnp.where(end_mask(plan, rim_strip.shape[1]), turned, jnp.zeros_like(turned))
    return turned


def orient_back(rim_strip, reverse, plan):
    masked = rim_strip
    if plan["ends"]:
        masked = jnp.where(end_mask(plan, rim_strip.shape[1]), masked, jnp.zeros_like(masked))
    return jnp.where(reverse[:, None, None], masked[:, ::-1], masked)


def pick_links(stacked, plan):
    index_lower, remote_lower = (plan["lower"][0], plan["lower"][1])
    index_upper, remote_upper = (plan["upper"][0], plan["upper"][1])
    own_lower = jnp.take(stacked, index_lower, axis=0)
    own_upper = jnp.take(stacked, index_upper, axis=0)
    if plan["halves"] == 1:
        return (own_lower, own_upper)
    partner = swap_rim(stacked, plan["half_bit"])
    got_lower = jnp.take(partner, index_lower, axis=0)
    got_upper = jnp.take(partner, index_upper, axis=0)
    return (
        jnp.where(remote_lower[:, None, None], got_lower, own_lower),
        jnp.where(remote_upper[:, None, None], got_upper, own_upper),
    )


def pick_back(grad_lower, grad_upper, plan):
    index_lower, remote_lower = (plan["lower"][0], plan["lower"][1])
    index_upper, remote_upper = (plan["upper"][0], plan["upper"][1])
    blank_rows = jnp.zeros((8 * grad_lower.shape[0],) + grad_lower.shape[1:], jnp.float32)
    if plan["halves"] == 1:
        return blank_rows.at[index_lower].add(grad_lower).at[index_upper].add(grad_upper)
    stay_lower = jnp.where(remote_lower[:, None, None], 0.0, grad_lower)
    away_lower = jnp.where(remote_lower[:, None, None], grad_lower, 0.0)
    stay_upper = jnp.where(remote_upper[:, None, None], 0.0, grad_upper)
    away_upper = jnp.where(remote_upper[:, None, None], grad_upper, 0.0)
    summed = blank_rows.at[index_lower].add(stay_lower).at[index_upper].add(stay_upper)
    partner = blank_rows.at[index_lower].add(away_lower).at[index_upper].add(away_upper)
    summed = summed + swap_back(partner, plan["half_bit"])
    return summed


def near_far(lower_edge, upper_edge, plan):
    step_size = plan["step"]
    far_step = plan["far"]
    near_lower = send_rim(upper_edge, step_size)
    near_upper = send_rim(lower_edge, -step_size)
    far_lower = send_rim(upper_edge, -far_step)
    far_upper = send_rim(lower_edge, far_step)
    return (
        near_lower,
        near_upper,
        jnp.concatenate([far_lower, lower_edge, far_upper, upper_edge], axis=0),
    )


def rim_forward(lower_edge, upper_edge, plan):
    near_lower, near_upper, direct = near_far(lower_edge, upper_edge, plan)
    device_pos = plan["device_pos"]
    at_lower = device_pos == 0
    at_upper = device_pos == plan["grid_side"] - 1
    mirrored = direct
    for bit_index in plan["bits"]:
        mirrored = swap_rim(mirrored, bit_index)
    stacked = jnp.concatenate([direct, mirrored], axis=0)
    link_lower, link_upper = pick_links(stacked, plan)
    link_lower = orient(link_lower, plan["lower"][2], plan)
    link_upper = orient(link_upper, plan["upper"][2], plan)
    lower_rim = jnp.where(at_lower, link_lower, near_lower)
    upper_rim = jnp.where(at_upper, link_upper, near_upper)
    return (lower_rim, upper_rim)


def rim_backward(grad_lower, grad_upper, plan):
    step_size = plan["step"]
    far_step = plan["far"]
    at_lower = plan["device_pos"] == 0
    at_upper = plan["device_pos"] == plan["grid_side"] - 1
    near_lower = jnp.where(at_lower, 0.0, grad_lower)
    near_upper = jnp.where(at_upper, 0.0, grad_upper)
    face_count = grad_lower.shape[0]
    link_lower = orient_back(jnp.where(at_lower, grad_lower, 0.0), plan["lower"][2], plan)
    link_upper = orient_back(jnp.where(at_upper, grad_upper, 0.0), plan["upper"][2], plan)
    stacked = pick_back(link_lower, link_upper, plan)
    half_rows = stacked.shape[0] // 2
    direct = stacked[:half_rows]
    mirrored = stacked[half_rows:]
    for bit_index in plan["bits"]:
        mirrored = swap_back(mirrored, bit_index)
    direct = direct + mirrored
    far_lower = direct[:face_count]
    own_lower = direct[face_count : 2 * face_count]
    far_upper = direct[2 * face_count : 3 * face_count]
    own_upper = direct[3 * face_count :]
    grad_upper_edge = own_upper + send_back(near_lower, -step_size) + send_back(far_lower, far_step)
    grad_lower_edge = own_lower + send_back(near_upper, step_size) + send_back(far_upper, -far_step)
    return (grad_lower_edge, grad_upper_edge)


def pad_tiles(local_tiles, rim_plans):
    column_plan, row_plan = rim_plans
    side_lower, side_upper = rim_forward(local_tiles[:, :, 0], local_tiles[:, :, -1], column_plan)
    widened = jnp.concatenate([side_lower[:, :, None], local_tiles, side_upper[:, :, None]], axis=2)
    top_rim, bottom_rim = rim_forward(widened[:, 0], widened[:, -1], row_plan)
    return jnp.concatenate([top_rim[:, None], widened, bottom_rim[:, None]], axis=1)


def pad_back(grad, rim_plans):
    column_plan, row_plan = rim_plans
    top_edge, bottom_edge = rim_backward(grad[:, 0], grad[:, -1], row_plan)
    widened = grad[:, 1:-1]
    widened = widened.at[:, 0].add(top_edge).at[:, -1].add(bottom_edge)
    left_edge, right_edge = rim_backward(widened[:, :, 0], widened[:, :, -1], column_plan)
    interior = widened[:, :, 1:-1]
    return interior.at[:, :, 0].add(left_edge).at[:, :, -1].add(right_edge)


def convolve(padded, weight):
    channels = weight.shape[-1]
    kernel = weight.reshape(3, 3, weight.shape[1], channels)
    return lax.conv_general_dilated(
        padded,
        kernel,
        (1, 1),
        "VALID",
        dimension_numbers=("NHWC", "HWIO", "NHWC"),
        preferred_element_type=jnp.float32,
    )


def convolve_back(grad, weight):
    kernel = weight.reshape(3, 3, weight.shape[1], weight.shape[2])[::-1, ::-1]
    return lax.conv_general_dilated(
        grad,
        kernel,
        (1, 1),
        ((2, 2), (2, 2)),
        dimension_numbers=("NHWC", "HWOI", "NHWC"),
        preferred_element_type=jnp.float32,
    )


def weight_grad(padded, grad):
    summed = lax.conv_general_dilated(
        padded,
        grad,
        (1, 1),
        "VALID",
        dimension_numbers=("CHWN", "IHWO", "HWNC"),
        preferred_element_type=jnp.float32,
    )
    return summed.reshape((9,) + summed.shape[2:])


def local(fields, weight_one, weight_two, cotangent, face_links, face_order):
    local_tiles = fields[0]
    face_count = local_tiles.shape[0]
    extent = local_tiles.shape[1]
    devices = lax.axis_size("tile")
    grid_side = math.isqrt(devices * face_count // 12)
    halves = devices // (grid_side * grid_side)
    levels = grid_side.bit_length() - 1
    device = lax.axis_index("tile")
    my_half = device // (grid_side * grid_side)
    grid_row = device // grid_side % grid_side
    grid_col = device % grid_side
    column_plan = make_plan(
        face_order,
        face_links,
        my_half,
        halves,
        face_count,
        grid_side,
        1,
        list(range(levels, 2 * levels)),
        (2, 3),
        grid_col,
        grid_row,
        False,
        2 * levels,
    )
    row_plan = make_plan(
        face_order,
        face_links,
        my_half,
        halves,
        face_count,
        grid_side,
        grid_side,
        list(range(levels)),
        (0, 1),
        grid_row,
        grid_col,
        True,
        2 * levels,
    )
    rim_plans = (column_plan, row_plan)
    padded_in = pad_tiles(local_tiles, rim_plans)
    pre_act = convolve(padded_in, weight_one)
    hidden = jax.nn.gelu(pre_act, approximate=True).astype(jnp.bfloat16)
    padded_hidden = pad_tiles(hidden, rim_plans)
    second = convolve(padded_hidden, weight_two)
    block_output = (local_tiles.astype(jnp.float32) + second).astype(jnp.bfloat16)
    grad_out = cotangent[0]
    grad_scale = 1.0 / math.sqrt(lax.axis_size("dp") * 12 * (grid_side * extent) ** 2)
    local_two = weight_grad(padded_hidden, grad_out) * grad_scale
    grad_two = lax.psum(local_two, ("tile", "dp"))
    rim_two = convolve_back(grad_out, weight_two).astype(jnp.bfloat16)
    rim_two = lax.optimization_barrier(rim_two).astype(jnp.float32)
    grad_hidden = pad_back(rim_two, rim_plans)
    gelu_pair = jax.vjp(partial(jax.nn.gelu, approximate=True), pre_act)
    grad_pre = gelu_pair[1](grad_hidden)[0].astype(jnp.bfloat16)
    local_one = weight_grad(padded_in, grad_pre) * grad_scale
    rim_one = convolve_back(grad_pre, weight_one).astype(jnp.bfloat16)
    rim_one = lax.optimization_barrier(rim_one).astype(jnp.float32)
    field_grad = (grad_out.astype(jnp.float32) + pad_back(rim_one, rim_plans)).astype(jnp.bfloat16)
    grad_two, local_one = lax.optimization_barrier((grad_two, local_one))
    grad_one = lax.psum(local_one, ("tile", "dp"))
    return (block_output[None], field_grad[None], grad_one, grad_two)


def solution(mesh):
    in_specs = (
        P("dp", "tile", None, None, None),
        P(),
        P(),
        P("dp", "tile", None, None, None),
        P(),
        P(),
    )
    out_specs = (P("dp", "tile", None, None, None), P("dp", "tile", None, None, None), P(), P())
    return jax.shard_map(local, mesh=mesh, in_specs=in_specs, out_specs=out_specs, check_vma=False)
```

```python
from functools import partial
import math

import jax
import jax.numpy as jnp
from jax import lax
from jax.sharding import PartitionSpec as P


def shortened(shard):
    return jax.tree.map(lambda a: a.astype(jnp.bfloat16) if a.dtype == jnp.float32 else a, shard)


def from_behind(value, axis, steps):
    count = lax.axis_size(axis)
    first, last = (max(0, -steps), min(count, count - steps))
    return lax.ppermute(value, axis, [(source, source + steps) for source in range(first, last)])


def swapped(shard, axis, apart):
    return lax.ppermute(shard, axis, [(i, i ^ 1 << apart) for i in range(lax.axis_size(axis))])


def send_rim(values, offset):
    return jax.tree.map(
        lambda part, own: part.astype(own.dtype),
        from_behind(shortened(values), "tile", offset),
        values,
    )


def swap_rim(values, bit_index):
    return jax.tree.map(
        lambda part, own: part.astype(own.dtype),
        swapped(shortened(values), "tile", bit_index),
        values,
    )


def send_back(values, offset):
    return jax.tree.map(
        lambda part, own: part.astype(own.dtype),
        from_behind(shortened(values), "tile", offset),
        values,
    )


def swap_back(values, bit_index):
    return jax.tree.map(
        lambda part, own: part.astype(own.dtype),
        swapped(shortened(values), "tile", bit_index),
        values,
    )


def link_table(face_order, face_links, my_half, face_count, which_side):
    lookup = jnp.arange(face_order.shape[0], dtype=jnp.int32)
    inverse = jnp.sum(
        lookup[None, :] * (face_order[None, :] == lookup[:, None]).astype(jnp.int32), axis=1
    ).astype(jnp.int32)
    face_ids = lax.dynamic_slice_in_dim(face_order, my_half * face_count, face_count)
    link_rows = jnp.take(face_links, face_ids, axis=0)[:, which_side]
    source = jnp.take(inverse, link_rows[:, 0])
    remote = source // face_count != my_half
    candidate = which_side % 2 * 2 + link_rows[:, 1]
    pick_index = ((link_rows[:, 2] * 4 + candidate) * face_count + source % face_count).astype(
        jnp.int32
    )
    return (pick_index, remote, link_rows[:, 2] == 1)


def make_plan(
    face_order,
    face_links,
    my_half,
    halves,
    face_count,
    grid_side,
    step_size,
    mirror_bits,
    side_pair,
    device_pos,
    along_pos,
    mask_ends,
    half_bit,
):
    plan = {
        "step": step_size,
        "far": (grid_side - 1) * step_size,
        "bits": mirror_bits,
        "half_bit": half_bit,
        "halves": halves,
        "device_pos": device_pos,
        "along_pos": along_pos,
        "grid_side": grid_side,
        "ends": mask_ends,
    }
    for label_name, which_side in (("lower", side_pair[0]), ("upper", side_pair[1])):
        plan[label_name] = link_table(face_order, face_links, my_half, face_count, which_side)
        if halves == 2:
            plan[label_name + "_partner"] = link_table(
                face_order, face_links, 1 - my_half, face_count, which_side
            )
    return plan


def end_mask(plan, length):
    positions = jnp.arange(length)
    along_pos = plan["along_pos"]
    cut_cells = (positions == 0) & (along_pos == 0) | (positions == length - 1) & (
        along_pos == plan["grid_side"] - 1
    )
    return jnp.logical_not(cut_cells)[None, :, None]


def orient(rim_strip, reverse, plan):
    turned = jnp.where(reverse[:, None, None], rim_strip[:, ::-1], rim_strip)
    if plan["ends"]:
        turned = jnp.where(end_mask(plan, rim_strip.shape[1]), turned, jnp.zeros_like(turned))
    return turned


def orient_back(rim_strip, reverse, plan):
    masked = rim_strip
    if plan["ends"]:
        masked = jnp.where(end_mask(plan, rim_strip.shape[1]), masked, jnp.zeros_like(masked))
    return jnp.where(reverse[:, None, None], masked[:, ::-1], masked)


def pick_links(stacked, plan):
    index_lower, remote_lower = (plan["lower"][0], plan["lower"][1])
    index_upper, remote_upper = (plan["upper"][0], plan["upper"][1])
    own_lower = jnp.take(stacked, index_lower, axis=0)
    own_upper = jnp.take(stacked, index_upper, axis=0)
    if plan["halves"] == 1:
        return (own_lower, own_upper)
    partner = swap_rim(stacked, plan["half_bit"])
    got_lower = jnp.take(partner, index_lower, axis=0)
    got_upper = jnp.take(partner, index_upper, axis=0)
    return (
        jnp.where(remote_lower[:, None, None], got_lower, own_lower),
        jnp.where(remote_upper[:, None, None], got_upper, own_upper),
    )


def pick_back(grad_lower, grad_upper, plan):
    index_lower, remote_lower = (plan["lower"][0], plan["lower"][1])
    index_upper, remote_upper = (plan["upper"][0], plan["upper"][1])
    blank_rows = jnp.zeros((8 * grad_lower.shape[0],) + grad_lower.shape[1:], jnp.float32)
    if plan["halves"] == 1:
        return blank_rows.at[index_lower].add(grad_lower).at[index_upper].add(grad_upper)
    stay_lower = jnp.where(remote_lower[:, None, None], 0.0, grad_lower)
    away_lower = jnp.where(remote_lower[:, None, None], grad_lower, 0.0)
    stay_upper = jnp.where(remote_upper[:, None, None], 0.0, grad_upper)
    away_upper = jnp.where(remote_upper[:, None, None], grad_upper, 0.0)
    summed = blank_rows.at[index_lower].add(stay_lower).at[index_upper].add(stay_upper)
    partner = blank_rows.at[index_lower].add(away_lower).at[index_upper].add(away_upper)
    summed = summed + swap_back(partner, plan["half_bit"])
    return summed


def cycled(value, plan, shift):
    count = lax.axis_size("tile")
    step_size, grid_side = (plan["step"], plan["grid_side"])
    pairs = []
    for source in range(count):
        position = source // step_size % grid_side
        moved = (position + shift) % grid_side
        pairs.append((source, source + (moved - position) * step_size))
    return lax.ppermute(value, "tile", pairs)


def mirror_masks(plan):
    mirror = sum(1 << bit_index for bit_index in plan["bits"])
    along = (plan["grid_side"] - 1) * plan["step"]
    return (mirror, mirror ^ along)


def xor_send(values, mask):
    count = lax.axis_size("tile")
    pairs = [(source, source ^ mask) for source in range(count)]
    joined = jnp.concatenate(values, axis=0)
    moved = lax.ppermute(shortened(joined), "tile", pairs).astype(joined.dtype)
    return jnp.split(moved, len(values), axis=0)


def shift_send(value, plan, shift):
    return cycled(shortened(value), plan, shift).astype(value.dtype)


def rim_forward(lower_edge, upper_edge, plan):
    row_mask, both_mask = mirror_masks(plan)
    from_lower = shift_send(upper_edge, plan, 1)
    from_upper = shift_send(lower_edge, plan, -1)
    row_lower, row_upper = xor_send((lower_edge, upper_edge), row_mask)
    both_lower, both_upper = xor_send((lower_edge, upper_edge), both_mask)
    device_pos = plan["device_pos"]
    at_lower = device_pos == 0
    at_upper = device_pos == plan["grid_side"] - 1
    stacked = jnp.concatenate(
        [from_lower, lower_edge, from_upper, upper_edge, both_upper, row_lower, both_lower, row_upper],
        axis=0,
    )
    link_lower, link_upper = pick_links(stacked, plan)
    link_lower = orient(link_lower, plan["lower"][2], plan)
    link_upper = orient(link_upper, plan["upper"][2], plan)
    lower_rim = jnp.where(at_lower, link_lower, from_lower)
    upper_rim = jnp.where(at_upper, link_upper, from_upper)
    return (lower_rim, upper_rim)


def rim_backward(grad_lower, grad_upper, plan):
    row_mask, both_mask = mirror_masks(plan)
    at_lower = plan["device_pos"] == 0
    at_upper = plan["device_pos"] == plan["grid_side"] - 1
    near_lower = jnp.where(at_lower, 0.0, grad_lower)
    near_upper = jnp.where(at_upper, 0.0, grad_upper)
    face_count = grad_lower.shape[0]
    link_lower = orient_back(jnp.where(at_lower, grad_lower, 0.0), plan["lower"][2], plan)
    link_upper = orient_back(jnp.where(at_upper, grad_upper, 0.0), plan["upper"][2], plan)
    stacked = pick_back(link_lower, link_upper, plan)
    parts = [stacked[k * face_count : (k + 1) * face_count] for k in range(8)]
    to_lower = shift_send(near_lower + parts[0], plan, -1)
    to_upper = shift_send(near_upper + parts[2], plan, 1)
    row_lower, row_upper = xor_send((parts[5], parts[7]), row_mask)
    both_lower, both_upper = xor_send((parts[6], parts[4]), both_mask)
    grad_lower_edge = parts[1] + to_upper + row_lower + both_lower
    grad_upper_edge = parts[3] + to_lower + row_upper + both_upper
    return (grad_lower_edge, grad_upper_edge)


def pad_tiles(local_tiles, rim_plans):
    column_plan, row_plan = rim_plans
    side_lower, side_upper = rim_forward(local_tiles[:, :, 0], local_tiles[:, :, -1], column_plan)
    widened = jnp.concatenate([side_lower[:, :, None], local_tiles, side_upper[:, :, None]], axis=2)
    top_rim, bottom_rim = rim_forward(widened[:, 0], widened[:, -1], row_plan)
    return jnp.concatenate([top_rim[:, None], widened, bottom_rim[:, None]], axis=1)


def pad_back(grad, rim_plans):
    column_plan, row_plan = rim_plans
    top_edge, bottom_edge = rim_backward(grad[:, 0], grad[:, -1], row_plan)
    widened = grad[:, 1:-1]
    widened = widened.at[:, 0].add(top_edge).at[:, -1].add(bottom_edge)
    left_edge, right_edge = rim_backward(widened[:, :, 0], widened[:, :, -1], column_plan)
    interior = widened[:, :, 1:-1]
    return interior.at[:, :, 0].add(left_edge).at[:, :, -1].add(right_edge)


def convolve(padded, weight):
    channels = weight.shape[-1]
    kernel = weight.reshape(3, 3, weight.shape[1], channels)
    return lax.conv_general_dilated(
        padded,
        kernel,
        (1, 1),
        "VALID",
        dimension_numbers=("NHWC", "HWIO", "NHWC"),
        preferred_element_type=jnp.float32,
    )


def convolve_back(grad, weight):
    kernel = weight.reshape(3, 3, weight.shape[1], weight.shape[2])[::-1, ::-1]
    return lax.conv_general_dilated(
        grad,
        kernel,
        (1, 1),
        ((2, 2), (2, 2)),
        dimension_numbers=("NHWC", "HWOI", "NHWC"),
        preferred_element_type=jnp.float32,
    )


def weight_grad(padded, grad):
    summed = lax.conv_general_dilated(
        padded,
        grad,
        (1, 1),
        "VALID",
        dimension_numbers=("CHWN", "IHWO", "HWNC"),
        preferred_element_type=jnp.float32,
    )
    return summed.reshape((9,) + summed.shape[2:])


def local(fields, weight_one, weight_two, cotangent, face_links, face_order):
    local_tiles = fields[0]
    face_count = local_tiles.shape[0]
    extent = local_tiles.shape[1]
    devices = lax.axis_size("tile")
    grid_side = math.isqrt(devices * face_count // 12)
    halves = devices // (grid_side * grid_side)
    levels = grid_side.bit_length() - 1
    device = lax.axis_index("tile")
    my_half = device // (grid_side * grid_side)
    grid_row = device // grid_side % grid_side
    grid_col = device % grid_side
    column_plan = make_plan(
        face_order,
        face_links,
        my_half,
        halves,
        face_count,
        grid_side,
        1,
        list(range(levels, 2 * levels)),
        (2, 3),
        grid_col,
        grid_row,
        False,
        2 * levels,
    )
    row_plan = make_plan(
        face_order,
        face_links,
        my_half,
        halves,
        face_count,
        grid_side,
        grid_side,
        list(range(levels)),
        (0, 1),
        grid_row,
        grid_col,
        True,
        2 * levels,
    )
    rim_plans = (column_plan, row_plan)
    padded_in = pad_tiles(local_tiles, rim_plans)
    pre_act = convolve(padded_in, weight_one)
    hidden = jax.nn.gelu(pre_act, approximate=True).astype(jnp.bfloat16)
    padded_hidden = pad_tiles(hidden, rim_plans)
    second = convolve(padded_hidden, weight_two)
    block_output = (local_tiles.astype(jnp.float32) + second).astype(jnp.bfloat16)
    grad_out = cotangent[0]
    grad_scale = 1.0 / math.sqrt(lax.axis_size("dp") * 12 * (grid_side * extent) ** 2)
    local_two = weight_grad(padded_hidden, grad_out) * grad_scale
    rim_two = convolve_back(grad_out, weight_two).astype(jnp.bfloat16)
    rim_two = lax.optimization_barrier(rim_two).astype(jnp.float32)
    grad_hidden = pad_back(rim_two, rim_plans)
    gelu_pair = jax.vjp(partial(jax.nn.gelu, approximate=True), pre_act)
    grad_pre = gelu_pair[1](grad_hidden)[0].astype(jnp.bfloat16)
    local_one = weight_grad(padded_in, grad_pre) * grad_scale
    rim_one = convolve_back(grad_pre, weight_one).astype(jnp.bfloat16)
    rim_one = lax.optimization_barrier(rim_one).astype(jnp.float32)
    field_grad = (grad_out.astype(jnp.float32) + pad_back(rim_one, rim_plans)).astype(jnp.bfloat16)
    grad_one, grad_two = lax.psum((local_one, local_two), ("tile", "dp"))
    return (block_output[None], field_grad[None], grad_one, grad_two)


def solution(mesh):
    in_specs = (
        P("dp", "tile", None, None, None),
        P(),
        P(),
        P("dp", "tile", None, None, None),
        P(),
        P(),
    )
    out_specs = (P("dp", "tile", None, None, None), P("dp", "tile", None, None, None), P(), P())
    return jax.shard_map(local, mesh=mesh, in_specs=in_specs, out_specs=out_specs, check_vma=False)
```

```python
from functools import partial
import math

import jax
import jax.numpy as jnp
from jax import lax
from jax.sharding import PartitionSpec as P


def shortened(shard):
    return jax.tree.map(lambda a: a.astype(jnp.bfloat16) if a.dtype == jnp.float32 else a, shard)


def from_behind(value, axis, steps):
    count = lax.axis_size(axis)
    first, last = (max(0, -steps), min(count, count - steps))
    return lax.ppermute(value, axis, [(source, source + steps) for source in range(first, last)])


def swapped(shard, axis, apart):
    return lax.ppermute(shard, axis, [(i, i ^ 1 << apart) for i in range(lax.axis_size(axis))])


def send_rim(values, offset):
    return jax.tree.map(
        lambda part, own: part.astype(own.dtype),
        from_behind(shortened(values), "tile", offset),
        values,
    )


def swap_rim(values, bit_index):
    return jax.tree.map(
        lambda part, own: part.astype(own.dtype),
        swapped(shortened(values), "tile", bit_index),
        values,
    )


def send_back(values, offset):
    return jax.tree.map(
        lambda part, own: part.astype(own.dtype),
        from_behind(shortened(values), "tile", offset),
        values,
    )


def swap_back(values, bit_index):
    return jax.tree.map(
        lambda part, own: part.astype(own.dtype),
        swapped(shortened(values), "tile", bit_index),
        values,
    )


def link_table(face_order, face_links, my_half, face_count, which_side):
    lookup = jnp.arange(face_order.shape[0], dtype=jnp.int32)
    inverse = jnp.sum(
        lookup[None, :] * (face_order[None, :] == lookup[:, None]).astype(jnp.int32), axis=1
    ).astype(jnp.int32)
    face_ids = lax.dynamic_slice_in_dim(face_order, my_half * face_count, face_count)
    link_rows = jnp.take(face_links, face_ids, axis=0)[:, which_side]
    source = jnp.take(inverse, link_rows[:, 0])
    remote = source // face_count != my_half
    candidate = link_rows[:, 1]
    pick_index = ((link_rows[:, 2] * 2 + candidate) * face_count + source % face_count).astype(
        jnp.int32
    )
    return (pick_index, remote, link_rows[:, 2] == 1)


def make_plan(
    face_order,
    face_links,
    my_half,
    halves,
    face_count,
    grid_side,
    step_size,
    mirror_bits,
    side_pair,
    device_pos,
    along_pos,
    mask_ends,
    half_bit,
):
    plan = {
        "step": step_size,
        "far": (grid_side - 1) * step_size,
        "bits": mirror_bits,
        "half_bit": half_bit,
        "halves": halves,
        "device_pos": device_pos,
        "along_pos": along_pos,
        "grid_side": grid_side,
        "ends": mask_ends,
    }
    for label_name, which_side in (("lower", side_pair[0]), ("upper", side_pair[1])):
        plan[label_name] = link_table(face_order, face_links, my_half, face_count, which_side)
        if halves == 2:
            plan[label_name + "_partner"] = link_table(
                face_order, face_links, 1 - my_half, face_count, which_side
            )
    return plan


def end_mask(plan, length):
    positions = jnp.arange(length)
    along_pos = plan["along_pos"]
    cut_cells = (positions == 0) & (along_pos == 0) | (positions == length - 1) & (
        along_pos == plan["grid_side"] - 1
    )
    return jnp.logical_not(cut_cells)[None, :, None]


def orient(rim_strip, reverse, plan):
    turned = jnp.where(reverse[:, None, None], rim_strip[:, ::-1], rim_strip)
    if plan["ends"]:
        turned = jnp.where(end_mask(plan, rim_strip.shape[1]), turned, jnp.zeros_like(turned))
    return turned


def orient_back(rim_strip, reverse, plan):
    masked = rim_strip
    if plan["ends"]:
        masked = jnp.where(end_mask(plan, rim_strip.shape[1]), masked, jnp.zeros_like(masked))
    return jnp.where(reverse[:, None, None], masked[:, ::-1], masked)


def pick_links(lower_stack, upper_stack, plan):
    index_lower, remote_lower = (plan["lower"][0], plan["lower"][1])
    index_upper, remote_upper = (plan["upper"][0], plan["upper"][1])
    own_lower = jnp.take(lower_stack, index_lower, axis=0)
    own_upper = jnp.take(upper_stack, index_upper, axis=0)
    if plan["halves"] == 1:
        return (own_lower, own_upper)
    partner_lower, partner_upper = jnp.split(
        swap_rim(jnp.concatenate([lower_stack, upper_stack], axis=0), plan["half_bit"]), 2, axis=0
    )
    got_lower = jnp.take(partner_lower, index_lower, axis=0)
    got_upper = jnp.take(partner_upper, index_upper, axis=0)
    return (
        jnp.where(remote_lower[:, None, None], got_lower, own_lower),
        jnp.where(remote_upper[:, None, None], got_upper, own_upper),
    )


def pick_back(grad_lower, grad_upper, plan):
    index_lower, remote_lower = (plan["lower"][0], plan["lower"][1])
    index_upper, remote_upper = (plan["upper"][0], plan["upper"][1])
    blank_rows = jnp.zeros((4 * grad_lower.shape[0],) + grad_lower.shape[1:], jnp.float32)
    if plan["halves"] == 1:
        return (blank_rows.at[index_lower].add(grad_lower), blank_rows.at[index_upper].add(grad_upper))
    stay_lower = jnp.where(remote_lower[:, None, None], 0.0, grad_lower)
    away_lower = jnp.where(remote_lower[:, None, None], grad_lower, 0.0)
    stay_upper = jnp.where(remote_upper[:, None, None], 0.0, grad_upper)
    away_upper = jnp.where(remote_upper[:, None, None], grad_upper, 0.0)
    away = jnp.concatenate(
        [blank_rows.at[index_lower].add(away_lower), blank_rows.at[index_upper].add(away_upper)], axis=0
    )
    back_lower, back_upper = jnp.split(swap_back(away, plan["half_bit"]), 2, axis=0)
    return (
        blank_rows.at[index_lower].add(stay_lower) + back_lower,
        blank_rows.at[index_upper].add(stay_upper) + back_upper,
    )


def cycled(value, plan, shift):
    count = lax.axis_size("tile")
    step_size, grid_side = (plan["step"], plan["grid_side"])
    pairs = []
    for source in range(count):
        position = source // step_size % grid_side
        moved = (position + shift) % grid_side
        pairs.append((source, source + (moved - position) * step_size))
    return lax.ppermute(value, "tile", pairs)


def mirror_masks(plan):
    mirror = sum(1 << bit_index for bit_index in plan["bits"])
    along = (plan["grid_side"] - 1) * plan["step"]
    return (mirror, mirror ^ along)


def xor_send(values, mask):
    count = lax.axis_size("tile")
    pairs = [(source, source ^ mask) for source in range(count)]
    joined = jnp.concatenate(values, axis=0)
    moved = lax.ppermute(shortened(joined), "tile", pairs).astype(joined.dtype)
    return jnp.split(moved, len(values), axis=0)


def shift_send(value, plan, shift):
    return cycled(shortened(value), plan, shift).astype(value.dtype)


def rim_forward(lower_edge, upper_edge, plan):
    row_mask, both_mask = mirror_masks(plan)
    from_lower = shift_send(upper_edge, plan, 1)
    from_upper = shift_send(lower_edge, plan, -1)
    row_lower, row_upper = xor_send((lower_edge, upper_edge), row_mask)
    both_lower, both_upper = xor_send((lower_edge, upper_edge), both_mask)
    device_pos = plan["device_pos"]
    at_lower = device_pos == 0
    at_upper = device_pos == plan["grid_side"] - 1
    lower_stack = jnp.concatenate([from_lower, lower_edge, both_upper, row_lower], axis=0)
    upper_stack = jnp.concatenate([from_upper, upper_edge, both_lower, row_upper], axis=0)
    link_lower, link_upper = pick_links(lower_stack, upper_stack, plan)
    link_lower = orient(link_lower, plan["lower"][2], plan)
    link_upper = orient(link_upper, plan["upper"][2], plan)
    lower_rim = jnp.where(at_lower, link_lower, from_lower)
    upper_rim = jnp.where(at_upper, link_upper, from_upper)
    return (lower_rim, upper_rim)


def rim_backward(grad_lower, grad_upper, plan):
    row_mask, both_mask = mirror_masks(plan)
    at_lower = plan["device_pos"] == 0
    at_upper = plan["device_pos"] == plan["grid_side"] - 1
    near_lower = jnp.where(at_lower, 0.0, grad_lower)
    near_upper = jnp.where(at_upper, 0.0, grad_upper)
    face_count = grad_lower.shape[0]
    link_lower = orient_back(jnp.where(at_lower, grad_lower, 0.0), plan["lower"][2], plan)
    link_upper = orient_back(jnp.where(at_upper, grad_upper, 0.0), plan["upper"][2], plan)
    lower_stack, upper_stack = pick_back(link_lower, link_upper, plan)
    low = [lower_stack[k * face_count : (k + 1) * face_count] for k in range(4)]
    up = [upper_stack[k * face_count : (k + 1) * face_count] for k in range(4)]
    to_lower = shift_send(near_lower + low[0], plan, -1)
    to_upper = shift_send(near_upper + up[0], plan, 1)
    row_lower, row_upper = xor_send((low[3], up[3]), row_mask)
    both_lower, both_upper = xor_send((up[2], low[2]), both_mask)
    grad_lower_edge = low[1] + to_upper + row_lower + both_lower
    grad_upper_edge = up[1] + to_lower + row_upper + both_upper
    return (grad_lower_edge, grad_upper_edge)


def pad_tiles(local_tiles, rim_plans):
    column_plan, row_plan = rim_plans
    side_lower, side_upper = rim_forward(local_tiles[:, :, 0], local_tiles[:, :, -1], column_plan)
    widened = jnp.concatenate([side_lower[:, :, None], local_tiles, side_upper[:, :, None]], axis=2)
    top_rim, bottom_rim = rim_forward(widened[:, 0], widened[:, -1], row_plan)
    return jnp.concatenate([top_rim[:, None], widened, bottom_rim[:, None]], axis=1)


def pad_back(grad, rim_plans):
    column_plan, row_plan = rim_plans
    top_edge, bottom_edge = rim_backward(grad[:, 0], grad[:, -1], row_plan)
    widened = grad[:, 1:-1]
    widened = jnp.concatenate(
        [widened[:, :1] + top_edge[:, None], widened[:, 1:-1], widened[:, -1:] + bottom_edge[:, None]],
        axis=1,
    )
    left_edge, right_edge = rim_backward(widened[:, :, 0], widened[:, :, -1], column_plan)
    interior = widened[:, :, 1:-1]
    return jnp.concatenate(
        [
            interior[:, :, :1] + left_edge[:, :, None],
            interior[:, :, 1:-1],
            interior[:, :, -1:] + right_edge[:, :, None],
        ],
        axis=2,
    )


def convolve(padded, weight):
    channels = weight.shape[-1]
    kernel = weight.reshape(3, 3, weight.shape[1], channels)
    return lax.conv_general_dilated(
        padded,
        kernel,
        (1, 1),
        "VALID",
        dimension_numbers=("NHWC", "HWIO", "NHWC"),
        preferred_element_type=jnp.float32,
    )


def convolve_back(grad, weight):
    kernel = weight.reshape(3, 3, weight.shape[1], weight.shape[2])[::-1, ::-1]
    return lax.conv_general_dilated(
        grad,
        kernel,
        (1, 1),
        ((2, 2), (2, 2)),
        dimension_numbers=("NHWC", "HWOI", "NHWC"),
        preferred_element_type=jnp.float32,
    )


def weight_grad(padded, grad):
    summed = lax.conv_general_dilated(
        padded,
        grad,
        (1, 1),
        "VALID",
        dimension_numbers=("CHWN", "IHWO", "HWNC"),
        preferred_element_type=jnp.float32,
    )
    return summed.reshape((9,) + summed.shape[2:])


def local(fields, weight_one, weight_two, cotangent, face_links, face_order):
    local_tiles = fields[0]
    face_count = local_tiles.shape[0]
    extent = local_tiles.shape[1]
    devices = lax.axis_size("tile")
    grid_side = math.isqrt(devices * face_count // 12)
    halves = devices // (grid_side * grid_side)
    levels = grid_side.bit_length() - 1
    device = lax.axis_index("tile")
    my_half = device // (grid_side * grid_side)
    grid_row = device // grid_side % grid_side
    grid_col = device % grid_side
    column_plan = make_plan(
        face_order,
        face_links,
        my_half,
        halves,
        face_count,
        grid_side,
        1,
        list(range(levels, 2 * levels)),
        (2, 3),
        grid_col,
        grid_row,
        False,
        2 * levels,
    )
    row_plan = make_plan(
        face_order,
        face_links,
        my_half,
        halves,
        face_count,
        grid_side,
        grid_side,
        list(range(levels)),
        (0, 1),
        grid_row,
        grid_col,
        True,
        2 * levels,
    )
    rim_plans = (column_plan, row_plan)
    padded_in = pad_tiles(local_tiles, rim_plans)
    pre_act = convolve(padded_in, weight_one)
    hidden = jax.nn.gelu(pre_act, approximate=True).astype(jnp.bfloat16)
    padded_hidden = pad_tiles(hidden, rim_plans)
    second = convolve(padded_hidden, weight_two)
    block_output = (local_tiles.astype(jnp.float32) + second).astype(jnp.bfloat16)
    grad_out = cotangent[0]
    grad_scale = 1.0 / math.sqrt(lax.axis_size("dp") * 12 * (grid_side * extent) ** 2)
    local_two = weight_grad(padded_hidden, grad_out) * grad_scale
    rim_two = convolve_back(grad_out, weight_two).astype(jnp.bfloat16)
    rim_two = lax.optimization_barrier(rim_two).astype(jnp.float32)
    grad_hidden = pad_back(rim_two, rim_plans)
    gelu_pair = jax.vjp(partial(jax.nn.gelu, approximate=True), pre_act)
    grad_pre = gelu_pair[1](grad_hidden)[0].astype(jnp.bfloat16)
    local_one = weight_grad(padded_in, grad_pre) * grad_scale
    rim_one = convolve_back(grad_pre, weight_one).astype(jnp.bfloat16)
    rim_one = lax.optimization_barrier(rim_one).astype(jnp.float32)
    field_grad = (grad_out.astype(jnp.float32) + pad_back(rim_one, rim_plans)).astype(jnp.bfloat16)
    grad_one, grad_two = lax.psum((local_one, local_two), ("tile", "dp"))
    return (block_output[None], field_grad[None], grad_one, grad_two)


def solution(mesh):
    in_specs = (
        P("dp", "tile", None, None, None),
        P(),
        P(),
        P("dp", "tile", None, None, None),
        P(),
        P(),
    )
    out_specs = (P("dp", "tile", None, None, None), P("dp", "tile", None, None, None), P(), P())
    return jax.shard_map(local, mesh=mesh, in_specs=in_specs, out_specs=out_specs, check_vma=False)
```

```python
from functools import partial
import itertools
import math

import jax
import jax.numpy as jnp
from jax import lax
from jax.sharding import PartitionSpec as P


def shortened(shard):
    return jax.tree.map(lambda a: a.astype(jnp.bfloat16) if a.dtype == jnp.float32 else a, shard)


def from_behind(value, axis, steps):
    count = lax.axis_size(axis)
    first, last = (max(0, -steps), min(count, count - steps))
    return lax.ppermute(value, axis, [(source, source + steps) for source in range(first, last)])


def swapped(shard, axis, apart):
    return lax.ppermute(shard, axis, [(i, i ^ 1 << apart) for i in range(lax.axis_size(axis))])


def send_rim(values, offset):
    return jax.tree.map(
        lambda part, own: part.astype(own.dtype),
        from_behind(shortened(values), "tile", offset),
        values,
    )


def swap_rim(values, bit_index):
    return jax.tree.map(
        lambda part, own: part.astype(own.dtype),
        swapped(shortened(values), "tile", bit_index),
        values,
    )


def send_back(values, offset):
    return jax.tree.map(
        lambda part, own: part.astype(own.dtype),
        from_behind(shortened(values), "tile", offset),
        values,
    )


def swap_back(values, bit_index):
    return jax.tree.map(
        lambda part, own: part.astype(own.dtype),
        swapped(shortened(values), "tile", bit_index),
        values,
    )


def link_table(face_order, face_links, my_half, face_count, which_side):
    lookup = jnp.arange(face_order.shape[0], dtype=jnp.int32)
    inverse = jnp.sum(
        lookup[None, :] * (face_order[None, :] == lookup[:, None]).astype(jnp.int32), axis=1
    ).astype(jnp.int32)
    face_ids = lax.dynamic_slice_in_dim(face_order, my_half * face_count, face_count)
    link_rows = jnp.take(face_links, face_ids, axis=0)[:, which_side]
    source = jnp.take(inverse, link_rows[:, 0])
    remote = source // face_count != my_half
    candidate = link_rows[:, 1]
    pick_index = ((link_rows[:, 2] * 2 + candidate) * face_count + source % face_count).astype(
        jnp.int32
    )
    return (pick_index, remote, link_rows[:, 2] == 1)


def make_plan(
    face_order,
    face_links,
    my_half,
    halves,
    face_count,
    grid_side,
    step_size,
    mirror_bits,
    side_pair,
    device_pos,
    along_pos,
    mask_ends,
    half_bit,
):
    plan = {
        "step": step_size,
        "far": (grid_side - 1) * step_size,
        "bits": mirror_bits,
        "half_bit": half_bit,
        "halves": halves,
        "device_pos": device_pos,
        "along_pos": along_pos,
        "grid_side": grid_side,
        "ends": mask_ends,
    }
    for label_name, which_side in (("lower", side_pair[0]), ("upper", side_pair[1])):
        plan[label_name] = link_table(face_order, face_links, my_half, face_count, which_side)
        if halves == 2:
            plan[label_name + "_partner"] = link_table(
                face_order, face_links, 1 - my_half, face_count, which_side
            )
    return plan


def end_mask(plan, length):
    positions = jnp.arange(length)
    along_pos = plan["along_pos"]
    cut_cells = (positions == 0) & (along_pos == 0) | (positions == length - 1) & (
        along_pos == plan["grid_side"] - 1
    )
    return jnp.logical_not(cut_cells)[None, :, None]


def orient(rim_strip, reverse, plan):
    turned = jnp.where(reverse[:, None, None], rim_strip[:, ::-1], rim_strip)
    if plan["ends"]:
        turned = jnp.where(end_mask(plan, rim_strip.shape[1]), turned, jnp.zeros_like(turned))
    return turned


def orient_back(rim_strip, reverse, plan):
    masked = rim_strip
    if plan["ends"]:
        masked = jnp.where(end_mask(plan, rim_strip.shape[1]), masked, jnp.zeros_like(masked))
    return jnp.where(reverse[:, None, None], masked[:, ::-1], masked)


def pick_links(lower_stack, upper_stack, plan):
    index_lower, remote_lower = (plan["lower"][0], plan["lower"][1])
    index_upper, remote_upper = (plan["upper"][0], plan["upper"][1])
    own_lower = jnp.take(lower_stack, index_lower, axis=0)
    own_upper = jnp.take(upper_stack, index_upper, axis=0)
    if plan["halves"] == 1:
        return (own_lower, own_upper)
    partner_lower, partner_upper = jnp.split(
        swap_rim(jnp.concatenate([lower_stack, upper_stack], axis=0), plan["half_bit"]), 2, axis=0
    )
    got_lower = jnp.take(partner_lower, index_lower, axis=0)
    got_upper = jnp.take(partner_upper, index_upper, axis=0)
    return (
        jnp.where(remote_lower[:, None, None], got_lower, own_lower),
        jnp.where(remote_upper[:, None, None], got_upper, own_upper),
    )


def pick_back(grad_lower, grad_upper, plan):
    index_lower, remote_lower = (plan["lower"][0], plan["lower"][1])
    index_upper, remote_upper = (plan["upper"][0], plan["upper"][1])
    blank_rows = jnp.zeros((4 * grad_lower.shape[0],) + grad_lower.shape[1:], jnp.float32)
    if plan["halves"] == 1:
        return (blank_rows.at[index_lower].add(grad_lower), blank_rows.at[index_upper].add(grad_upper))
    stay_lower = jnp.where(remote_lower[:, None, None], 0.0, grad_lower)
    away_lower = jnp.where(remote_lower[:, None, None], grad_lower, 0.0)
    stay_upper = jnp.where(remote_upper[:, None, None], 0.0, grad_upper)
    away_upper = jnp.where(remote_upper[:, None, None], grad_upper, 0.0)
    away = jnp.concatenate(
        [blank_rows.at[index_lower].add(away_lower), blank_rows.at[index_upper].add(away_upper)], axis=0
    )
    back_lower, back_upper = jnp.split(swap_back(away, plan["half_bit"]), 2, axis=0)
    return (
        blank_rows.at[index_lower].add(stay_lower) + back_lower,
        blank_rows.at[index_upper].add(stay_upper) + back_upper,
    )


def cycled(value, plan, shift):
    count = lax.axis_size("tile")
    step_size, grid_side = (plan["step"], plan["grid_side"])
    pairs = []
    for source in range(count):
        position = source // step_size % grid_side
        moved = (position + shift) % grid_side
        pairs.append((source, source + (moved - position) * step_size))
    return lax.ppermute(value, "tile", pairs)


def mirror_masks(plan):
    mirror = sum(1 << bit_index for bit_index in plan["bits"])
    along = (plan["grid_side"] - 1) * plan["step"]
    return (mirror, mirror ^ along)


def xor_send(values, mask):
    count = lax.axis_size("tile")
    pairs = [(source, source ^ mask) for source in range(count)]
    joined = jnp.concatenate(values, axis=0)
    moved = lax.ppermute(shortened(joined), "tile", pairs).astype(joined.dtype)
    return jnp.split(moved, len(values), axis=0)


def shift_send(value, plan, shift):
    return cycled(shortened(value), plan, shift).astype(value.dtype)


def exchange(sends_list, plan):
    row_mask, both_mask = mirror_masks(plan)
    count = lax.axis_size("tile")
    received = [dict() for _ in sends_list]
    for key in ("up", "down", "row", "both"):
        pieces = [sends[key] for sends in sends_list]
        cuts = list(itertools.accumulate(piece.shape[1] for piece in pieces))[:-1]
        joined = jnp.concatenate([shortened(piece) for piece in pieces], axis=1)
        if key == "up":
            moved = cycled(joined, plan, 1)
        elif key == "down":
            moved = cycled(joined, plan, -1)
        else:
            mask = row_mask if key == "row" else both_mask
            moved = lax.ppermute(joined, "tile", [(source, source ^ mask) for source in range(count)])
        for got, piece, part in zip(received, pieces, jnp.split(moved, cuts, axis=1)):
            got[key] = part.astype(piece.dtype)
    return received


def forward_sends(lower_edge, upper_edge):
    both_edges = jnp.concatenate([lower_edge, upper_edge], axis=0)
    return {"up": upper_edge, "down": lower_edge, "row": both_edges, "both": both_edges}


def forward_finish(got, lower_edge, upper_edge, plan):
    from_lower, from_upper = (got["up"], got["down"])
    row_lower, row_upper = jnp.split(got["row"], 2, axis=0)
    both_lower, both_upper = jnp.split(got["both"], 2, axis=0)
    at_lower = plan["device_pos"] == 0
    at_upper = plan["device_pos"] == plan["grid_side"] - 1
    lower_stack = jnp.concatenate([from_lower, lower_edge, both_upper, row_lower], axis=0)
    upper_stack = jnp.concatenate([from_upper, upper_edge, both_lower, row_upper], axis=0)
    link_lower, link_upper = pick_links(lower_stack, upper_stack, plan)
    link_lower = orient(link_lower, plan["lower"][2], plan)
    link_upper = orient(link_upper, plan["upper"][2], plan)
    lower_rim = jnp.where(at_lower, link_lower, from_lower)
    upper_rim = jnp.where(at_upper, link_upper, from_upper)
    return (lower_rim, upper_rim)


def backward_sends(grad_lower, grad_upper, plan):
    at_lower = plan["device_pos"] == 0
    at_upper = plan["device_pos"] == plan["grid_side"] - 1
    near_lower = jnp.where(at_lower, 0.0, grad_lower)
    near_upper = jnp.where(at_upper, 0.0, grad_upper)
    face_count = grad_lower.shape[0]
    link_lower = orient_back(jnp.where(at_lower, grad_lower, 0.0), plan["lower"][2], plan)
    link_upper = orient_back(jnp.where(at_upper, grad_upper, 0.0), plan["upper"][2], plan)
    lower_stack, upper_stack = pick_back(link_lower, link_upper, plan)
    low = [lower_stack[k * face_count : (k + 1) * face_count] for k in range(4)]
    up = [upper_stack[k * face_count : (k + 1) * face_count] for k in range(4)]
    sends = {
        "down": near_lower + low[0],
        "up": near_upper + up[0],
        "row": jnp.concatenate([low[3], up[3]], axis=0),
        "both": jnp.concatenate([up[2], low[2]], axis=0),
    }
    return (sends, (low[1], up[1]))


def backward_finish(got, kept):
    row_lower, row_upper = jnp.split(got["row"], 2, axis=0)
    both_lower, both_upper = jnp.split(got["both"], 2, axis=0)
    grad_lower_edge = kept[0] + got["up"] + row_lower + both_lower
    grad_upper_edge = kept[1] + got["down"] + row_upper + both_upper
    return (grad_lower_edge, grad_upper_edge)


def add_ends(values, lower, upper, axis):
    first = lax.slice_in_dim(values, 0, 1, axis=axis)
    middle = lax.slice_in_dim(values, 1, values.shape[axis] - 1, axis=axis)
    last = lax.slice_in_dim(values, values.shape[axis] - 1, values.shape[axis], axis=axis)
    return jnp.concatenate(
        [first + jnp.expand_dims(lower, axis), middle, last + jnp.expand_dims(upper, axis)], axis=axis
    )


def pad_pair(tiles, grad, rim_plans):
    column_plan, row_plan = rim_plans
    back_plans = (dict(column_plan, ends=True), dict(row_plan, ends=False))
    padded, grad_tiles = (None, None)
    for stage in range(2):
        plan = rim_plans[stage]
        sends_list = []
        if tiles is not None:
            edges = (tiles[:, :, 0], tiles[:, :, -1]) if stage == 0 else (tiles[:, 0], tiles[:, -1])
            sends_list.append(forward_sends(*edges))
        if grad is not None:
            grad_edges = (grad[:, :, 0], grad[:, :, -1]) if stage == 0 else (grad[:, 0], grad[:, -1])
            grad_sends, kept = backward_sends(*grad_edges, back_plans[stage])
            sends_list.append(grad_sends)
        received = exchange(sends_list, plan)
        if tiles is not None:
            lower_rim, upper_rim = forward_finish(received[0], *edges, plan)
            tiles = jnp.concatenate(
                [jnp.expand_dims(lower_rim, 2 - stage), tiles, jnp.expand_dims(upper_rim, 2 - stage)],
                axis=2 - stage,
            )
        if grad is not None:
            lower_grad, upper_grad = backward_finish(received[-1], kept)
            inner = grad[:, :, 1:-1] if stage == 0 else grad[:, 1:-1]
            grad = add_ends(inner, lower_grad, upper_grad, 2 - stage)
    return (tiles, grad)


def convolve(padded, weight):
    channels = weight.shape[-1]
    kernel = weight.reshape(3, 3, weight.shape[1], channels)
    return lax.conv_general_dilated(
        padded,
        kernel,
        (1, 1),
        "VALID",
        dimension_numbers=("NHWC", "HWIO", "NHWC"),
        preferred_element_type=jnp.float32,
    )


def convolve_back(grad, weight):
    kernel = weight.reshape(3, 3, weight.shape[1], weight.shape[2])[::-1, ::-1]
    return lax.conv_general_dilated(
        grad,
        kernel,
        (1, 1),
        ((2, 2), (2, 2)),
        dimension_numbers=("NHWC", "HWOI", "NHWC"),
        preferred_element_type=jnp.float32,
    )


def weight_grad(padded, grad):
    summed = lax.conv_general_dilated(
        padded,
        grad,
        (1, 1),
        "VALID",
        dimension_numbers=("CHWN", "IHWO", "HWNC"),
        preferred_element_type=jnp.float32,
    )
    return summed.reshape((9,) + summed.shape[2:])


def local(fields, weight_one, weight_two, cotangent, face_links, face_order):
    local_tiles = fields[0]
    face_count = local_tiles.shape[0]
    extent = local_tiles.shape[1]
    devices = lax.axis_size("tile")
    grid_side = math.isqrt(devices * face_count // 12)
    halves = devices // (grid_side * grid_side)
    levels = grid_side.bit_length() - 1
    device = lax.axis_index("tile")
    my_half = device // (grid_side * grid_side)
    grid_row = device // grid_side % grid_side
    grid_col = device % grid_side
    column_plan = make_plan(
        face_order,
        face_links,
        my_half,
        halves,
        face_count,
        grid_side,
        1,
        list(range(levels, 2 * levels)),
        (2, 3),
        grid_col,
        grid_row,
        False,
        2 * levels,
    )
    row_plan = make_plan(
        face_order,
        face_links,
        my_half,
        halves,
        face_count,
        grid_side,
        grid_side,
        list(range(levels)),
        (0, 1),
        grid_row,
        grid_col,
        True,
        2 * levels,
    )
    rim_plans = (column_plan, row_plan)
    grad_out = cotangent[0]
    rim_two = convolve_back(grad_out, weight_two).astype(jnp.bfloat16)
    rim_two = lax.optimization_barrier(rim_two).astype(jnp.float32)
    padded_in, grad_hidden = pad_pair(local_tiles, rim_two, rim_plans)
    pre_act = convolve(padded_in, weight_one)
    hidden = jax.nn.gelu(pre_act, approximate=True).astype(jnp.bfloat16)
    padded_hidden = pad_pair(hidden, None, rim_plans)[0]
    second = convolve(padded_hidden, weight_two)
    block_output = (local_tiles.astype(jnp.float32) + second).astype(jnp.bfloat16)
    grad_scale = 1.0 / math.sqrt(lax.axis_size("dp") * 12 * (grid_side * extent) ** 2)
    local_two = weight_grad(padded_hidden, grad_out) * grad_scale
    gelu_pair = jax.vjp(partial(jax.nn.gelu, approximate=True), pre_act)
    grad_pre = gelu_pair[1](grad_hidden)[0].astype(jnp.bfloat16)
    local_one = weight_grad(padded_in, grad_pre) * grad_scale
    rim_one = convolve_back(grad_pre, weight_one).astype(jnp.bfloat16)
    rim_one = lax.optimization_barrier(rim_one).astype(jnp.float32)
    field_grad = (grad_out.astype(jnp.float32) + pad_pair(None, rim_one, rim_plans)[1]).astype(jnp.bfloat16)
    grad_one, grad_two = lax.psum((local_one, local_two), ("tile", "dp"))
    return (block_output[None], field_grad[None], grad_one, grad_two)


def solution(mesh):
    in_specs = (
        P("dp", "tile", None, None, None),
        P(),
        P(),
        P("dp", "tile", None, None, None),
        P(),
        P(),
    )
    out_specs = (P("dp", "tile", None, None, None), P("dp", "tile", None, None, None), P(), P())
    return jax.shard_map(local, mesh=mesh, in_specs=in_specs, out_specs=out_specs, check_vma=False)
```

```python
from functools import partial
import itertools
import math

import jax
import jax.numpy as jnp
from jax import lax
from jax.sharding import PartitionSpec as P


def shortened(shard):
    return jax.tree.map(lambda a: a.astype(jnp.bfloat16) if a.dtype == jnp.float32 else a, shard)


def from_behind(value, axis, steps):
    count = lax.axis_size(axis)
    first, last = (max(0, -steps), min(count, count - steps))
    return lax.ppermute(value, axis, [(source, source + steps) for source in range(first, last)])


def swapped(shard, axis, apart):
    return lax.ppermute(shard, axis, [(i, i ^ 1 << apart) for i in range(lax.axis_size(axis))])


def send_rim(values, offset):
    return jax.tree.map(
        lambda part, own: part.astype(own.dtype),
        from_behind(shortened(values), "tile", offset),
        values,
    )


def swap_rim(values, bit_index):
    return jax.tree.map(
        lambda part, own: part.astype(own.dtype),
        swapped(shortened(values), "tile", bit_index),
        values,
    )


def send_back(values, offset):
    return jax.tree.map(
        lambda part, own: part.astype(own.dtype),
        from_behind(shortened(values), "tile", offset),
        values,
    )


def swap_back(values, bit_index):
    return jax.tree.map(
        lambda part, own: part.astype(own.dtype),
        swapped(shortened(values), "tile", bit_index),
        values,
    )


def link_table(face_order, face_links, my_half, face_count, which_side):
    lookup = jnp.arange(face_order.shape[0], dtype=jnp.int32)
    inverse = jnp.sum(
        lookup[None, :] * (face_order[None, :] == lookup[:, None]).astype(jnp.int32), axis=1
    ).astype(jnp.int32)
    face_ids = lax.dynamic_slice_in_dim(face_order, my_half * face_count, face_count)
    link_rows = jnp.take(face_links, face_ids, axis=0)[:, which_side]
    source = jnp.take(inverse, link_rows[:, 0])
    remote = source // face_count != my_half
    candidate = link_rows[:, 1]
    pick_index = ((link_rows[:, 2] * 2 + candidate) * face_count + source % face_count).astype(
        jnp.int32
    )
    return (pick_index, remote, link_rows[:, 2] == 1)


def make_plan(
    face_order,
    face_links,
    my_half,
    halves,
    face_count,
    grid_side,
    step_size,
    mirror_bits,
    side_pair,
    device_pos,
    along_pos,
    mask_ends,
    half_bit,
):
    plan = {
        "step": step_size,
        "far": (grid_side - 1) * step_size,
        "bits": mirror_bits,
        "half_bit": half_bit,
        "halves": halves,
        "device_pos": device_pos,
        "along_pos": along_pos,
        "grid_side": grid_side,
        "ends": mask_ends,
    }
    for label_name, which_side in (("lower", side_pair[0]), ("upper", side_pair[1])):
        plan[label_name] = link_table(face_order, face_links, my_half, face_count, which_side)
        if halves == 2:
            plan[label_name + "_partner"] = link_table(
                face_order, face_links, 1 - my_half, face_count, which_side
            )
    return plan


def end_mask(plan, length):
    positions = jnp.arange(length)
    along_pos = plan["along_pos"]
    cut_cells = (positions == 0) & (along_pos == 0) | (positions == length - 1) & (
        along_pos == plan["grid_side"] - 1
    )
    return jnp.logical_not(cut_cells)[None, :, None]


def orient(rim_strip, reverse, plan):
    turned = jnp.where(reverse[:, None, None], rim_strip[:, ::-1], rim_strip)
    if plan["ends"]:
        turned = jnp.where(end_mask(plan, rim_strip.shape[1]), turned, jnp.zeros_like(turned))
    return turned


def orient_back(rim_strip, reverse, plan):
    masked = rim_strip
    if plan["ends"]:
        masked = jnp.where(end_mask(plan, rim_strip.shape[1]), masked, jnp.zeros_like(masked))
    return jnp.where(reverse[:, None, None], masked[:, ::-1], masked)


def pick_links(lower_stack, upper_stack, plan):
    index_lower, remote_lower = (plan["lower"][0], plan["lower"][1])
    index_upper, remote_upper = (plan["upper"][0], plan["upper"][1])
    own_lower = jnp.take(lower_stack, index_lower, axis=0)
    own_upper = jnp.take(upper_stack, index_upper, axis=0)
    if plan["halves"] == 1:
        return (own_lower, own_upper)
    partner_lower, partner_upper = jnp.split(
        swap_rim(jnp.concatenate([lower_stack, upper_stack], axis=0), plan["half_bit"]), 2, axis=0
    )
    got_lower = jnp.take(partner_lower, index_lower, axis=0)
    got_upper = jnp.take(partner_upper, index_upper, axis=0)
    return (
        jnp.where(remote_lower[:, None, None], got_lower, own_lower),
        jnp.where(remote_upper[:, None, None], got_upper, own_upper),
    )


def pick_back(grad_lower, grad_upper, plan):
    index_lower, remote_lower = (plan["lower"][0], plan["lower"][1])
    index_upper, remote_upper = (plan["upper"][0], plan["upper"][1])
    blank_rows = jnp.zeros((4 * grad_lower.shape[0],) + grad_lower.shape[1:], jnp.float32)
    if plan["halves"] == 1:
        return (blank_rows.at[index_lower].add(grad_lower), blank_rows.at[index_upper].add(grad_upper))
    stay_lower = jnp.where(remote_lower[:, None, None], 0.0, grad_lower)
    away_lower = jnp.where(remote_lower[:, None, None], grad_lower, 0.0)
    stay_upper = jnp.where(remote_upper[:, None, None], 0.0, grad_upper)
    away_upper = jnp.where(remote_upper[:, None, None], grad_upper, 0.0)
    away = jnp.concatenate(
        [blank_rows.at[index_lower].add(away_lower), blank_rows.at[index_upper].add(away_upper)], axis=0
    )
    back_lower, back_upper = jnp.split(swap_back(away, plan["half_bit"]), 2, axis=0)
    return (
        blank_rows.at[index_lower].add(stay_lower) + back_lower,
        blank_rows.at[index_upper].add(stay_upper) + back_upper,
    )


def cycled(value, plan, shift):
    count = lax.axis_size("tile")
    step_size, grid_side = (plan["step"], plan["grid_side"])
    pairs = []
    for source in range(count):
        position = source // step_size % grid_side
        moved = (position + shift) % grid_side
        pairs.append((source, source + (moved - position) * step_size))
    return lax.ppermute(value, "tile", pairs)


def mirror_masks(plan):
    mirror = sum(1 << bit_index for bit_index in plan["bits"])
    along = (plan["grid_side"] - 1) * plan["step"]
    return (mirror, mirror ^ along)


def xor_send(values, mask):
    count = lax.axis_size("tile")
    pairs = [(source, source ^ mask) for source in range(count)]
    joined = jnp.concatenate(values, axis=0)
    moved = lax.ppermute(shortened(joined), "tile", pairs).astype(joined.dtype)
    return jnp.split(moved, len(values), axis=0)


def shift_send(value, plan, shift):
    return cycled(shortened(value), plan, shift).astype(value.dtype)


def exchange(sends_list, plan):
    row_mask, both_mask = mirror_masks(plan)
    count = lax.axis_size("tile")
    received = [dict() for _ in sends_list]
    for key in ("up", "down", "row", "both"):
        pieces = [sends[key] for sends in sends_list]
        cuts = list(itertools.accumulate(piece.shape[1] for piece in pieces))[:-1]
        joined = jnp.concatenate([shortened(piece) for piece in pieces], axis=1)
        if key == "up":
            moved = cycled(joined, plan, 1)
        elif key == "down":
            moved = cycled(joined, plan, -1)
        else:
            mask = row_mask if key == "row" else both_mask
            moved = lax.ppermute(joined, "tile", [(source, source ^ mask) for source in range(count)])
        for got, piece, part in zip(received, pieces, jnp.split(moved, cuts, axis=1)):
            got[key] = part.astype(piece.dtype)
    return received


def forward_sends(lower_edge, upper_edge):
    both_edges = jnp.concatenate([lower_edge, upper_edge], axis=0)
    return {"up": upper_edge, "down": lower_edge, "row": both_edges, "both": both_edges}


def forward_finish(got, lower_edge, upper_edge, plan):
    from_lower, from_upper = (got["up"], got["down"])
    row_lower, row_upper = jnp.split(got["row"], 2, axis=0)
    both_lower, both_upper = jnp.split(got["both"], 2, axis=0)
    at_lower = plan["device_pos"] == 0
    at_upper = plan["device_pos"] == plan["grid_side"] - 1
    lower_stack = jnp.concatenate([from_lower, lower_edge, both_upper, row_lower], axis=0)
    upper_stack = jnp.concatenate([from_upper, upper_edge, both_lower, row_upper], axis=0)
    link_lower, link_upper = pick_links(lower_stack, upper_stack, plan)
    link_lower = orient(link_lower, plan["lower"][2], plan)
    link_upper = orient(link_upper, plan["upper"][2], plan)
    lower_rim = jnp.where(at_lower, link_lower, from_lower)
    upper_rim = jnp.where(at_upper, link_upper, from_upper)
    return (lower_rim, upper_rim)


def backward_sends(grad_lower, grad_upper, plan):
    at_lower = plan["device_pos"] == 0
    at_upper = plan["device_pos"] == plan["grid_side"] - 1
    near_lower = jnp.where(at_lower, 0.0, grad_lower)
    near_upper = jnp.where(at_upper, 0.0, grad_upper)
    face_count = grad_lower.shape[0]
    link_lower = orient_back(jnp.where(at_lower, grad_lower, 0.0), plan["lower"][2], plan)
    link_upper = orient_back(jnp.where(at_upper, grad_upper, 0.0), plan["upper"][2], plan)
    lower_stack, upper_stack = pick_back(link_lower, link_upper, plan)
    low = [lower_stack[k * face_count : (k + 1) * face_count] for k in range(4)]
    up = [upper_stack[k * face_count : (k + 1) * face_count] for k in range(4)]
    sends = {
        "down": near_lower + low[0],
        "up": near_upper + up[0],
        "row": jnp.concatenate([low[3], up[3]], axis=0),
        "both": jnp.concatenate([up[2], low[2]], axis=0),
    }
    return (sends, (low[1], up[1]))


def backward_finish(got, kept):
    row_lower, row_upper = jnp.split(got["row"], 2, axis=0)
    both_lower, both_upper = jnp.split(got["both"], 2, axis=0)
    grad_lower_edge = kept[0] + got["up"] + row_lower + both_lower
    grad_upper_edge = kept[1] + got["down"] + row_upper + both_upper
    return (grad_lower_edge, grad_upper_edge)


def add_ends(values, lower, upper, axis):
    first = lax.slice_in_dim(values, 0, 1, axis=axis)
    middle = lax.slice_in_dim(values, 1, values.shape[axis] - 1, axis=axis)
    last = lax.slice_in_dim(values, values.shape[axis] - 1, values.shape[axis], axis=axis)
    return jnp.concatenate(
        [first + jnp.expand_dims(lower, axis), middle, last + jnp.expand_dims(upper, axis)], axis=axis
    )


def pad_pair(tiles, grad, rim_plans):
    column_plan, row_plan = rim_plans
    back_plans = (dict(column_plan, ends=True), dict(row_plan, ends=False))
    padded, grad_tiles = (None, None)
    for stage in range(2):
        plan = rim_plans[stage]
        sends_list = []
        if tiles is not None:
            edges = (tiles[:, :, 0], tiles[:, :, -1]) if stage == 0 else (tiles[:, 0], tiles[:, -1])
            sends_list.append(forward_sends(*edges))
        if grad is not None:
            grad_edges = (grad[:, :, 0], grad[:, :, -1]) if stage == 0 else (grad[:, 0], grad[:, -1])
            grad_sends, kept = backward_sends(*grad_edges, back_plans[stage])
            sends_list.append(grad_sends)
        received = exchange(sends_list, plan)
        if tiles is not None:
            lower_rim, upper_rim = forward_finish(received[0], *edges, plan)
            tiles = jnp.concatenate(
                [jnp.expand_dims(lower_rim, 2 - stage), tiles, jnp.expand_dims(upper_rim, 2 - stage)],
                axis=2 - stage,
            )
        if grad is not None:
            lower_grad, upper_grad = backward_finish(received[-1], kept)
            inner = grad[:, :, 1:-1] if stage == 0 else grad[:, 1:-1]
            grad = add_ends(inner, lower_grad, upper_grad, 2 - stage)
    return (tiles, grad)


def convolve(padded, weight):
    channels = weight.shape[-1]
    kernel = weight.reshape(3, 3, weight.shape[1], channels)
    return lax.conv_general_dilated(
        padded,
        kernel,
        (1, 1),
        "VALID",
        dimension_numbers=("NHWC", "HWIO", "NHWC"),
        preferred_element_type=jnp.float32,
    )


def convolve_back(grad, weight):
    kernel = weight.reshape(3, 3, weight.shape[1], weight.shape[2])[::-1, ::-1]
    return lax.conv_general_dilated(
        grad,
        kernel,
        (1, 1),
        ((2, 2), (2, 2)),
        dimension_numbers=("NHWC", "HWOI", "NHWC"),
        preferred_element_type=jnp.float32,
    )


def weight_grad(padded, grad):
    summed = lax.conv_general_dilated(
        padded,
        grad,
        (1, 1),
        "VALID",
        dimension_numbers=("CHWN", "IHWO", "HWNC"),
        preferred_element_type=jnp.float32,
    )
    return summed.reshape((9,) + summed.shape[2:])


def local(fields, weight_one, weight_two, cotangent, face_links, face_order):
    local_tiles = fields[0]
    face_count = local_tiles.shape[0]
    extent = local_tiles.shape[1]
    devices = lax.axis_size("tile")
    grid_side = math.isqrt(devices * face_count // 12)
    halves = devices // (grid_side * grid_side)
    levels = grid_side.bit_length() - 1
    device = lax.axis_index("tile")
    my_half = device // (grid_side * grid_side)
    grid_row = device // grid_side % grid_side
    grid_col = device % grid_side
    column_plan = make_plan(
        face_order,
        face_links,
        my_half,
        halves,
        face_count,
        grid_side,
        1,
        list(range(levels, 2 * levels)),
        (2, 3),
        grid_col,
        grid_row,
        False,
        2 * levels,
    )
    row_plan = make_plan(
        face_order,
        face_links,
        my_half,
        halves,
        face_count,
        grid_side,
        grid_side,
        list(range(levels)),
        (0, 1),
        grid_row,
        grid_col,
        True,
        2 * levels,
    )
    rim_plans = (column_plan, row_plan)
    grad_out = cotangent[0]
    rim_two = convolve_back(grad_out, weight_two).astype(jnp.bfloat16)
    rim_two = lax.optimization_barrier(rim_two).astype(jnp.float32)
    padded_in, grad_hidden = pad_pair(local_tiles, rim_two, rim_plans)
    pre_act = convolve(padded_in, weight_one)
    hidden = jax.nn.gelu(pre_act, approximate=True).astype(jnp.bfloat16)
    padded_hidden = pad_pair(hidden, None, rim_plans)[0]
    second = convolve(padded_hidden, weight_two)
    block_output = (local_tiles.astype(jnp.float32) + second).astype(jnp.bfloat16)
    grad_scale = 1.0 / math.sqrt(lax.axis_size("dp") * 12 * (grid_side * extent) ** 2)
    local_two = weight_grad(padded_hidden, grad_out) * grad_scale
    gelu_pair = jax.vjp(partial(jax.nn.gelu, approximate=True), pre_act)
    grad_pre = gelu_pair[1](grad_hidden)[0].astype(jnp.bfloat16)
    local_one = weight_grad(padded_in, grad_pre) * grad_scale
    rim_one = convolve_back(grad_pre, weight_one).astype(jnp.bfloat16)
    rim_one, local_one, local_two = lax.optimization_barrier((rim_one, local_one, local_two))
    rim_one = rim_one.astype(jnp.float32)
    field_grad = (grad_out.astype(jnp.float32) + pad_pair(None, rim_one, rim_plans)[1]).astype(jnp.bfloat16)
    grad_one, grad_two = lax.psum((local_one, local_two), ("tile", "dp"))
    return (block_output[None], field_grad[None], grad_one, grad_two)


def solution(mesh):
    in_specs = (
        P("dp", "tile", None, None, None),
        P(),
        P(),
        P("dp", "tile", None, None, None),
        P(),
        P(),
    )
    out_specs = (P("dp", "tile", None, None, None), P("dp", "tile", None, None, None), P(), P())
    return jax.shard_map(local, mesh=mesh, in_specs=in_specs, out_specs=out_specs, check_vma=False)
```

```python
from functools import partial
import itertools
import math

import jax
import jax.numpy as jnp
from jax import lax
from jax.sharding import PartitionSpec as P


def shortened(shard):
    return jax.tree.map(lambda a: a.astype(jnp.bfloat16) if a.dtype == jnp.float32 else a, shard)


def from_behind(value, axis, steps):
    count = lax.axis_size(axis)
    first, last = (max(0, -steps), min(count, count - steps))
    return lax.ppermute(value, axis, [(source, source + steps) for source in range(first, last)])


def swapped(shard, axis, apart):
    return lax.ppermute(shard, axis, [(i, i ^ 1 << apart) for i in range(lax.axis_size(axis))])


def send_rim(values, offset):
    return jax.tree.map(
        lambda part, own: part.astype(own.dtype),
        from_behind(shortened(values), "tile", offset),
        values,
    )


def swap_rim(values, bit_index):
    return jax.tree.map(
        lambda part, own: part.astype(own.dtype),
        swapped(shortened(values), "tile", bit_index),
        values,
    )


def send_back(values, offset):
    return jax.tree.map(
        lambda part, own: part.astype(own.dtype),
        from_behind(shortened(values), "tile", offset),
        values,
    )


def swap_back(values, bit_index):
    return jax.tree.map(
        lambda part, own: part.astype(own.dtype),
        swapped(shortened(values), "tile", bit_index),
        values,
    )


def link_table(face_order, face_links, my_half, face_count, which_side):
    lookup = jnp.arange(face_order.shape[0], dtype=jnp.int32)
    inverse = jnp.sum(
        lookup[None, :] * (face_order[None, :] == lookup[:, None]).astype(jnp.int32), axis=1
    ).astype(jnp.int32)
    face_ids = lax.dynamic_slice_in_dim(face_order, my_half * face_count, face_count)
    link_rows = jnp.take(face_links, face_ids, axis=0)[:, which_side]
    source = jnp.take(inverse, link_rows[:, 0])
    remote = source // face_count != my_half
    candidate = link_rows[:, 1]
    pick_index = ((link_rows[:, 2] * 2 + candidate) * face_count + source % face_count).astype(
        jnp.int32
    )
    return (pick_index, remote, link_rows[:, 2] == 1)


def make_plan(
    face_order,
    face_links,
    my_half,
    halves,
    face_count,
    grid_side,
    step_size,
    mirror_bits,
    side_pair,
    device_pos,
    along_pos,
    mask_ends,
    half_bit,
):
    plan = {
        "step": step_size,
        "far": (grid_side - 1) * step_size,
        "bits": mirror_bits,
        "half_bit": half_bit,
        "halves": halves,
        "device_pos": device_pos,
        "along_pos": along_pos,
        "grid_side": grid_side,
        "ends": mask_ends,
    }
    for label_name, which_side in (("lower", side_pair[0]), ("upper", side_pair[1])):
        plan[label_name] = link_table(face_order, face_links, my_half, face_count, which_side)
        if halves == 2:
            plan[label_name + "_partner"] = link_table(
                face_order, face_links, 1 - my_half, face_count, which_side
            )
    return plan


def end_mask(plan, length):
    positions = jnp.arange(length)
    along_pos = plan["along_pos"]
    cut_cells = (positions == 0) & (along_pos == 0) | (positions == length - 1) & (
        along_pos == plan["grid_side"] - 1
    )
    return jnp.logical_not(cut_cells)[None, :, None]


def orient(rim_strip, reverse, plan):
    turned = jnp.where(reverse[:, None, None], rim_strip[:, ::-1], rim_strip)
    if plan["ends"]:
        turned = jnp.where(end_mask(plan, rim_strip.shape[1]), turned, jnp.zeros_like(turned))
    return turned


def orient_back(rim_strip, reverse, plan):
    masked = rim_strip
    if plan["ends"]:
        masked = jnp.where(end_mask(plan, rim_strip.shape[1]), masked, jnp.zeros_like(masked))
    return jnp.where(reverse[:, None, None], masked[:, ::-1], masked)


def select_rows(stack, index):
    onehot = (index[:, None] == jnp.arange(stack.shape[0])[None, :]).astype(stack.dtype)
    chosen = jnp.einsum("fk,k...->f...", onehot, stack, preferred_element_type=jnp.float32)
    return chosen.astype(stack.dtype)


def spread_rows(values, index, rows):
    onehot = (index[:, None] == jnp.arange(rows)[None, :]).astype(jnp.float32)
    return jnp.einsum(
        "fk,f...->k...",
        onehot,
        values,
        precision=lax.Precision.HIGHEST,
        preferred_element_type=jnp.float32,
    )


def pick_links(lower_stack, upper_stack, plan):
    index_lower, remote_lower = (plan["lower"][0], plan["lower"][1])
    index_upper, remote_upper = (plan["upper"][0], plan["upper"][1])
    own_lower = select_rows(lower_stack, index_lower)
    own_upper = select_rows(upper_stack, index_upper)
    if plan["halves"] == 1:
        return (own_lower, own_upper)
    partner_lower, partner_upper = jnp.split(
        swap_rim(jnp.concatenate([lower_stack, upper_stack], axis=0), plan["half_bit"]), 2, axis=0
    )
    got_lower = select_rows(partner_lower, index_lower)
    got_upper = select_rows(partner_upper, index_upper)
    return (
        jnp.where(remote_lower[:, None, None], got_lower, own_lower),
        jnp.where(remote_upper[:, None, None], got_upper, own_upper),
    )


def pick_back(grad_lower, grad_upper, plan):
    index_lower, remote_lower = (plan["lower"][0], plan["lower"][1])
    index_upper, remote_upper = (plan["upper"][0], plan["upper"][1])
    rows = 4 * grad_lower.shape[0]
    if plan["halves"] == 1:
        return (spread_rows(grad_lower, index_lower, rows), spread_rows(grad_upper, index_upper, rows))
    stay_lower = jnp.where(remote_lower[:, None, None], 0.0, grad_lower)
    away_lower = jnp.where(remote_lower[:, None, None], grad_lower, 0.0)
    stay_upper = jnp.where(remote_upper[:, None, None], 0.0, grad_upper)
    away_upper = jnp.where(remote_upper[:, None, None], grad_upper, 0.0)
    away = jnp.concatenate(
        [spread_rows(away_lower, index_lower, rows), spread_rows(away_upper, index_upper, rows)], axis=0
    )
    back_lower, back_upper = jnp.split(swap_back(away, plan["half_bit"]), 2, axis=0)
    return (
        spread_rows(stay_lower, index_lower, rows) + back_lower,
        spread_rows(stay_upper, index_upper, rows) + back_upper,
    )


def cycled(value, plan, shift):
    count = lax.axis_size("tile")
    step_size, grid_side = (plan["step"], plan["grid_side"])
    pairs = []
    for source in range(count):
        position = source // step_size % grid_side
        moved = (position + shift) % grid_side
        pairs.append((source, source + (moved - position) * step_size))
    return lax.ppermute(value, "tile", pairs)


def mirror_masks(plan):
    mirror = sum(1 << bit_index for bit_index in plan["bits"])
    along = (plan["grid_side"] - 1) * plan["step"]
    return (mirror, mirror ^ along)


def xor_send(values, mask):
    count = lax.axis_size("tile")
    pairs = [(source, source ^ mask) for source in range(count)]
    joined = jnp.concatenate(values, axis=0)
    moved = lax.ppermute(shortened(joined), "tile", pairs).astype(joined.dtype)
    return jnp.split(moved, len(values), axis=0)


def shift_send(value, plan, shift):
    return cycled(shortened(value), plan, shift).astype(value.dtype)


def exchange(sends_list, plan):
    row_mask, both_mask = mirror_masks(plan)
    count = lax.axis_size("tile")
    received = [dict() for _ in sends_list]
    for key in ("up", "down", "row", "both"):
        pieces = [sends[key] for sends in sends_list]
        cuts = list(itertools.accumulate(piece.shape[1] for piece in pieces))[:-1]
        joined = jnp.concatenate([shortened(piece) for piece in pieces], axis=1)
        if key == "up":
            moved = cycled(joined, plan, 1)
        elif key == "down":
            moved = cycled(joined, plan, -1)
        else:
            mask = row_mask if key == "row" else both_mask
            moved = lax.ppermute(joined, "tile", [(source, source ^ mask) for source in range(count)])
        for got, piece, part in zip(received, pieces, jnp.split(moved, cuts, axis=1)):
            got[key] = part.astype(piece.dtype)
    return received


def forward_sends(lower_edge, upper_edge):
    both_edges = jnp.concatenate([lower_edge, upper_edge], axis=0)
    return {"up": upper_edge, "down": lower_edge, "row": both_edges, "both": both_edges}


def forward_finish(got, lower_edge, upper_edge, plan):
    from_lower, from_upper = (got["up"], got["down"])
    row_lower, row_upper = jnp.split(got["row"], 2, axis=0)
    both_lower, both_upper = jnp.split(got["both"], 2, axis=0)
    at_lower = plan["device_pos"] == 0
    at_upper = plan["device_pos"] == plan["grid_side"] - 1
    lower_stack = jnp.concatenate([from_lower, lower_edge, both_upper, row_lower], axis=0)
    upper_stack = jnp.concatenate([from_upper, upper_edge, both_lower, row_upper], axis=0)
    link_lower, link_upper = pick_links(lower_stack, upper_stack, plan)
    link_lower = orient(link_lower, plan["lower"][2], plan)
    link_upper = orient(link_upper, plan["upper"][2], plan)
    lower_rim = jnp.where(at_lower, link_lower, from_lower)
    upper_rim = jnp.where(at_upper, link_upper, from_upper)
    return (lower_rim, upper_rim)


def backward_sends(grad_lower, grad_upper, plan):
    at_lower = plan["device_pos"] == 0
    at_upper = plan["device_pos"] == plan["grid_side"] - 1
    near_lower = jnp.where(at_lower, 0.0, grad_lower)
    near_upper = jnp.where(at_upper, 0.0, grad_upper)
    face_count = grad_lower.shape[0]
    link_lower = orient_back(jnp.where(at_lower, grad_lower, 0.0), plan["lower"][2], plan)
    link_upper = orient_back(jnp.where(at_upper, grad_upper, 0.0), plan["upper"][2], plan)
    lower_stack, upper_stack = pick_back(link_lower, link_upper, plan)
    low = [lower_stack[k * face_count : (k + 1) * face_count] for k in range(4)]
    up = [upper_stack[k * face_count : (k + 1) * face_count] for k in range(4)]
    sends = {
        "down": near_lower + low[0],
        "up": near_upper + up[0],
        "row": jnp.concatenate([low[3], up[3]], axis=0),
        "both": jnp.concatenate([up[2], low[2]], axis=0),
    }
    return (sends, (low[1], up[1]))


def backward_finish(got, kept):
    row_lower, row_upper = jnp.split(got["row"], 2, axis=0)
    both_lower, both_upper = jnp.split(got["both"], 2, axis=0)
    grad_lower_edge = kept[0] + got["up"] + row_lower + both_lower
    grad_upper_edge = kept[1] + got["down"] + row_upper + both_upper
    return (grad_lower_edge, grad_upper_edge)


def add_ends(values, lower, upper, axis):
    first = lax.slice_in_dim(values, 0, 1, axis=axis)
    middle = lax.slice_in_dim(values, 1, values.shape[axis] - 1, axis=axis)
    last = lax.slice_in_dim(values, values.shape[axis] - 1, values.shape[axis], axis=axis)
    return jnp.concatenate(
        [first + jnp.expand_dims(lower, axis), middle, last + jnp.expand_dims(upper, axis)], axis=axis
    )


def pad_pair(tiles, grad, rim_plans):
    column_plan, row_plan = rim_plans
    back_plans = (dict(column_plan, ends=True), dict(row_plan, ends=False))
    padded, grad_tiles = (None, None)
    for stage in range(2):
        plan = rim_plans[stage]
        sends_list = []
        if tiles is not None:
            edges = (tiles[:, :, 0], tiles[:, :, -1]) if stage == 0 else (tiles[:, 0], tiles[:, -1])
            sends_list.append(forward_sends(*edges))
        if grad is not None:
            grad_edges = (grad[:, :, 0], grad[:, :, -1]) if stage == 0 else (grad[:, 0], grad[:, -1])
            grad_sends, kept = backward_sends(*grad_edges, back_plans[stage])
            sends_list.append(grad_sends)
        received = exchange(sends_list, plan)
        if tiles is not None:
            lower_rim, upper_rim = forward_finish(received[0], *edges, plan)
            tiles = jnp.concatenate(
                [jnp.expand_dims(lower_rim, 2 - stage), tiles, jnp.expand_dims(upper_rim, 2 - stage)],
                axis=2 - stage,
            )
        if grad is not None:
            lower_grad, upper_grad = backward_finish(received[-1], kept)
            inner = grad[:, :, 1:-1] if stage == 0 else grad[:, 1:-1]
            grad = add_ends(inner, lower_grad, upper_grad, 2 - stage)
    return (tiles, grad)


def convolve(padded, weight):
    channels = weight.shape[-1]
    kernel = weight.reshape(3, 3, weight.shape[1], channels)
    return lax.conv_general_dilated(
        padded,
        kernel,
        (1, 1),
        "VALID",
        dimension_numbers=("NHWC", "HWIO", "NHWC"),
        preferred_element_type=jnp.float32,
    )


def convolve_back(grad, weight):
    kernel = weight.reshape(3, 3, weight.shape[1], weight.shape[2])[::-1, ::-1]
    return lax.conv_general_dilated(
        grad,
        kernel,
        (1, 1),
        ((2, 2), (2, 2)),
        dimension_numbers=("NHWC", "HWOI", "NHWC"),
        preferred_element_type=jnp.float32,
    )


def weight_grad(padded, grad):
    summed = lax.conv_general_dilated(
        padded,
        grad,
        (1, 1),
        "VALID",
        dimension_numbers=("CHWN", "IHWO", "HWNC"),
        preferred_element_type=jnp.float32,
    )
    return summed.reshape((9,) + summed.shape[2:])


def local(fields, weight_one, weight_two, cotangent, face_links, face_order):
    local_tiles = fields[0]
    face_count = local_tiles.shape[0]
    extent = local_tiles.shape[1]
    devices = lax.axis_size("tile")
    grid_side = math.isqrt(devices * face_count // 12)
    halves = devices // (grid_side * grid_side)
    levels = grid_side.bit_length() - 1
    device = lax.axis_index("tile")
    my_half = device // (grid_side * grid_side)
    grid_row = device // grid_side % grid_side
    grid_col = device % grid_side
    column_plan = make_plan(
        face_order,
        face_links,
        my_half,
        halves,
        face_count,
        grid_side,
        1,
        list(range(levels, 2 * levels)),
        (2, 3),
        grid_col,
        grid_row,
        False,
        2 * levels,
    )
    row_plan = make_plan(
        face_order,
        face_links,
        my_half,
        halves,
        face_count,
        grid_side,
        grid_side,
        list(range(levels)),
        (0, 1),
        grid_row,
        grid_col,
        True,
        2 * levels,
    )
    rim_plans = (column_plan, row_plan)
    grad_out = cotangent[0]
    rim_two = convolve_back(grad_out, weight_two).astype(jnp.bfloat16)
    rim_two = lax.optimization_barrier(rim_two).astype(jnp.float32)
    padded_in, grad_hidden = pad_pair(local_tiles, rim_two, rim_plans)
    pre_act = convolve(padded_in, weight_one)
    hidden = jax.nn.gelu(pre_act, approximate=True).astype(jnp.bfloat16)
    padded_hidden = pad_pair(hidden, None, rim_plans)[0]
    second = convolve(padded_hidden, weight_two)
    block_output = (local_tiles.astype(jnp.float32) + second).astype(jnp.bfloat16)
    grad_scale = 1.0 / math.sqrt(lax.axis_size("dp") * 12 * (grid_side * extent) ** 2)
    local_two = weight_grad(padded_hidden, grad_out) * grad_scale
    gelu_pair = jax.vjp(partial(jax.nn.gelu, approximate=True), pre_act)
    grad_pre = gelu_pair[1](grad_hidden)[0].astype(jnp.bfloat16)
    local_one = weight_grad(padded_in, grad_pre) * grad_scale
    rim_one = convolve_back(grad_pre, weight_one).astype(jnp.bfloat16)
    rim_one, local_one, local_two = lax.optimization_barrier((rim_one, local_one, local_two))
    rim_one = rim_one.astype(jnp.float32)
    field_grad = (grad_out.astype(jnp.float32) + pad_pair(None, rim_one, rim_plans)[1]).astype(jnp.bfloat16)
    grad_one, grad_two = lax.psum((local_one, local_two), ("tile", "dp"))
    return (block_output[None], field_grad[None], grad_one, grad_two)


def solution(mesh):
    in_specs = (
        P("dp", "tile", None, None, None),
        P(),
        P(),
        P("dp", "tile", None, None, None),
        P(),
        P(),
    )
    out_specs = (P("dp", "tile", None, None, None), P("dp", "tile", None, None, None), P(), P())
    return jax.shard_map(local, mesh=mesh, in_specs=in_specs, out_specs=out_specs, check_vma=False)
```

```python
from functools import partial
import itertools
import math

import jax
import jax.numpy as jnp
from jax import lax
from jax.sharding import PartitionSpec as P


def shortened(shard):
    return jax.tree.map(lambda a: a.astype(jnp.bfloat16) if a.dtype == jnp.float32 else a, shard)


def from_behind(value, axis, steps):
    count = lax.axis_size(axis)
    first, last = (max(0, -steps), min(count, count - steps))
    return lax.ppermute(value, axis, [(source, source + steps) for source in range(first, last)])


def swapped(shard, axis, apart):
    return lax.ppermute(shard, axis, [(i, i ^ 1 << apart) for i in range(lax.axis_size(axis))])


def send_rim(values, offset):
    return jax.tree.map(
        lambda part, own: part.astype(own.dtype),
        from_behind(shortened(values), "tile", offset),
        values,
    )


def swap_rim(values, bit_index):
    return jax.tree.map(
        lambda part, own: part.astype(own.dtype),
        swapped(shortened(values), "tile", bit_index),
        values,
    )


def send_back(values, offset):
    return jax.tree.map(
        lambda part, own: part.astype(own.dtype),
        from_behind(shortened(values), "tile", offset),
        values,
    )


def swap_back(values, bit_index):
    return jax.tree.map(
        lambda part, own: part.astype(own.dtype),
        swapped(shortened(values), "tile", bit_index),
        values,
    )


def link_table(face_order, face_links, my_half, face_count, which_side):
    lookup = jnp.arange(face_order.shape[0], dtype=jnp.int32)
    inverse = jnp.sum(
        lookup[None, :] * (face_order[None, :] == lookup[:, None]).astype(jnp.int32), axis=1
    ).astype(jnp.int32)
    face_ids = lax.dynamic_slice_in_dim(face_order, my_half * face_count, face_count)
    link_rows = jnp.take(face_links, face_ids, axis=0)[:, which_side]
    source = jnp.take(inverse, link_rows[:, 0])
    remote = source // face_count != my_half
    candidate = link_rows[:, 1]
    pick_index = ((link_rows[:, 2] * 2 + candidate) * face_count + source % face_count).astype(
        jnp.int32
    )
    return (pick_index, remote, link_rows[:, 2] == 1)


def make_plan(
    face_order,
    face_links,
    my_half,
    halves,
    face_count,
    grid_side,
    step_size,
    mirror_bits,
    side_pair,
    device_pos,
    along_pos,
    mask_ends,
    half_bit,
):
    plan = {
        "step": step_size,
        "far": (grid_side - 1) * step_size,
        "bits": mirror_bits,
        "half_bit": half_bit,
        "halves": halves,
        "device_pos": device_pos,
        "along_pos": along_pos,
        "grid_side": grid_side,
        "ends": mask_ends,
    }
    for label_name, which_side in (("lower", side_pair[0]), ("upper", side_pair[1])):
        plan[label_name] = link_table(face_order, face_links, my_half, face_count, which_side)
        if halves == 2:
            plan[label_name + "_partner"] = link_table(
                face_order, face_links, 1 - my_half, face_count, which_side
            )
    return plan


def end_mask(plan, length):
    positions = jnp.arange(length)
    along_pos = plan["along_pos"]
    cut_cells = (positions == 0) & (along_pos == 0) | (positions == length - 1) & (
        along_pos == plan["grid_side"] - 1
    )
    return jnp.logical_not(cut_cells)[None, :, None]


def orient(rim_strip, reverse, plan):
    turned = jnp.where(reverse[:, None, None], rim_strip[:, ::-1], rim_strip)
    if plan["ends"]:
        turned = jnp.where(end_mask(plan, rim_strip.shape[1]), turned, jnp.zeros_like(turned))
    return turned


def orient_back(rim_strip, reverse, plan):
    masked = rim_strip
    if plan["ends"]:
        masked = jnp.where(end_mask(plan, rim_strip.shape[1]), masked, jnp.zeros_like(masked))
    return jnp.where(reverse[:, None, None], masked[:, ::-1], masked)


def select_rows(stack, index):
    onehot = (index[:, None] == jnp.arange(stack.shape[0])[None, :]).astype(stack.dtype)
    chosen = jnp.einsum("fk,k...->f...", onehot, stack, preferred_element_type=jnp.float32)
    return chosen.astype(stack.dtype)


def spread_rows(values, index, rows):
    onehot = (index[:, None] == jnp.arange(rows)[None, :]).astype(jnp.float32)
    return jnp.einsum(
        "fk,f...->k...",
        onehot,
        values,
        precision=lax.Precision.HIGHEST,
        preferred_element_type=jnp.float32,
    )


def pick_links(lower_stack, upper_stack, plan):
    index_lower, remote_lower = (plan["lower"][0], plan["lower"][1])
    index_upper, remote_upper = (plan["upper"][0], plan["upper"][1])
    own_lower = select_rows(lower_stack, index_lower)
    own_upper = select_rows(upper_stack, index_upper)
    if plan["halves"] == 1:
        return (own_lower, own_upper)
    partner_lower, partner_upper = jnp.split(
        swap_rim(jnp.concatenate([lower_stack, upper_stack], axis=0), plan["half_bit"]), 2, axis=0
    )
    got_lower = select_rows(partner_lower, index_lower)
    got_upper = select_rows(partner_upper, index_upper)
    return (
        jnp.where(remote_lower[:, None, None], got_lower, own_lower),
        jnp.where(remote_upper[:, None, None], got_upper, own_upper),
    )


def pick_back(grad_lower, grad_upper, plan):
    index_lower, remote_lower = (plan["lower"][0], plan["lower"][1])
    index_upper, remote_upper = (plan["upper"][0], plan["upper"][1])
    rows = 4 * grad_lower.shape[0]
    if plan["halves"] == 1:
        return (spread_rows(grad_lower, index_lower, rows), spread_rows(grad_upper, index_upper, rows))
    stay_lower = jnp.where(remote_lower[:, None, None], 0.0, grad_lower)
    away_lower = jnp.where(remote_lower[:, None, None], grad_lower, 0.0)
    stay_upper = jnp.where(remote_upper[:, None, None], 0.0, grad_upper)
    away_upper = jnp.where(remote_upper[:, None, None], grad_upper, 0.0)
    away = jnp.concatenate(
        [spread_rows(away_lower, index_lower, rows), spread_rows(away_upper, index_upper, rows)], axis=0
    )
    back_lower, back_upper = jnp.split(swap_back(away, plan["half_bit"]), 2, axis=0)
    return (
        spread_rows(stay_lower, index_lower, rows) + back_lower,
        spread_rows(stay_upper, index_upper, rows) + back_upper,
    )


def cycled(value, plan, shift):
    count = lax.axis_size("tile")
    step_size, grid_side = (plan["step"], plan["grid_side"])
    pairs = []
    for source in range(count):
        position = source // step_size % grid_side
        moved = (position + shift) % grid_side
        pairs.append((source, source + (moved - position) * step_size))
    return lax.ppermute(value, "tile", pairs)


def mirror_masks(plan):
    mirror = sum(1 << bit_index for bit_index in plan["bits"])
    along = (plan["grid_side"] - 1) * plan["step"]
    return (mirror, mirror ^ along)


def xor_send(values, mask):
    count = lax.axis_size("tile")
    pairs = [(source, source ^ mask) for source in range(count)]
    joined = jnp.concatenate(values, axis=0)
    moved = lax.ppermute(shortened(joined), "tile", pairs).astype(joined.dtype)
    return jnp.split(moved, len(values), axis=0)


def shift_send(value, plan, shift):
    return cycled(shortened(value), plan, shift).astype(value.dtype)


def exchange(sends_list, plan):
    row_mask, both_mask = mirror_masks(plan)
    count = lax.axis_size("tile")
    received = [dict() for _ in sends_list]
    for key in ("up", "down", "row", "both"):
        pieces = [sends[key] for sends in sends_list]
        flat = [shortened(piece).reshape(piece.shape[0], -1) for piece in pieces]
        cuts = list(itertools.accumulate(piece.shape[1] for piece in flat))[:-1]
        joined = jnp.concatenate(flat, axis=1)
        if key == "up":
            moved = cycled(joined, plan, 1)
        elif key == "down":
            moved = cycled(joined, plan, -1)
        else:
            mask = row_mask if key == "row" else both_mask
            moved = lax.ppermute(joined, "tile", [(source, source ^ mask) for source in range(count)])
        for got, piece, part in zip(received, pieces, jnp.split(moved, cuts, axis=1)):
            got[key] = part.reshape(piece.shape).astype(piece.dtype)
    return received


def forward_sends(lower_edge, upper_edge):
    both_edges = jnp.concatenate([lower_edge, upper_edge], axis=0)
    return {"up": upper_edge, "down": lower_edge, "row": both_edges, "both": both_edges}


def forward_finish(got, lower_edge, upper_edge, plan):
    from_lower, from_upper = (got["up"], got["down"])
    row_lower, row_upper = jnp.split(got["row"], 2, axis=0)
    both_lower, both_upper = jnp.split(got["both"], 2, axis=0)
    at_lower = plan["device_pos"] == 0
    at_upper = plan["device_pos"] == plan["grid_side"] - 1
    lower_stack = jnp.concatenate([from_lower, lower_edge, both_upper, row_lower], axis=0)
    upper_stack = jnp.concatenate([from_upper, upper_edge, both_lower, row_upper], axis=0)
    link_lower, link_upper = pick_links(lower_stack, upper_stack, plan)
    link_lower = orient(link_lower, plan["lower"][2], plan)
    link_upper = orient(link_upper, plan["upper"][2], plan)
    lower_rim = jnp.where(at_lower, link_lower, from_lower)
    upper_rim = jnp.where(at_upper, link_upper, from_upper)
    return (lower_rim, upper_rim)


def backward_sends(grad_lower, grad_upper, plan):
    at_lower = plan["device_pos"] == 0
    at_upper = plan["device_pos"] == plan["grid_side"] - 1
    near_lower = jnp.where(at_lower, 0.0, grad_lower)
    near_upper = jnp.where(at_upper, 0.0, grad_upper)
    face_count = grad_lower.shape[0]
    link_lower = orient_back(jnp.where(at_lower, grad_lower, 0.0), plan["lower"][2], plan)
    link_upper = orient_back(jnp.where(at_upper, grad_upper, 0.0), plan["upper"][2], plan)
    lower_stack, upper_stack = pick_back(link_lower, link_upper, plan)
    low = [lower_stack[k * face_count : (k + 1) * face_count] for k in range(4)]
    up = [upper_stack[k * face_count : (k + 1) * face_count] for k in range(4)]
    sends = {
        "down": near_lower + low[0],
        "up": near_upper + up[0],
        "row": jnp.concatenate([low[3], up[3]], axis=0),
        "both": jnp.concatenate([up[2], low[2]], axis=0),
    }
    return (sends, (low[1], up[1]))


def backward_finish(got, kept):
    row_lower, row_upper = jnp.split(got["row"], 2, axis=0)
    both_lower, both_upper = jnp.split(got["both"], 2, axis=0)
    grad_lower_edge = kept[0] + got["up"] + row_lower + both_lower
    grad_upper_edge = kept[1] + got["down"] + row_upper + both_upper
    return (grad_lower_edge, grad_upper_edge)


def add_ends(values, lower, upper, axis):
    first = lax.slice_in_dim(values, 0, 1, axis=axis)
    middle = lax.slice_in_dim(values, 1, values.shape[axis] - 1, axis=axis)
    last = lax.slice_in_dim(values, values.shape[axis] - 1, values.shape[axis], axis=axis)
    return jnp.concatenate(
        [first + jnp.expand_dims(lower, axis), middle, last + jnp.expand_dims(upper, axis)], axis=axis
    )


def pad_pair(tiles, grad, rim_plans):
    column_plan, row_plan = rim_plans
    back_plans = (dict(column_plan, ends=True), dict(row_plan, ends=False))
    padded, grad_tiles = (None, None)
    for stage in range(2):
        plan = rim_plans[stage]
        sends_list = []
        if tiles is not None:
            edges = (tiles[:, :, 0], tiles[:, :, -1]) if stage == 0 else (tiles[:, 0], tiles[:, -1])
            sends_list.append(forward_sends(*edges))
        if grad is not None:
            grad_edges = (grad[:, :, 0], grad[:, :, -1]) if stage == 0 else (grad[:, 0], grad[:, -1])
            grad_sends, kept = backward_sends(*grad_edges, back_plans[stage])
            sends_list.append(grad_sends)
        received = exchange(sends_list, plan)
        if tiles is not None:
            lower_rim, upper_rim = forward_finish(received[0], *edges, plan)
            tiles = jnp.concatenate(
                [jnp.expand_dims(lower_rim, 2 - stage), tiles, jnp.expand_dims(upper_rim, 2 - stage)],
                axis=2 - stage,
            )
        if grad is not None:
            lower_grad, upper_grad = backward_finish(received[-1], kept)
            inner = grad[:, :, 1:-1] if stage == 0 else grad[:, 1:-1]
            grad = add_ends(inner, lower_grad, upper_grad, 2 - stage)
    return (tiles, grad)


def convolve(padded, weight):
    channels = weight.shape[-1]
    kernel = weight.reshape(3, 3, weight.shape[1], channels)
    return lax.conv_general_dilated(
        padded,
        kernel,
        (1, 1),
        "VALID",
        dimension_numbers=("NHWC", "HWIO", "NHWC"),
        preferred_element_type=jnp.float32,
    )


def convolve_back(grad, weight):
    kernel = weight.reshape(3, 3, weight.shape[1], weight.shape[2])[::-1, ::-1]
    return lax.conv_general_dilated(
        grad,
        kernel,
        (1, 1),
        ((2, 2), (2, 2)),
        dimension_numbers=("NHWC", "HWOI", "NHWC"),
        preferred_element_type=jnp.float32,
    )


def weight_grad(padded, grad):
    summed = lax.conv_general_dilated(
        padded,
        grad,
        (1, 1),
        "VALID",
        dimension_numbers=("CHWN", "IHWO", "HWNC"),
        preferred_element_type=jnp.float32,
    )
    return summed.reshape((9,) + summed.shape[2:])


def local(fields, weight_one, weight_two, cotangent, face_links, face_order):
    local_tiles = fields[0]
    face_count = local_tiles.shape[0]
    extent = local_tiles.shape[1]
    devices = lax.axis_size("tile")
    grid_side = math.isqrt(devices * face_count // 12)
    halves = devices // (grid_side * grid_side)
    levels = grid_side.bit_length() - 1
    device = lax.axis_index("tile")
    my_half = device // (grid_side * grid_side)
    grid_row = device // grid_side % grid_side
    grid_col = device % grid_side
    column_plan = make_plan(
        face_order,
        face_links,
        my_half,
        halves,
        face_count,
        grid_side,
        1,
        list(range(levels, 2 * levels)),
        (2, 3),
        grid_col,
        grid_row,
        False,
        2 * levels,
    )
    row_plan = make_plan(
        face_order,
        face_links,
        my_half,
        halves,
        face_count,
        grid_side,
        grid_side,
        list(range(levels)),
        (0, 1),
        grid_row,
        grid_col,
        True,
        2 * levels,
    )
    rim_plans = (column_plan, row_plan)
    grad_out = cotangent[0]
    channels = grad_out.shape[-1]
    rim_two = convolve_back(grad_out, weight_two).astype(jnp.bfloat16)
    rim_two = lax.optimization_barrier(rim_two).astype(jnp.float32)
    shifted = [
        jnp.pad(grad_out, ((0, 0), (offset // 3, 2 - offset // 3), (offset % 3, 2 - offset % 3), (0, 0)))
        for offset in range(9)
    ]
    joined = jnp.concatenate([rim_two] + [part.astype(jnp.float32) for part in shifted], axis=-1)
    padded_in, joined_back = pad_pair(local_tiles, joined, rim_plans)
    grad_hidden = joined_back[..., :channels]
    gathered = joined_back[..., channels:].reshape(-1, 9, channels)
    pre_act = convolve(padded_in, weight_one)
    hidden = jax.nn.gelu(pre_act, approximate=True).astype(jnp.bfloat16)
    grad_scale = 1.0 / math.sqrt(lax.axis_size("dp") * 12 * (grid_side * extent) ** 2)
    flat_hidden = hidden.reshape(-1, channels)
    high = gathered.astype(jnp.bfloat16)
    low = (gathered - high.astype(jnp.float32)).astype(jnp.bfloat16)
    local_two = sum(
        jnp.einsum("qi,qko->kio", flat_hidden, part, preferred_element_type=jnp.float32)
        for part in (high, low)
    )
    local_two = local_two * grad_scale
    gelu_pair = jax.vjp(partial(jax.nn.gelu, approximate=True), pre_act)
    grad_pre = gelu_pair[1](grad_hidden)[0].astype(jnp.bfloat16)
    local_one = weight_grad(padded_in, grad_pre) * grad_scale
    rim_one = convolve_back(grad_pre, weight_one).astype(jnp.bfloat16)
    rim_one, local_one, local_two, hidden = lax.optimization_barrier((rim_one, local_one, local_two, hidden))
    rim_one = rim_one.astype(jnp.float32)
    padded_hidden = pad_pair(hidden, None, rim_plans)[0]
    second = convolve(padded_hidden, weight_two)
    block_output = (local_tiles.astype(jnp.float32) + second).astype(jnp.bfloat16)
    field_grad = (grad_out.astype(jnp.float32) + pad_pair(None, rim_one, rim_plans)[1]).astype(jnp.bfloat16)
    grad_one, grad_two = lax.psum((local_one, local_two), ("tile", "dp"))
    return (block_output[None], field_grad[None], grad_one, grad_two)


def solution(mesh):
    in_specs = (
        P("dp", "tile", None, None, None),
        P(),
        P(),
        P("dp", "tile", None, None, None),
        P(),
        P(),
    )
    out_specs = (P("dp", "tile", None, None, None), P("dp", "tile", None, None, None), P(), P())
    return jax.shard_map(local, mesh=mesh, in_specs=in_specs, out_specs=out_specs, check_vma=False)
```

```python
from functools import partial
import itertools
import math

import jax
import jax.numpy as jnp
from jax import lax
from jax.sharding import PartitionSpec as P


def shortened(shard):
    return jax.tree.map(lambda a: a.astype(jnp.bfloat16) if a.dtype == jnp.float32 else a, shard)


def from_behind(value, axis, steps):
    count = lax.axis_size(axis)
    first, last = (max(0, -steps), min(count, count - steps))
    return lax.ppermute(value, axis, [(source, source + steps) for source in range(first, last)])


def swapped(shard, axis, apart):
    return lax.ppermute(shard, axis, [(i, i ^ 1 << apart) for i in range(lax.axis_size(axis))])


def send_rim(values, offset):
    return jax.tree.map(
        lambda part, own: part.astype(own.dtype),
        from_behind(shortened(values), "tile", offset),
        values,
    )


def swap_rim(values, bit_index):
    return jax.tree.map(
        lambda part, own: part.astype(own.dtype),
        swapped(shortened(values), "tile", bit_index),
        values,
    )


def send_back(values, offset):
    return jax.tree.map(
        lambda part, own: part.astype(own.dtype),
        from_behind(shortened(values), "tile", offset),
        values,
    )


def swap_back(values, bit_index):
    return jax.tree.map(
        lambda part, own: part.astype(own.dtype),
        swapped(shortened(values), "tile", bit_index),
        values,
    )


def link_table(face_order, face_links, my_half, face_count, which_side):
    lookup = jnp.arange(face_order.shape[0], dtype=jnp.int32)
    inverse = jnp.sum(
        lookup[None, :] * (face_order[None, :] == lookup[:, None]).astype(jnp.int32), axis=1
    ).astype(jnp.int32)
    face_ids = lax.dynamic_slice_in_dim(face_order, my_half * face_count, face_count)
    link_rows = jnp.take(face_links, face_ids, axis=0)[:, which_side]
    source = jnp.take(inverse, link_rows[:, 0])
    remote = source // face_count != my_half
    candidate = link_rows[:, 1]
    pick_index = ((link_rows[:, 2] * 2 + candidate) * face_count + source % face_count).astype(
        jnp.int32
    )
    return (pick_index, remote, link_rows[:, 2] == 1)


def make_plan(
    face_order,
    face_links,
    my_half,
    halves,
    face_count,
    grid_side,
    step_size,
    mirror_bits,
    side_pair,
    device_pos,
    along_pos,
    mask_ends,
    half_bit,
):
    plan = {
        "step": step_size,
        "far": (grid_side - 1) * step_size,
        "bits": mirror_bits,
        "half_bit": half_bit,
        "halves": halves,
        "device_pos": device_pos,
        "along_pos": along_pos,
        "grid_side": grid_side,
        "ends": mask_ends,
    }
    for label_name, which_side in (("lower", side_pair[0]), ("upper", side_pair[1])):
        plan[label_name] = link_table(face_order, face_links, my_half, face_count, which_side)
        if halves == 2:
            plan[label_name + "_partner"] = link_table(
                face_order, face_links, 1 - my_half, face_count, which_side
            )
    return plan


def end_mask(plan, length):
    positions = jnp.arange(length)
    along_pos = plan["along_pos"]
    cut_cells = (positions == 0) & (along_pos == 0) | (positions == length - 1) & (
        along_pos == plan["grid_side"] - 1
    )
    return jnp.logical_not(cut_cells)[None, :, None]


def orient(rim_strip, reverse, plan):
    turned = jnp.where(reverse[:, None, None], rim_strip[:, ::-1], rim_strip)
    if plan["ends"]:
        turned = jnp.where(end_mask(plan, rim_strip.shape[1]), turned, jnp.zeros_like(turned))
    return turned


def orient_back(rim_strip, reverse, plan):
    masked = rim_strip
    if plan["ends"]:
        masked = jnp.where(end_mask(plan, rim_strip.shape[1]), masked, jnp.zeros_like(masked))
    return jnp.where(reverse[:, None, None], masked[:, ::-1], masked)


def select_rows(stack, index):
    onehot = (index[:, None] == jnp.arange(stack.shape[0])[None, :]).astype(stack.dtype)
    chosen = jnp.einsum("fk,k...->f...", onehot, stack, preferred_element_type=jnp.float32)
    return chosen.astype(stack.dtype)


def spread_rows(values, index, rows):
    onehot = (index[:, None] == jnp.arange(rows)[None, :]).astype(jnp.float32)
    return jnp.einsum(
        "fk,f...->k...",
        onehot,
        values,
        precision=lax.Precision.HIGHEST,
        preferred_element_type=jnp.float32,
    )


def pick_links(lower_stack, upper_stack, plan):
    index_lower, remote_lower = (plan["lower"][0], plan["lower"][1])
    index_upper, remote_upper = (plan["upper"][0], plan["upper"][1])
    own_lower = select_rows(lower_stack, index_lower)
    own_upper = select_rows(upper_stack, index_upper)
    if plan["halves"] == 1:
        return (own_lower, own_upper)
    partner_lower, partner_upper = jnp.split(
        swap_rim(jnp.concatenate([lower_stack, upper_stack], axis=0), plan["half_bit"]), 2, axis=0
    )
    got_lower = select_rows(partner_lower, index_lower)
    got_upper = select_rows(partner_upper, index_upper)
    return (
        jnp.where(remote_lower[:, None, None], got_lower, own_lower),
        jnp.where(remote_upper[:, None, None], got_upper, own_upper),
    )


def pick_back(grad_lower, grad_upper, plan):
    index_lower, remote_lower = (plan["lower"][0], plan["lower"][1])
    index_upper, remote_upper = (plan["upper"][0], plan["upper"][1])
    rows = 4 * grad_lower.shape[0]
    if plan["halves"] == 1:
        return (spread_rows(grad_lower, index_lower, rows), spread_rows(grad_upper, index_upper, rows))
    stay_lower = jnp.where(remote_lower[:, None, None], 0.0, grad_lower)
    away_lower = jnp.where(remote_lower[:, None, None], grad_lower, 0.0)
    stay_upper = jnp.where(remote_upper[:, None, None], 0.0, grad_upper)
    away_upper = jnp.where(remote_upper[:, None, None], grad_upper, 0.0)
    away = jnp.concatenate(
        [spread_rows(away_lower, index_lower, rows), spread_rows(away_upper, index_upper, rows)], axis=0
    )
    back_lower, back_upper = jnp.split(swap_back(away, plan["half_bit"]), 2, axis=0)
    return (
        spread_rows(stay_lower, index_lower, rows) + back_lower,
        spread_rows(stay_upper, index_upper, rows) + back_upper,
    )


def cycled(value, plan, shift):
    count = lax.axis_size("tile")
    step_size, grid_side = (plan["step"], plan["grid_side"])
    pairs = []
    for source in range(count):
        position = source // step_size % grid_side
        moved = (position + shift) % grid_side
        pairs.append((source, source + (moved - position) * step_size))
    return lax.ppermute(value, "tile", pairs)


def mirror_masks(plan):
    mirror = sum(1 << bit_index for bit_index in plan["bits"])
    along = (plan["grid_side"] - 1) * plan["step"]
    return (mirror, mirror ^ along)


def xor_send(values, mask):
    count = lax.axis_size("tile")
    pairs = [(source, source ^ mask) for source in range(count)]
    joined = jnp.concatenate(values, axis=0)
    moved = lax.ppermute(shortened(joined), "tile", pairs).astype(joined.dtype)
    return jnp.split(moved, len(values), axis=0)


def shift_send(value, plan, shift):
    return cycled(shortened(value), plan, shift).astype(value.dtype)


def exchange(sends_list, plan):
    row_mask, both_mask = mirror_masks(plan)
    count = lax.axis_size("tile")
    received = [dict() for _ in sends_list]
    for key in ("up", "down", "row", "both"):
        pieces = [sends[key] for sends in sends_list]
        cuts = list(itertools.accumulate(piece.shape[1] for piece in pieces))[:-1]
        joined = jnp.concatenate([shortened(piece) for piece in pieces], axis=1)
        if key == "up":
            moved = cycled(joined, plan, 1)
        elif key == "down":
            moved = cycled(joined, plan, -1)
        else:
            mask = row_mask if key == "row" else both_mask
            moved = lax.ppermute(joined, "tile", [(source, source ^ mask) for source in range(count)])
        for got, piece, part in zip(received, pieces, jnp.split(moved, cuts, axis=1)):
            got[key] = part.astype(piece.dtype)
    return received


def forward_sends(lower_edge, upper_edge):
    both_edges = jnp.concatenate([lower_edge, upper_edge], axis=0)
    return {"up": upper_edge, "down": lower_edge, "row": both_edges, "both": both_edges}


def forward_finish(got, lower_edge, upper_edge, plan):
    from_lower, from_upper = (got["up"], got["down"])
    row_lower, row_upper = jnp.split(got["row"], 2, axis=0)
    both_lower, both_upper = jnp.split(got["both"], 2, axis=0)
    at_lower = plan["device_pos"] == 0
    at_upper = plan["device_pos"] == plan["grid_side"] - 1
    lower_stack = jnp.concatenate([from_lower, lower_edge, both_upper, row_lower], axis=0)
    upper_stack = jnp.concatenate([from_upper, upper_edge, both_lower, row_upper], axis=0)
    link_lower, link_upper = pick_links(lower_stack, upper_stack, plan)
    link_lower = orient(link_lower, plan["lower"][2], plan)
    link_upper = orient(link_upper, plan["upper"][2], plan)
    lower_rim = jnp.where(at_lower, link_lower, from_lower)
    upper_rim = jnp.where(at_upper, link_upper, from_upper)
    return (lower_rim, upper_rim)


def backward_sends(grad_lower, grad_upper, plan):
    at_lower = plan["device_pos"] == 0
    at_upper = plan["device_pos"] == plan["grid_side"] - 1
    near_lower = jnp.where(at_lower, 0.0, grad_lower)
    near_upper = jnp.where(at_upper, 0.0, grad_upper)
    face_count = grad_lower.shape[0]
    link_lower = orient_back(jnp.where(at_lower, grad_lower, 0.0), plan["lower"][2], plan)
    link_upper = orient_back(jnp.where(at_upper, grad_upper, 0.0), plan["upper"][2], plan)
    lower_stack, upper_stack = pick_back(link_lower, link_upper, plan)
    low = [lower_stack[k * face_count : (k + 1) * face_count] for k in range(4)]
    up = [upper_stack[k * face_count : (k + 1) * face_count] for k in range(4)]
    sends = {
        "down": near_lower + low[0],
        "up": near_upper + up[0],
        "row": jnp.concatenate([low[3], up[3]], axis=0),
        "both": jnp.concatenate([up[2], low[2]], axis=0),
    }
    return (sends, (low[1], up[1]))


def backward_finish(got, kept):
    row_lower, row_upper = jnp.split(got["row"], 2, axis=0)
    both_lower, both_upper = jnp.split(got["both"], 2, axis=0)
    grad_lower_edge = kept[0] + got["up"] + row_lower + both_lower
    grad_upper_edge = kept[1] + got["down"] + row_upper + both_upper
    return (grad_lower_edge, grad_upper_edge)


def add_ends(values, lower, upper, axis):
    first = lax.slice_in_dim(values, 0, 1, axis=axis)
    middle = lax.slice_in_dim(values, 1, values.shape[axis] - 1, axis=axis)
    last = lax.slice_in_dim(values, values.shape[axis] - 1, values.shape[axis], axis=axis)
    return jnp.concatenate(
        [first + jnp.expand_dims(lower, axis), middle, last + jnp.expand_dims(upper, axis)], axis=axis
    )


def pad_pair(tiles, grad, rim_plans):
    column_plan, row_plan = rim_plans
    back_plans = (dict(column_plan, ends=True), dict(row_plan, ends=False))
    padded, grad_tiles = (None, None)
    for stage in range(2):
        plan = rim_plans[stage]
        sends_list = []
        if tiles is not None:
            edges = (tiles[:, :, 0], tiles[:, :, -1]) if stage == 0 else (tiles[:, 0], tiles[:, -1])
            sends_list.append(forward_sends(*edges))
        if grad is not None:
            grad_edges = (grad[:, :, 0], grad[:, :, -1]) if stage == 0 else (grad[:, 0], grad[:, -1])
            grad_sends, kept = backward_sends(*grad_edges, back_plans[stage])
            sends_list.append(grad_sends)
        received = exchange(sends_list, plan)
        if tiles is not None:
            lower_rim, upper_rim = forward_finish(received[0], *edges, plan)
            tiles = jnp.concatenate(
                [jnp.expand_dims(lower_rim, 2 - stage), tiles, jnp.expand_dims(upper_rim, 2 - stage)],
                axis=2 - stage,
            )
        if grad is not None:
            lower_grad, upper_grad = backward_finish(received[-1], kept)
            inner = grad[:, :, 1:-1] if stage == 0 else grad[:, 1:-1]
            grad = add_ends(inner, lower_grad, upper_grad, 2 - stage)
    return (tiles, grad)


def convolve(padded, weight):
    channels = weight.shape[-1]
    kernel = weight.reshape(3, 3, weight.shape[1], channels)
    return lax.conv_general_dilated(
        padded,
        kernel,
        (1, 1),
        "VALID",
        dimension_numbers=("NHWC", "HWIO", "NHWC"),
        preferred_element_type=jnp.float32,
    )


def convolve_back(grad, weight):
    kernel = weight.reshape(3, 3, weight.shape[1], weight.shape[2])[::-1, ::-1]
    return lax.conv_general_dilated(
        grad,
        kernel,
        (1, 1),
        ((2, 2), (2, 2)),
        dimension_numbers=("NHWC", "HWOI", "NHWC"),
        preferred_element_type=jnp.float32,
    )


def weight_grad(padded, grad):
    summed = lax.conv_general_dilated(
        padded,
        grad,
        (1, 1),
        "VALID",
        dimension_numbers=("CHWN", "IHWO", "HWNC"),
        preferred_element_type=jnp.float32,
    )
    return summed.reshape((9,) + summed.shape[2:])


def local(fields, weight_one, weight_two, cotangent, face_links, face_order):
    local_tiles = fields[0]
    face_count = local_tiles.shape[0]
    extent = local_tiles.shape[1]
    devices = lax.axis_size("tile")
    grid_side = math.isqrt(devices * face_count // 12)
    halves = devices // (grid_side * grid_side)
    levels = grid_side.bit_length() - 1
    device = lax.axis_index("tile")
    my_half = device // (grid_side * grid_side)
    grid_row = device // grid_side % grid_side
    grid_col = device % grid_side
    column_plan = make_plan(
        face_order,
        face_links,
        my_half,
        halves,
        face_count,
        grid_side,
        1,
        list(range(levels, 2 * levels)),
        (2, 3),
        grid_col,
        grid_row,
        False,
        2 * levels,
    )
    row_plan = make_plan(
        face_order,
        face_links,
        my_half,
        halves,
        face_count,
        grid_side,
        grid_side,
        list(range(levels)),
        (0, 1),
        grid_row,
        grid_col,
        True,
        2 * levels,
    )
    rim_plans = (column_plan, row_plan)
    grad_out = cotangent[0]
    rim_two = convolve_back(grad_out, weight_two).astype(jnp.bfloat16)
    rim_two = lax.optimization_barrier(rim_two).astype(jnp.float32)
    padded_in, grad_hidden = pad_pair(local_tiles, rim_two, rim_plans)
    pre_act = convolve(padded_in, weight_one)
    hidden = jax.nn.gelu(pre_act, approximate=True).astype(jnp.bfloat16)
    padded_hidden = pad_pair(hidden, None, rim_plans)[0]
    grad_scale = 1.0 / math.sqrt(lax.axis_size("dp") * 12 * (grid_side * extent) ** 2)
    local_two = weight_grad(padded_hidden, grad_out) * grad_scale
    gelu_pair = jax.vjp(partial(jax.nn.gelu, approximate=True), pre_act)
    grad_pre = gelu_pair[1](grad_hidden)[0].astype(jnp.bfloat16)
    local_one = weight_grad(padded_in, grad_pre) * grad_scale
    rim_one = convolve_back(grad_pre, weight_one).astype(jnp.bfloat16)
    rim_one, local_one, local_two, padded_hidden = lax.optimization_barrier(
        (rim_one, local_one, local_two, padded_hidden)
    )
    rim_one = rim_one.astype(jnp.float32)
    second = convolve(padded_hidden, weight_two)
    block_output = (local_tiles.astype(jnp.float32) + second).astype(jnp.bfloat16)
    field_grad = (grad_out.astype(jnp.float32) + pad_pair(None, rim_one, rim_plans)[1]).astype(jnp.bfloat16)
    grad_one, grad_two = lax.psum((local_one, local_two), ("tile", "dp"))
    return (block_output[None], field_grad[None], grad_one, grad_two)


def solution(mesh):
    in_specs = (
        P("dp", "tile", None, None, None),
        P(),
        P(),
        P("dp", "tile", None, None, None),
        P(),
        P(),
    )
    out_specs = (P("dp", "tile", None, None, None), P("dp", "tile", None, None, None), P(), P())
    return jax.shard_map(local, mesh=mesh, in_specs=in_specs, out_specs=out_specs, check_vma=False)
```

```python
from functools import partial
import itertools
import math

import jax
import jax.numpy as jnp
from jax import lax
from jax.sharding import PartitionSpec as P


def shortened(shard):
    return jax.tree.map(lambda a: a.astype(jnp.bfloat16) if a.dtype == jnp.float32 else a, shard)


def from_behind(value, axis, steps):
    count = lax.axis_size(axis)
    first, last = (max(0, -steps), min(count, count - steps))
    return lax.ppermute(value, axis, [(source, source + steps) for source in range(first, last)])


def swapped(shard, axis, apart):
    return lax.ppermute(shard, axis, [(i, i ^ 1 << apart) for i in range(lax.axis_size(axis))])


def send_rim(values, offset):
    return jax.tree.map(
        lambda part, own: part.astype(own.dtype),
        from_behind(shortened(values), "tile", offset),
        values,
    )


def swap_rim(values, bit_index):
    return jax.tree.map(
        lambda part, own: part.astype(own.dtype),
        swapped(shortened(values), "tile", bit_index),
        values,
    )


def send_back(values, offset):
    return jax.tree.map(
        lambda part, own: part.astype(own.dtype),
        from_behind(shortened(values), "tile", offset),
        values,
    )


def swap_back(values, bit_index):
    return jax.tree.map(
        lambda part, own: part.astype(own.dtype),
        swapped(shortened(values), "tile", bit_index),
        values,
    )


def link_table(face_order, face_links, my_half, face_count, which_side):
    lookup = jnp.arange(face_order.shape[0], dtype=jnp.int32)
    inverse = jnp.sum(
        lookup[None, :] * (face_order[None, :] == lookup[:, None]).astype(jnp.int32), axis=1
    ).astype(jnp.int32)
    face_ids = lax.dynamic_slice_in_dim(face_order, my_half * face_count, face_count)
    link_rows = jnp.take(face_links, face_ids, axis=0)[:, which_side]
    source = jnp.take(inverse, link_rows[:, 0])
    remote = source // face_count != my_half
    candidate = link_rows[:, 1]
    pick_index = ((link_rows[:, 2] * 2 + candidate) * face_count + source % face_count).astype(
        jnp.int32
    )
    return (pick_index, remote, link_rows[:, 2] == 1)


def make_plan(
    face_order,
    face_links,
    my_half,
    halves,
    face_count,
    grid_side,
    step_size,
    mirror_bits,
    side_pair,
    device_pos,
    along_pos,
    mask_ends,
    half_bit,
):
    plan = {
        "step": step_size,
        "far": (grid_side - 1) * step_size,
        "bits": mirror_bits,
        "half_bit": half_bit,
        "halves": halves,
        "device_pos": device_pos,
        "along_pos": along_pos,
        "grid_side": grid_side,
        "ends": mask_ends,
    }
    for label_name, which_side in (("lower", side_pair[0]), ("upper", side_pair[1])):
        plan[label_name] = link_table(face_order, face_links, my_half, face_count, which_side)
        if halves == 2:
            plan[label_name + "_partner"] = link_table(
                face_order, face_links, 1 - my_half, face_count, which_side
            )
    return plan


def end_mask(plan, length):
    positions = jnp.arange(length)
    along_pos = plan["along_pos"]
    cut_cells = (positions == 0) & (along_pos == 0) | (positions == length - 1) & (
        along_pos == plan["grid_side"] - 1
    )
    return jnp.logical_not(cut_cells)[None, :, None]


def orient(rim_strip, reverse, plan):
    turned = jnp.where(reverse[:, None, None], rim_strip[:, ::-1], rim_strip)
    if plan["ends"]:
        turned = jnp.where(end_mask(plan, rim_strip.shape[1]), turned, jnp.zeros_like(turned))
    return turned


def orient_back(rim_strip, reverse, plan):
    masked = rim_strip
    if plan["ends"]:
        masked = jnp.where(end_mask(plan, rim_strip.shape[1]), masked, jnp.zeros_like(masked))
    return jnp.where(reverse[:, None, None], masked[:, ::-1], masked)


def select_rows(stack, index):
    onehot = (index[:, None] == jnp.arange(stack.shape[0])[None, :]).astype(stack.dtype)
    chosen = jnp.einsum("fk,k...->f...", onehot, stack, preferred_element_type=jnp.float32)
    return chosen.astype(stack.dtype)


def spread_rows(values, index, rows):
    onehot = (index[:, None] == jnp.arange(rows)[None, :]).astype(jnp.float32)
    return jnp.einsum(
        "fk,f...->k...",
        onehot,
        values,
        precision=lax.Precision.HIGHEST,
        preferred_element_type=jnp.float32,
    )


def pick_links(lower_stack, upper_stack, plan):
    index_lower, remote_lower = (plan["lower"][0], plan["lower"][1])
    index_upper, remote_upper = (plan["upper"][0], plan["upper"][1])
    own_lower = select_rows(lower_stack, index_lower)
    own_upper = select_rows(upper_stack, index_upper)
    if plan["halves"] == 1:
        return (own_lower, own_upper)
    partner_lower, partner_upper = jnp.split(
        swap_rim(jnp.concatenate([lower_stack, upper_stack], axis=0), plan["half_bit"]), 2, axis=0
    )
    got_lower = select_rows(partner_lower, index_lower)
    got_upper = select_rows(partner_upper, index_upper)
    return (
        jnp.where(remote_lower[:, None, None], got_lower, own_lower),
        jnp.where(remote_upper[:, None, None], got_upper, own_upper),
    )


def pick_back(grad_lower, grad_upper, plan):
    index_lower, remote_lower = (plan["lower"][0], plan["lower"][1])
    index_upper, remote_upper = (plan["upper"][0], plan["upper"][1])
    rows = 4 * grad_lower.shape[0]
    if plan["halves"] == 1:
        return (spread_rows(grad_lower, index_lower, rows), spread_rows(grad_upper, index_upper, rows))
    stay_lower = jnp.where(remote_lower[:, None, None], 0.0, grad_lower)
    away_lower = jnp.where(remote_lower[:, None, None], grad_lower, 0.0)
    stay_upper = jnp.where(remote_upper[:, None, None], 0.0, grad_upper)
    away_upper = jnp.where(remote_upper[:, None, None], grad_upper, 0.0)
    away = jnp.concatenate(
        [spread_rows(away_lower, index_lower, rows), spread_rows(away_upper, index_upper, rows)], axis=0
    )
    back_lower, back_upper = jnp.split(swap_back(away, plan["half_bit"]), 2, axis=0)
    return (
        spread_rows(stay_lower, index_lower, rows) + back_lower,
        spread_rows(stay_upper, index_upper, rows) + back_upper,
    )


def cycled(value, plan, shift):
    count = lax.axis_size("tile")
    step_size, grid_side = (plan["step"], plan["grid_side"])
    pairs = []
    for source in range(count):
        position = source // step_size % grid_side
        moved = (position + shift) % grid_side
        pairs.append((source, source + (moved - position) * step_size))
    return lax.ppermute(value, "tile", pairs)


def mirror_masks(plan):
    mirror = sum(1 << bit_index for bit_index in plan["bits"])
    along = (plan["grid_side"] - 1) * plan["step"]
    return (mirror, mirror ^ along)


def xor_send(values, mask):
    count = lax.axis_size("tile")
    pairs = [(source, source ^ mask) for source in range(count)]
    joined = jnp.concatenate(values, axis=0)
    moved = lax.ppermute(shortened(joined), "tile", pairs).astype(joined.dtype)
    return jnp.split(moved, len(values), axis=0)


def shift_send(value, plan, shift):
    return cycled(shortened(value), plan, shift).astype(value.dtype)


def exchange(sends_list, plan):
    row_mask, both_mask = mirror_masks(plan)
    count = lax.axis_size("tile")
    received = [dict() for _ in sends_list]
    for key in ("up", "down", "row", "both"):
        pieces = [sends[key] for sends in sends_list]
        cuts = list(itertools.accumulate(piece.shape[1] for piece in pieces))[:-1]
        joined = jnp.concatenate([shortened(piece) for piece in pieces], axis=1)
        if key == "up":
            moved = cycled(joined, plan, 1)
        elif key == "down":
            moved = cycled(joined, plan, -1)
        else:
            mask = row_mask if key == "row" else both_mask
            moved = lax.ppermute(joined, "tile", [(source, source ^ mask) for source in range(count)])
        for got, piece, part in zip(received, pieces, jnp.split(moved, cuts, axis=1)):
            got[key] = part.astype(piece.dtype)
    return received


def forward_sends(lower_edge, upper_edge):
    both_edges = jnp.concatenate([lower_edge, upper_edge], axis=0)
    return {"up": upper_edge, "down": lower_edge, "row": both_edges, "both": both_edges}


def forward_finish(got, lower_edge, upper_edge, plan):
    from_lower, from_upper = (got["up"], got["down"])
    row_lower, row_upper = jnp.split(got["row"], 2, axis=0)
    both_lower, both_upper = jnp.split(got["both"], 2, axis=0)
    at_lower = plan["device_pos"] == 0
    at_upper = plan["device_pos"] == plan["grid_side"] - 1
    lower_stack = jnp.concatenate([from_lower, lower_edge, both_upper, row_lower], axis=0)
    upper_stack = jnp.concatenate([from_upper, upper_edge, both_lower, row_upper], axis=0)
    link_lower, link_upper = pick_links(lower_stack, upper_stack, plan)
    link_lower = orient(link_lower, plan["lower"][2], plan)
    link_upper = orient(link_upper, plan["upper"][2], plan)
    lower_rim = jnp.where(at_lower, link_lower, from_lower)
    upper_rim = jnp.where(at_upper, link_upper, from_upper)
    return (lower_rim, upper_rim)


def backward_sends(grad_lower, grad_upper, plan):
    at_lower = plan["device_pos"] == 0
    at_upper = plan["device_pos"] == plan["grid_side"] - 1
    near_lower = jnp.where(at_lower, 0.0, grad_lower)
    near_upper = jnp.where(at_upper, 0.0, grad_upper)
    face_count = grad_lower.shape[0]
    link_lower = orient_back(jnp.where(at_lower, grad_lower, 0.0), plan["lower"][2], plan)
    link_upper = orient_back(jnp.where(at_upper, grad_upper, 0.0), plan["upper"][2], plan)
    lower_stack, upper_stack = pick_back(link_lower, link_upper, plan)
    low = [lower_stack[k * face_count : (k + 1) * face_count] for k in range(4)]
    up = [upper_stack[k * face_count : (k + 1) * face_count] for k in range(4)]
    sends = {
        "down": near_lower + low[0],
        "up": near_upper + up[0],
        "row": jnp.concatenate([low[3], up[3]], axis=0),
        "both": jnp.concatenate([up[2], low[2]], axis=0),
    }
    return (sends, (low[1], up[1]))


def backward_finish(got, kept):
    row_lower, row_upper = jnp.split(got["row"], 2, axis=0)
    both_lower, both_upper = jnp.split(got["both"], 2, axis=0)
    grad_lower_edge = kept[0] + got["up"] + row_lower + both_lower
    grad_upper_edge = kept[1] + got["down"] + row_upper + both_upper
    return (grad_lower_edge, grad_upper_edge)


def add_ends(values, lower, upper, axis):
    first = lax.slice_in_dim(values, 0, 1, axis=axis)
    middle = lax.slice_in_dim(values, 1, values.shape[axis] - 1, axis=axis)
    last = lax.slice_in_dim(values, values.shape[axis] - 1, values.shape[axis], axis=axis)
    return jnp.concatenate(
        [first + jnp.expand_dims(lower, axis), middle, last + jnp.expand_dims(upper, axis)], axis=axis
    )


def pad_pair(tiles, grad, rim_plans):
    column_plan, row_plan = rim_plans
    back_plans = (dict(column_plan, ends=True), dict(row_plan, ends=False))
    padded, grad_tiles = (None, None)
    for stage in range(2):
        plan = rim_plans[stage]
        sends_list = []
        if tiles is not None:
            edges = (tiles[:, :, 0], tiles[:, :, -1]) if stage == 0 else (tiles[:, 0], tiles[:, -1])
            sends_list.append(forward_sends(*edges))
        if grad is not None:
            grad_edges = (grad[:, :, 0], grad[:, :, -1]) if stage == 0 else (grad[:, 0], grad[:, -1])
            grad_sends, kept = backward_sends(*grad_edges, back_plans[stage])
            sends_list.append(grad_sends)
        received = exchange(sends_list, plan)
        if tiles is not None:
            lower_rim, upper_rim = forward_finish(received[0], *edges, plan)
            tiles = jnp.concatenate(
                [jnp.expand_dims(lower_rim, 2 - stage), tiles, jnp.expand_dims(upper_rim, 2 - stage)],
                axis=2 - stage,
            )
        if grad is not None:
            lower_grad, upper_grad = backward_finish(received[-1], kept)
            inner = grad[:, :, 1:-1] if stage == 0 else grad[:, 1:-1]
            grad = add_ends(inner, lower_grad, upper_grad, 2 - stage)
    return (tiles, grad)


def forward_step(tiles, axis, plan):
    edges = (lax.index_in_dim(tiles, 0, axis, False), lax.index_in_dim(tiles, -1, axis, False))

    def finish(got):
        lower_rim, upper_rim = forward_finish(got, *edges, plan)
        return jnp.concatenate(
            [jnp.expand_dims(lower_rim, axis), tiles, jnp.expand_dims(upper_rim, axis)], axis=axis
        )

    return (forward_sends(*edges), finish)


def backward_step(grad, axis, plan):
    edges = (lax.index_in_dim(grad, 0, axis, False), lax.index_in_dim(grad, -1, axis, False))
    sends, kept = backward_sends(*edges, plan)

    def finish(got):
        lower_grad, upper_grad = backward_finish(got, kept)
        inner = lax.slice_in_dim(grad, 1, grad.shape[axis] - 1, axis=axis)
        return add_ends(inner, lower_grad, upper_grad, axis)

    return (sends, finish)


def run_round(steps, plan):
    received = exchange([sends for sends, _ in steps], plan)
    return [finish(got) for (_, finish), got in zip(steps, received)]


def convolve(padded, weight):
    channels = weight.shape[-1]
    kernel = weight.reshape(3, 3, weight.shape[1], channels)
    return lax.conv_general_dilated(
        padded,
        kernel,
        (1, 1),
        "VALID",
        dimension_numbers=("NHWC", "HWIO", "NHWC"),
        preferred_element_type=jnp.float32,
    )


def convolve_back(grad, weight):
    kernel = weight.reshape(3, 3, weight.shape[1], weight.shape[2])[::-1, ::-1]
    return lax.conv_general_dilated(
        grad,
        kernel,
        (1, 1),
        ((2, 2), (2, 2)),
        dimension_numbers=("NHWC", "HWOI", "NHWC"),
        preferred_element_type=jnp.float32,
    )


def weight_grad(padded, grad):
    summed = lax.conv_general_dilated(
        padded,
        grad,
        (1, 1),
        "VALID",
        dimension_numbers=("CHWN", "IHWO", "HWNC"),
        preferred_element_type=jnp.float32,
    )
    return summed.reshape((9,) + summed.shape[2:])


def local(fields, weight_one, weight_two, cotangent, face_links, face_order):
    local_tiles = fields[0]
    face_count = local_tiles.shape[0]
    extent = local_tiles.shape[1]
    devices = lax.axis_size("tile")
    grid_side = math.isqrt(devices * face_count // 12)
    halves = devices // (grid_side * grid_side)
    levels = grid_side.bit_length() - 1
    device = lax.axis_index("tile")
    my_half = device // (grid_side * grid_side)
    grid_row = device // grid_side % grid_side
    grid_col = device % grid_side
    column_plan = make_plan(
        face_order,
        face_links,
        my_half,
        halves,
        face_count,
        grid_side,
        1,
        list(range(levels, 2 * levels)),
        (2, 3),
        grid_col,
        grid_row,
        False,
        2 * levels,
    )
    row_plan = make_plan(
        face_order,
        face_links,
        my_half,
        halves,
        face_count,
        grid_side,
        grid_side,
        list(range(levels)),
        (0, 1),
        grid_row,
        grid_col,
        True,
        2 * levels,
    )
    rim_plans = (column_plan, row_plan)
    grad_out = cotangent[0]
    rim_two = convolve_back(grad_out, weight_two).astype(jnp.bfloat16)
    rim_two = lax.optimization_barrier(rim_two).astype(jnp.float32)
    (widened_in,) = run_round([forward_step(local_tiles, 2, column_plan)], column_plan)
    padded_in, rows_back = run_round(
        [forward_step(widened_in, 1, row_plan), backward_step(rim_two, 1, row_plan)], row_plan
    )
    pre_act = convolve(padded_in, weight_one)
    hidden = jax.nn.gelu(pre_act, approximate=True).astype(jnp.bfloat16)
    grad_hidden, widened_hidden = run_round(
        [backward_step(rows_back, 2, column_plan), forward_step(hidden, 2, column_plan)], column_plan
    )
    (padded_hidden,) = run_round([forward_step(widened_hidden, 1, row_plan)], row_plan)
    second = convolve(padded_hidden, weight_two)
    block_output = (local_tiles.astype(jnp.float32) + second).astype(jnp.bfloat16)
    grad_scale = 1.0 / math.sqrt(lax.axis_size("dp") * 12 * (grid_side * extent) ** 2)
    local_two = weight_grad(padded_hidden, grad_out) * grad_scale
    gelu_pair = jax.vjp(partial(jax.nn.gelu, approximate=True), pre_act)
    grad_pre = gelu_pair[1](grad_hidden)[0].astype(jnp.bfloat16)
    local_one = weight_grad(padded_in, grad_pre) * grad_scale
    rim_one = convolve_back(grad_pre, weight_one).astype(jnp.bfloat16)
    rim_one, local_one, local_two = lax.optimization_barrier((rim_one, local_one, local_two))
    rim_one = rim_one.astype(jnp.float32)
    field_grad = (grad_out.astype(jnp.float32) + pad_pair(None, rim_one, rim_plans)[1]).astype(jnp.bfloat16)
    grad_one, grad_two = lax.psum((local_one, local_two), ("tile", "dp"))
    return (block_output[None], field_grad[None], grad_one, grad_two)


def solution(mesh):
    in_specs = (
        P("dp", "tile", None, None, None),
        P(),
        P(),
        P("dp", "tile", None, None, None),
        P(),
        P(),
    )
    out_specs = (P("dp", "tile", None, None, None), P("dp", "tile", None, None, None), P(), P())
    return jax.shard_map(local, mesh=mesh, in_specs=in_specs, out_specs=out_specs, check_vma=False)
```

```python
from functools import partial
import itertools
import math

import jax
import jax.numpy as jnp
from jax import lax
from jax.sharding import PartitionSpec as P


def shortened(shard):
    return jax.tree.map(lambda a: a.astype(jnp.bfloat16) if a.dtype == jnp.float32 else a, shard)


def from_behind(value, axis, steps):
    count = lax.axis_size(axis)
    first, last = (max(0, -steps), min(count, count - steps))
    return lax.ppermute(value, axis, [(source, source + steps) for source in range(first, last)])


def swapped(shard, axis, apart):
    return lax.ppermute(shard, axis, [(i, i ^ 1 << apart) for i in range(lax.axis_size(axis))])


def send_rim(values, offset):
    return jax.tree.map(
        lambda part, own: part.astype(own.dtype),
        from_behind(shortened(values), "tile", offset),
        values,
    )


def swap_rim(values, bit_index):
    return jax.tree.map(
        lambda part, own: part.astype(own.dtype),
        swapped(shortened(values), "tile", bit_index),
        values,
    )


def send_back(values, offset):
    return jax.tree.map(
        lambda part, own: part.astype(own.dtype),
        from_behind(shortened(values), "tile", offset),
        values,
    )


def swap_back(values, bit_index):
    return jax.tree.map(
        lambda part, own: part.astype(own.dtype),
        swapped(shortened(values), "tile", bit_index),
        values,
    )


def link_table(face_order, face_links, my_half, face_count, which_side):
    lookup = jnp.arange(face_order.shape[0], dtype=jnp.int32)
    inverse = jnp.sum(
        lookup[None, :] * (face_order[None, :] == lookup[:, None]).astype(jnp.int32), axis=1
    ).astype(jnp.int32)
    face_ids = lax.dynamic_slice_in_dim(face_order, my_half * face_count, face_count)
    link_rows = jnp.take(face_links, face_ids, axis=0)[:, which_side]
    source = jnp.take(inverse, link_rows[:, 0])
    remote = source // face_count != my_half
    candidate = link_rows[:, 1]
    pick_index = ((link_rows[:, 2] * 2 + candidate) * face_count + source % face_count).astype(
        jnp.int32
    )
    return (pick_index, remote, link_rows[:, 2] == 1)


def make_plan(
    face_order,
    face_links,
    my_half,
    halves,
    face_count,
    grid_side,
    step_size,
    mirror_bits,
    side_pair,
    device_pos,
    along_pos,
    mask_ends,
    half_bit,
):
    plan = {
        "step": step_size,
        "far": (grid_side - 1) * step_size,
        "bits": mirror_bits,
        "half_bit": half_bit,
        "halves": halves,
        "device_pos": device_pos,
        "along_pos": along_pos,
        "grid_side": grid_side,
        "ends": mask_ends,
    }
    for label_name, which_side in (("lower", side_pair[0]), ("upper", side_pair[1])):
        plan[label_name] = link_table(face_order, face_links, my_half, face_count, which_side)
        if halves == 2:
            plan[label_name + "_partner"] = link_table(
                face_order, face_links, 1 - my_half, face_count, which_side
            )
    return plan


def end_mask(plan, length):
    positions = jnp.arange(length)
    along_pos = plan["along_pos"]
    cut_cells = (positions == 0) & (along_pos == 0) | (positions == length - 1) & (
        along_pos == plan["grid_side"] - 1
    )
    return jnp.logical_not(cut_cells)[None, :, None]


def orient(rim_strip, reverse, plan):
    turned = jnp.where(reverse[:, None, None], rim_strip[:, ::-1], rim_strip)
    if plan["ends"]:
        turned = jnp.where(end_mask(plan, rim_strip.shape[1]), turned, jnp.zeros_like(turned))
    return turned


def orient_back(rim_strip, reverse, plan):
    masked = rim_strip
    if plan["ends"]:
        masked = jnp.where(end_mask(plan, rim_strip.shape[1]), masked, jnp.zeros_like(masked))
    return jnp.where(reverse[:, None, None], masked[:, ::-1], masked)


def select_rows(stack, index):
    onehot = (index[:, None] == jnp.arange(stack.shape[0])[None, :]).astype(stack.dtype)
    chosen = jnp.einsum("fk,k...->f...", onehot, stack, preferred_element_type=jnp.float32)
    return chosen.astype(stack.dtype)


def spread_rows(values, index, rows):
    if values.dtype == jnp.bfloat16:
        onehot = (jnp.arange(rows)[:, None] == index[None, :]).astype(jnp.bfloat16)
        return jnp.einsum("kf,f...->k...", onehot, values, preferred_element_type=jnp.float32)
    onehot = (index[:, None] == jnp.arange(rows)[None, :]).astype(jnp.float32)
    return jnp.einsum(
        "fk,f...->k...",
        onehot,
        values,
        precision=lax.Precision.HIGHEST,
        preferred_element_type=jnp.float32,
    )


def pick_links(lower_stack, upper_stack, plan):
    index_lower, remote_lower = (plan["lower"][0], plan["lower"][1])
    index_upper, remote_upper = (plan["upper"][0], plan["upper"][1])
    own_lower = select_rows(lower_stack, index_lower)
    own_upper = select_rows(upper_stack, index_upper)
    if plan["halves"] == 1:
        return (own_lower, own_upper)
    partner_lower, partner_upper = jnp.split(
        swap_rim(jnp.concatenate([lower_stack, upper_stack], axis=0), plan["half_bit"]), 2, axis=0
    )
    got_lower = select_rows(partner_lower, index_lower)
    got_upper = select_rows(partner_upper, index_upper)
    return (
        jnp.where(remote_lower[:, None, None], got_lower, own_lower),
        jnp.where(remote_upper[:, None, None], got_upper, own_upper),
    )


def pick_back(grad_lower, grad_upper, plan):
    index_lower, remote_lower = (plan["lower"][0], plan["lower"][1])
    index_upper, remote_upper = (plan["upper"][0], plan["upper"][1])
    rows = 4 * grad_lower.shape[0]
    if plan["halves"] == 1:
        return (spread_rows(grad_lower, index_lower, rows), spread_rows(grad_upper, index_upper, rows))
    stay_lower = jnp.where(remote_lower[:, None, None], 0.0, grad_lower)
    away_lower = jnp.where(remote_lower[:, None, None], grad_lower, 0.0)
    stay_upper = jnp.where(remote_upper[:, None, None], 0.0, grad_upper)
    away_upper = jnp.where(remote_upper[:, None, None], grad_upper, 0.0)
    away = jnp.concatenate(
        [spread_rows(away_lower, index_lower, rows), spread_rows(away_upper, index_upper, rows)], axis=0
    )
    back_lower, back_upper = jnp.split(swap_back(away, plan["half_bit"]), 2, axis=0)
    return (
        spread_rows(stay_lower, index_lower, rows) + back_lower,
        spread_rows(stay_upper, index_upper, rows) + back_upper,
    )


def cycled(value, plan, shift):
    count = lax.axis_size("tile")
    step_size, grid_side = (plan["step"], plan["grid_side"])
    pairs = []
    for source in range(count):
        position = source // step_size % grid_side
        moved = (position + shift) % grid_side
        pairs.append((source, source + (moved - position) * step_size))
    return lax.ppermute(value, "tile", pairs)


def mirror_masks(plan):
    mirror = sum(1 << bit_index for bit_index in plan["bits"])
    along = (plan["grid_side"] - 1) * plan["step"]
    return (mirror, mirror ^ along)


def xor_send(values, mask):
    count = lax.axis_size("tile")
    pairs = [(source, source ^ mask) for source in range(count)]
    joined = jnp.concatenate(values, axis=0)
    moved = lax.ppermute(shortened(joined), "tile", pairs).astype(joined.dtype)
    return jnp.split(moved, len(values), axis=0)


def shift_send(value, plan, shift):
    return cycled(shortened(value), plan, shift).astype(value.dtype)


def exchange(sends_list, plan):
    row_mask, both_mask = mirror_masks(plan)
    count = lax.axis_size("tile")
    received = [dict() for _ in sends_list]
    for key in ("up", "down", "row", "both"):
        pieces = [sends[key] for sends in sends_list]
        cuts = list(itertools.accumulate(piece.shape[1] for piece in pieces))[:-1]
        joined = jnp.concatenate([shortened(piece) for piece in pieces], axis=1)
        if key == "up":
            moved = cycled(joined, plan, 1)
        elif key == "down":
            moved = cycled(joined, plan, -1)
        else:
            mask = row_mask if key == "row" else both_mask
            moved = lax.ppermute(joined, "tile", [(source, source ^ mask) for source in range(count)])
        for got, piece, part in zip(received, pieces, jnp.split(moved, cuts, axis=1)):
            got[key] = part.astype(piece.dtype)
    return received


def forward_sends(lower_edge, upper_edge):
    both_edges = jnp.concatenate([lower_edge, upper_edge], axis=0)
    return {"up": upper_edge, "down": lower_edge, "row": both_edges, "both": both_edges}


def forward_finish(got, lower_edge, upper_edge, plan):
    from_lower, from_upper = (got["up"], got["down"])
    row_lower, row_upper = jnp.split(got["row"], 2, axis=0)
    both_lower, both_upper = jnp.split(got["both"], 2, axis=0)
    at_lower = plan["device_pos"] == 0
    at_upper = plan["device_pos"] == plan["grid_side"] - 1
    lower_stack = jnp.concatenate([from_lower, lower_edge, both_upper, row_lower], axis=0)
    upper_stack = jnp.concatenate([from_upper, upper_edge, both_lower, row_upper], axis=0)
    link_lower, link_upper = pick_links(lower_stack, upper_stack, plan)
    link_lower = orient(link_lower, plan["lower"][2], plan)
    link_upper = orient(link_upper, plan["upper"][2], plan)
    lower_rim = jnp.where(at_lower, link_lower, from_lower)
    upper_rim = jnp.where(at_upper, link_upper, from_upper)
    return (lower_rim, upper_rim)


def backward_sends(grad_lower, grad_upper, plan):
    at_lower = plan["device_pos"] == 0
    at_upper = plan["device_pos"] == plan["grid_side"] - 1
    near_lower = jnp.where(at_lower, 0.0, grad_lower)
    near_upper = jnp.where(at_upper, 0.0, grad_upper)
    face_count = grad_lower.shape[0]
    link_lower = orient_back(jnp.where(at_lower, grad_lower, 0.0), plan["lower"][2], plan)
    link_upper = orient_back(jnp.where(at_upper, grad_upper, 0.0), plan["upper"][2], plan)
    lower_stack, upper_stack = pick_back(link_lower, link_upper, plan)
    low = [lower_stack[k * face_count : (k + 1) * face_count] for k in range(4)]
    up = [upper_stack[k * face_count : (k + 1) * face_count] for k in range(4)]
    sends = {
        "down": near_lower + low[0],
        "up": near_upper + up[0],
        "row": jnp.concatenate([low[3], up[3]], axis=0),
        "both": jnp.concatenate([up[2], low[2]], axis=0),
    }
    return (sends, (low[1], up[1]))


def backward_finish(got, kept):
    row_lower, row_upper = jnp.split(got["row"], 2, axis=0)
    both_lower, both_upper = jnp.split(got["both"], 2, axis=0)
    grad_lower_edge = kept[0] + got["up"] + row_lower + both_lower
    grad_upper_edge = kept[1] + got["down"] + row_upper + both_upper
    return (grad_lower_edge, grad_upper_edge)


def add_ends(values, lower, upper, axis):
    first = lax.slice_in_dim(values, 0, 1, axis=axis)
    middle = lax.slice_in_dim(values, 1, values.shape[axis] - 1, axis=axis)
    last = lax.slice_in_dim(values, values.shape[axis] - 1, values.shape[axis], axis=axis)
    return jnp.concatenate(
        [first + jnp.expand_dims(lower, axis), middle, last + jnp.expand_dims(upper, axis)], axis=axis
    )


def pad_pair(tiles, grad, rim_plans):
    column_plan, row_plan = rim_plans
    back_plans = (dict(column_plan, ends=True), dict(row_plan, ends=False))
    padded, grad_tiles = (None, None)
    for stage in range(2):
        plan = rim_plans[stage]
        sends_list = []
        if tiles is not None:
            edges = (tiles[:, :, 0], tiles[:, :, -1]) if stage == 0 else (tiles[:, 0], tiles[:, -1])
            sends_list.append(forward_sends(*edges))
        if grad is not None:
            grad_edges = (grad[:, :, 0], grad[:, :, -1]) if stage == 0 else (grad[:, 0], grad[:, -1])
            grad_sends, kept = backward_sends(*grad_edges, back_plans[stage])
            sends_list.append(grad_sends)
        received = exchange(sends_list, plan)
        if tiles is not None:
            lower_rim, upper_rim = forward_finish(received[0], *edges, plan)
            tiles = jnp.concatenate(
                [jnp.expand_dims(lower_rim, 2 - stage), tiles, jnp.expand_dims(upper_rim, 2 - stage)],
                axis=2 - stage,
            )
        if grad is not None:
            lower_grad, upper_grad = backward_finish(received[-1], kept)
            inner = grad[:, :, 1:-1] if stage == 0 else grad[:, 1:-1]
            grad = add_ends(inner, lower_grad, upper_grad, 2 - stage)
    return (tiles, grad)


def convolve(padded, weight):
    channels = weight.shape[-1]
    kernel = weight.reshape(3, 3, weight.shape[1], channels)
    return lax.conv_general_dilated(
        padded,
        kernel,
        (1, 1),
        "VALID",
        dimension_numbers=("NHWC", "HWIO", "NHWC"),
        preferred_element_type=jnp.float32,
    )


def convolve_back(grad, weight):
    kernel = weight.reshape(3, 3, weight.shape[1], weight.shape[2])[::-1, ::-1]
    return lax.conv_general_dilated(
        grad,
        kernel,
        (1, 1),
        ((2, 2), (2, 2)),
        dimension_numbers=("NHWC", "HWOI", "NHWC"),
        preferred_element_type=jnp.float32,
    )


def weight_grad(padded, grad):
    summed = lax.conv_general_dilated(
        padded,
        grad,
        (1, 1),
        "VALID",
        dimension_numbers=("CHWN", "IHWO", "HWNC"),
        preferred_element_type=jnp.float32,
    )
    return summed.reshape((9,) + summed.shape[2:])


def local(fields, weight_one, weight_two, cotangent, face_links, face_order):
    local_tiles = fields[0]
    face_count = local_tiles.shape[0]
    extent = local_tiles.shape[1]
    devices = lax.axis_size("tile")
    grid_side = math.isqrt(devices * face_count // 12)
    halves = devices // (grid_side * grid_side)
    levels = grid_side.bit_length() - 1
    device = lax.axis_index("tile")
    my_half = device // (grid_side * grid_side)
    grid_row = device // grid_side % grid_side
    grid_col = device % grid_side
    column_plan = make_plan(
        face_order,
        face_links,
        my_half,
        halves,
        face_count,
        grid_side,
        1,
        list(range(levels, 2 * levels)),
        (2, 3),
        grid_col,
        grid_row,
        False,
        2 * levels,
    )
    row_plan = make_plan(
        face_order,
        face_links,
        my_half,
        halves,
        face_count,
        grid_side,
        grid_side,
        list(range(levels)),
        (0, 1),
        grid_row,
        grid_col,
        True,
        2 * levels,
    )
    rim_plans = (column_plan, row_plan)
    grad_out = cotangent[0]
    rim_two = convolve_back(grad_out, weight_two).astype(jnp.bfloat16)
    rim_two = lax.optimization_barrier(rim_two)
    padded_in, grad_hidden = pad_pair(local_tiles, rim_two, rim_plans)
    pre_act = convolve(padded_in, weight_one)
    hidden = jax.nn.gelu(pre_act, approximate=True).astype(jnp.bfloat16)
    padded_hidden = pad_pair(hidden, None, rim_plans)[0]
    second = convolve(padded_hidden, weight_two)
    block_output = (local_tiles.astype(jnp.float32) + second).astype(jnp.bfloat16)
    grad_scale = 1.0 / math.sqrt(lax.axis_size("dp") * 12 * (grid_side * extent) ** 2)
    local_two = weight_grad(padded_hidden, grad_out) * grad_scale
    gelu_pair = jax.vjp(partial(jax.nn.gelu, approximate=True), pre_act)
    grad_pre = gelu_pair[1](grad_hidden)[0].astype(jnp.bfloat16)
    local_one = weight_grad(padded_in, grad_pre) * grad_scale
    rim_one = convolve_back(grad_pre, weight_one).astype(jnp.bfloat16)
    rim_one, local_one, local_two = lax.optimization_barrier((rim_one, local_one, local_two))
    field_grad = (grad_out.astype(jnp.float32) + pad_pair(None, rim_one, rim_plans)[1]).astype(jnp.bfloat16)
    grad_one, grad_two = lax.psum((local_one, local_two), ("tile", "dp"))
    return (block_output[None], field_grad[None], grad_one, grad_two)


def solution(mesh):
    in_specs = (
        P("dp", "tile", None, None, None),
        P(),
        P(),
        P("dp", "tile", None, None, None),
        P(),
        P(),
    )
    out_specs = (P("dp", "tile", None, None, None), P("dp", "tile", None, None, None), P(), P())
    return jax.shard_map(local, mesh=mesh, in_specs=in_specs, out_specs=out_specs, check_vma=False)
```

```python
from functools import partial
import itertools
import math

import jax
import jax.numpy as jnp
from jax import lax
from jax.sharding import PartitionSpec as P


def shortened(shard):
    return jax.tree.map(lambda a: a.astype(jnp.bfloat16) if a.dtype == jnp.float32 else a, shard)


def from_behind(value, axis, steps):
    count = lax.axis_size(axis)
    first, last = (max(0, -steps), min(count, count - steps))
    return lax.ppermute(value, axis, [(source, source + steps) for source in range(first, last)])


def swapped(shard, axis, apart):
    return lax.ppermute(shard, axis, [(i, i ^ 1 << apart) for i in range(lax.axis_size(axis))])


def send_rim(values, offset):
    return jax.tree.map(
        lambda part, own: part.astype(own.dtype),
        from_behind(shortened(values), "tile", offset),
        values,
    )


def swap_rim(values, bit_index):
    return jax.tree.map(
        lambda part, own: part.astype(own.dtype),
        swapped(shortened(values), "tile", bit_index),
        values,
    )


def send_back(values, offset):
    return jax.tree.map(
        lambda part, own: part.astype(own.dtype),
        from_behind(shortened(values), "tile", offset),
        values,
    )


def swap_back(values, bit_index):
    return jax.tree.map(
        lambda part, own: part.astype(own.dtype),
        swapped(shortened(values), "tile", bit_index),
        values,
    )


def link_table(face_order, face_links, my_half, face_count, which_side):
    lookup = jnp.arange(face_order.shape[0], dtype=jnp.int32)
    inverse = jnp.sum(
        lookup[None, :] * (face_order[None, :] == lookup[:, None]).astype(jnp.int32), axis=1
    ).astype(jnp.int32)
    face_ids = lax.dynamic_slice_in_dim(face_order, my_half * face_count, face_count)
    link_rows = jnp.take(face_links, face_ids, axis=0)[:, which_side]
    source = jnp.take(inverse, link_rows[:, 0])
    remote = source // face_count != my_half
    candidate = link_rows[:, 1]
    pick_index = ((link_rows[:, 2] * 2 + candidate) * face_count + source % face_count).astype(
        jnp.int32
    )
    return (pick_index, remote, link_rows[:, 2] == 1)


def make_plan(
    face_order,
    face_links,
    my_half,
    halves,
    face_count,
    grid_side,
    step_size,
    mirror_bits,
    side_pair,
    device_pos,
    along_pos,
    mask_ends,
    half_bit,
):
    plan = {
        "step": step_size,
        "far": (grid_side - 1) * step_size,
        "bits": mirror_bits,
        "half_bit": half_bit,
        "halves": halves,
        "device_pos": device_pos,
        "along_pos": along_pos,
        "grid_side": grid_side,
        "ends": mask_ends,
    }
    for label_name, which_side in (("lower", side_pair[0]), ("upper", side_pair[1])):
        plan[label_name] = link_table(face_order, face_links, my_half, face_count, which_side)
        if halves == 2:
            plan[label_name + "_partner"] = link_table(
                face_order, face_links, 1 - my_half, face_count, which_side
            )
    return plan


def end_mask(plan, length):
    positions = jnp.arange(length)
    along_pos = plan["along_pos"]
    cut_cells = (positions == 0) & (along_pos == 0) | (positions == length - 1) & (
        along_pos == plan["grid_side"] - 1
    )
    return jnp.logical_not(cut_cells)[None, :, None]


def orient(rim_strip, reverse, plan):
    turned = jnp.where(reverse[:, None, None], rim_strip[:, ::-1], rim_strip)
    if plan["ends"]:
        turned = jnp.where(end_mask(plan, rim_strip.shape[1]), turned, jnp.zeros_like(turned))
    return turned


def orient_back(rim_strip, reverse, plan):
    masked = rim_strip
    if plan["ends"]:
        masked = jnp.where(end_mask(plan, rim_strip.shape[1]), masked, jnp.zeros_like(masked))
    return jnp.where(reverse[:, None, None], masked[:, ::-1], masked)


def select_rows(stack, index):
    onehot = (index[:, None] == jnp.arange(stack.shape[0])[None, :]).astype(stack.dtype)
    chosen = jnp.einsum("fk,k...->f...", onehot, stack, preferred_element_type=jnp.float32)
    return chosen.astype(stack.dtype)


def spread_rows(values, index, rows):
    onehot = (jnp.arange(rows)[:, None] == index[None, :]).astype(jnp.bfloat16)
    if values.dtype == jnp.bfloat16:
        return jnp.einsum("kf,f...->k...", onehot, values, preferred_element_type=jnp.float32)
    pieces = []
    rest = values
    for _ in range(3):
        piece = rest.astype(jnp.bfloat16)
        pieces.append(piece)
        rest = rest - piece.astype(jnp.float32)
    spread = [
        jnp.einsum("kf,f...->k...", onehot, piece, preferred_element_type=jnp.float32) for piece in pieces
    ]
    return (spread[0] + spread[1]) + spread[2]


def pick_links(lower_stack, upper_stack, plan):
    index_lower, remote_lower = (plan["lower"][0], plan["lower"][1])
    index_upper, remote_upper = (plan["upper"][0], plan["upper"][1])
    own_lower = select_rows(lower_stack, index_lower)
    own_upper = select_rows(upper_stack, index_upper)
    if plan["halves"] == 1:
        return (own_lower, own_upper)
    partner_lower, partner_upper = jnp.split(
        swap_rim(jnp.concatenate([lower_stack, upper_stack], axis=0), plan["half_bit"]), 2, axis=0
    )
    got_lower = select_rows(partner_lower, index_lower)
    got_upper = select_rows(partner_upper, index_upper)
    return (
        jnp.where(remote_lower[:, None, None], got_lower, own_lower),
        jnp.where(remote_upper[:, None, None], got_upper, own_upper),
    )


def pick_back(grad_lower, grad_upper, plan):
    index_lower, remote_lower = (plan["lower"][0], plan["lower"][1])
    index_upper, remote_upper = (plan["upper"][0], plan["upper"][1])
    rows = 4 * grad_lower.shape[0]
    if plan["halves"] == 1:
        return (spread_rows(grad_lower, index_lower, rows), spread_rows(grad_upper, index_upper, rows))
    stay_lower = jnp.where(remote_lower[:, None, None], 0.0, grad_lower)
    away_lower = jnp.where(remote_lower[:, None, None], grad_lower, 0.0)
    stay_upper = jnp.where(remote_upper[:, None, None], 0.0, grad_upper)
    away_upper = jnp.where(remote_upper[:, None, None], grad_upper, 0.0)
    away = jnp.concatenate(
        [spread_rows(away_lower, index_lower, rows), spread_rows(away_upper, index_upper, rows)], axis=0
    )
    back_lower, back_upper = jnp.split(swap_back(away, plan["half_bit"]), 2, axis=0)
    return (
        spread_rows(stay_lower, index_lower, rows) + back_lower,
        spread_rows(stay_upper, index_upper, rows) + back_upper,
    )


def cycled(value, plan, shift):
    count = lax.axis_size("tile")
    step_size, grid_side = (plan["step"], plan["grid_side"])
    pairs = []
    for source in range(count):
        position = source // step_size % grid_side
        moved = (position + shift) % grid_side
        pairs.append((source, source + (moved - position) * step_size))
    return lax.ppermute(value, "tile", pairs)


def mirror_masks(plan):
    mirror = sum(1 << bit_index for bit_index in plan["bits"])
    along = (plan["grid_side"] - 1) * plan["step"]
    return (mirror, mirror ^ along)


def xor_send(values, mask):
    count = lax.axis_size("tile")
    pairs = [(source, source ^ mask) for source in range(count)]
    joined = jnp.concatenate(values, axis=0)
    moved = lax.ppermute(shortened(joined), "tile", pairs).astype(joined.dtype)
    return jnp.split(moved, len(values), axis=0)


def shift_send(value, plan, shift):
    return cycled(shortened(value), plan, shift).astype(value.dtype)


def exchange(sends_list, plan):
    row_mask, both_mask = mirror_masks(plan)
    count = lax.axis_size("tile")
    received = [dict() for _ in sends_list]
    for key in ("up", "down", "row", "both"):
        pieces = [sends[key] for sends in sends_list]
        cuts = list(itertools.accumulate(piece.shape[1] for piece in pieces))[:-1]
        joined = jnp.concatenate([shortened(piece) for piece in pieces], axis=1)
        if key == "up":
            moved = cycled(joined, plan, 1)
        elif key == "down":
            moved = cycled(joined, plan, -1)
        else:
            mask = row_mask if key == "row" else both_mask
            moved = lax.ppermute(joined, "tile", [(source, source ^ mask) for source in range(count)])
        for got, piece, part in zip(received, pieces, jnp.split(moved, cuts, axis=1)):
            got[key] = part.astype(piece.dtype)
    return received


def forward_sends(lower_edge, upper_edge):
    both_edges = jnp.concatenate([lower_edge, upper_edge], axis=0)
    return {"up": upper_edge, "down": lower_edge, "row": both_edges, "both": both_edges}


def forward_finish(got, lower_edge, upper_edge, plan):
    from_lower, from_upper = (got["up"], got["down"])
    row_lower, row_upper = jnp.split(got["row"], 2, axis=0)
    both_lower, both_upper = jnp.split(got["both"], 2, axis=0)
    at_lower = plan["device_pos"] == 0
    at_upper = plan["device_pos"] == plan["grid_side"] - 1
    lower_stack = jnp.concatenate([from_lower, lower_edge, both_upper, row_lower], axis=0)
    upper_stack = jnp.concatenate([from_upper, upper_edge, both_lower, row_upper], axis=0)
    link_lower, link_upper = pick_links(lower_stack, upper_stack, plan)
    link_lower = orient(link_lower, plan["lower"][2], plan)
    link_upper = orient(link_upper, plan["upper"][2], plan)
    lower_rim = jnp.where(at_lower, link_lower, from_lower)
    upper_rim = jnp.where(at_upper, link_upper, from_upper)
    return (lower_rim, upper_rim)


def backward_sends(grad_lower, grad_upper, plan):
    at_lower = plan["device_pos"] == 0
    at_upper = plan["device_pos"] == plan["grid_side"] - 1
    near_lower = jnp.where(at_lower, 0.0, grad_lower)
    near_upper = jnp.where(at_upper, 0.0, grad_upper)
    face_count = grad_lower.shape[0]
    link_lower = orient_back(jnp.where(at_lower, grad_lower, 0.0), plan["lower"][2], plan)
    link_upper = orient_back(jnp.where(at_upper, grad_upper, 0.0), plan["upper"][2], plan)
    lower_stack, upper_stack = pick_back(link_lower, link_upper, plan)
    low = [lower_stack[k * face_count : (k + 1) * face_count] for k in range(4)]
    up = [upper_stack[k * face_count : (k + 1) * face_count] for k in range(4)]
    sends = {
        "down": near_lower + low[0],
        "up": near_upper + up[0],
        "row": jnp.concatenate([low[3], up[3]], axis=0),
        "both": jnp.concatenate([up[2], low[2]], axis=0),
    }
    return (sends, (low[1], up[1]))


def backward_finish(got, kept):
    row_lower, row_upper = jnp.split(got["row"], 2, axis=0)
    both_lower, both_upper = jnp.split(got["both"], 2, axis=0)
    grad_lower_edge = kept[0] + got["up"] + row_lower + both_lower
    grad_upper_edge = kept[1] + got["down"] + row_upper + both_upper
    return (grad_lower_edge, grad_upper_edge)


def add_ends(values, lower, upper, axis):
    first = lax.slice_in_dim(values, 0, 1, axis=axis)
    middle = lax.slice_in_dim(values, 1, values.shape[axis] - 1, axis=axis)
    last = lax.slice_in_dim(values, values.shape[axis] - 1, values.shape[axis], axis=axis)
    return jnp.concatenate(
        [first + jnp.expand_dims(lower, axis), middle, last + jnp.expand_dims(upper, axis)], axis=axis
    )


def pad_pair(tiles, grad, rim_plans):
    column_plan, row_plan = rim_plans
    back_plans = (dict(column_plan, ends=True), dict(row_plan, ends=False))
    padded, grad_tiles = (None, None)
    for stage in range(2):
        plan = rim_plans[stage]
        sends_list = []
        if tiles is not None:
            edges = (tiles[:, :, 0], tiles[:, :, -1]) if stage == 0 else (tiles[:, 0], tiles[:, -1])
            sends_list.append(forward_sends(*edges))
        if grad is not None:
            grad_edges = (grad[:, :, 0], grad[:, :, -1]) if stage == 0 else (grad[:, 0], grad[:, -1])
            grad_sends, kept = backward_sends(*grad_edges, back_plans[stage])
            sends_list.append(grad_sends)
        received = exchange(sends_list, plan)
        if tiles is not None:
            lower_rim, upper_rim = forward_finish(received[0], *edges, plan)
            tiles = jnp.concatenate(
                [jnp.expand_dims(lower_rim, 2 - stage), tiles, jnp.expand_dims(upper_rim, 2 - stage)],
                axis=2 - stage,
            )
        if grad is not None:
            lower_grad, upper_grad = backward_finish(received[-1], kept)
            inner = grad[:, :, 1:-1] if stage == 0 else grad[:, 1:-1]
            grad = add_ends(inner, lower_grad, upper_grad, 2 - stage)
    return (tiles, grad)


def convolve(padded, weight):
    channels = weight.shape[-1]
    kernel = weight.reshape(3, 3, weight.shape[1], channels)
    return lax.conv_general_dilated(
        padded,
        kernel,
        (1, 1),
        "VALID",
        dimension_numbers=("NHWC", "HWIO", "NHWC"),
        preferred_element_type=jnp.float32,
    )


def convolve_back(grad, weight):
    kernel = weight.reshape(3, 3, weight.shape[1], weight.shape[2])[::-1, ::-1]
    return lax.conv_general_dilated(
        grad,
        kernel,
        (1, 1),
        ((2, 2), (2, 2)),
        dimension_numbers=("NHWC", "HWOI", "NHWC"),
        preferred_element_type=jnp.float32,
    )


def weight_grad(padded, grad):
    summed = lax.conv_general_dilated(
        padded,
        grad,
        (1, 1),
        "VALID",
        dimension_numbers=("CHWN", "IHWO", "HWNC"),
        preferred_element_type=jnp.float32,
    )
    return summed.reshape((9,) + summed.shape[2:])


def local(fields, weight_one, weight_two, cotangent, face_links, face_order):
    local_tiles = fields[0]
    face_count = local_tiles.shape[0]
    extent = local_tiles.shape[1]
    devices = lax.axis_size("tile")
    grid_side = math.isqrt(devices * face_count // 12)
    halves = devices // (grid_side * grid_side)
    levels = grid_side.bit_length() - 1
    device = lax.axis_index("tile")
    my_half = device // (grid_side * grid_side)
    grid_row = device // grid_side % grid_side
    grid_col = device % grid_side
    column_plan = make_plan(
        face_order,
        face_links,
        my_half,
        halves,
        face_count,
        grid_side,
        1,
        list(range(levels, 2 * levels)),
        (2, 3),
        grid_col,
        grid_row,
        False,
        2 * levels,
    )
    row_plan = make_plan(
        face_order,
        face_links,
        my_half,
        halves,
        face_count,
        grid_side,
        grid_side,
        list(range(levels)),
        (0, 1),
        grid_row,
        grid_col,
        True,
        2 * levels,
    )
    rim_plans = (column_plan, row_plan)
    grad_out = cotangent[0]
    rim_two = convolve_back(grad_out, weight_two).astype(jnp.bfloat16)
    rim_two = lax.optimization_barrier(rim_two)
    padded_in, grad_hidden = pad_pair(local_tiles, rim_two, rim_plans)
    pre_act = convolve(padded_in, weight_one)
    hidden = jax.nn.gelu(pre_act, approximate=True).astype(jnp.bfloat16)
    padded_hidden = pad_pair(hidden, None, rim_plans)[0]
    second = convolve(padded_hidden, weight_two)
    block_output = (local_tiles.astype(jnp.float32) + second).astype(jnp.bfloat16)
    grad_scale = 1.0 / math.sqrt(lax.axis_size("dp") * 12 * (grid_side * extent) ** 2)
    local_two = weight_grad(padded_hidden, grad_out) * grad_scale
    gelu_pair = jax.vjp(partial(jax.nn.gelu, approximate=True), pre_act)
    grad_pre = gelu_pair[1](grad_hidden)[0].astype(jnp.bfloat16)
    local_one = weight_grad(padded_in, grad_pre) * grad_scale
    rim_one = convolve_back(grad_pre, weight_one).astype(jnp.bfloat16)
    rim_one, local_one, local_two = lax.optimization_barrier((rim_one, local_one, local_two))
    field_grad = (grad_out.astype(jnp.float32) + pad_pair(None, rim_one, rim_plans)[1]).astype(jnp.bfloat16)
    grad_one, grad_two = lax.psum((local_one, local_two), ("tile", "dp"))
    return (block_output[None], field_grad[None], grad_one, grad_two)


def solution(mesh):
    in_specs = (
        P("dp", "tile", None, None, None),
        P(),
        P(),
        P("dp", "tile", None, None, None),
        P(),
        P(),
    )
    out_specs = (P("dp", "tile", None, None, None), P("dp", "tile", None, None, None), P(), P())
    return jax.shard_map(local, mesh=mesh, in_specs=in_specs, out_specs=out_specs, check_vma=False)
```

```python
from functools import partial
import itertools
import math

import jax
import jax.numpy as jnp
from jax import lax
from jax.sharding import PartitionSpec as P


def shortened(shard):
    return jax.tree.map(lambda a: a.astype(jnp.bfloat16) if a.dtype == jnp.float32 else a, shard)


def from_behind(value, axis, steps):
    count = lax.axis_size(axis)
    first, last = (max(0, -steps), min(count, count - steps))
    return lax.ppermute(value, axis, [(source, source + steps) for source in range(first, last)])


def swapped(shard, axis, apart):
    return lax.ppermute(shard, axis, [(i, i ^ 1 << apart) for i in range(lax.axis_size(axis))])


def send_rim(values, offset):
    return jax.tree.map(
        lambda part, own: part.astype(own.dtype),
        from_behind(shortened(values), "tile", offset),
        values,
    )


def swap_rim(values, bit_index):
    return jax.tree.map(
        lambda part, own: part.astype(own.dtype),
        swapped(shortened(values), "tile", bit_index),
        values,
    )


def send_back(values, offset):
    return jax.tree.map(
        lambda part, own: part.astype(own.dtype),
        from_behind(shortened(values), "tile", offset),
        values,
    )


def swap_back(values, bit_index):
    return jax.tree.map(
        lambda part, own: part.astype(own.dtype),
        swapped(shortened(values), "tile", bit_index),
        values,
    )


def link_table(face_order, face_links, my_half, face_count, which_side):
    lookup = jnp.arange(face_order.shape[0], dtype=jnp.int32)
    inverse = jnp.sum(
        lookup[None, :] * (face_order[None, :] == lookup[:, None]).astype(jnp.int32), axis=1
    ).astype(jnp.int32)
    face_ids = lax.dynamic_slice_in_dim(face_order, my_half * face_count, face_count)
    link_rows = jnp.take(face_links, face_ids, axis=0)[:, which_side]
    source = jnp.take(inverse, link_rows[:, 0])
    remote = source // face_count != my_half
    candidate = link_rows[:, 1]
    pick_index = ((link_rows[:, 2] * 2 + candidate) * face_count + source % face_count).astype(
        jnp.int32
    )
    return (pick_index, remote, link_rows[:, 2] == 1)


def make_plan(
    face_order,
    face_links,
    my_half,
    halves,
    face_count,
    grid_side,
    step_size,
    mirror_bits,
    side_pair,
    device_pos,
    along_pos,
    mask_ends,
    half_bit,
):
    plan = {
        "step": step_size,
        "far": (grid_side - 1) * step_size,
        "bits": mirror_bits,
        "half_bit": half_bit,
        "halves": halves,
        "device_pos": device_pos,
        "along_pos": along_pos,
        "grid_side": grid_side,
        "ends": mask_ends,
    }
    for label_name, which_side in (("lower", side_pair[0]), ("upper", side_pair[1])):
        plan[label_name] = link_table(face_order, face_links, my_half, face_count, which_side)
        if halves == 2:
            plan[label_name + "_partner"] = link_table(
                face_order, face_links, 1 - my_half, face_count, which_side
            )
    return plan


def end_mask(plan, length):
    positions = jnp.arange(length)
    along_pos = plan["along_pos"]
    cut_cells = (positions == 0) & (along_pos == 0) | (positions == length - 1) & (
        along_pos == plan["grid_side"] - 1
    )
    return jnp.logical_not(cut_cells)[None, :, None]


def orient(rim_strip, reverse, plan):
    turned = jnp.where(reverse[:, None, None], rim_strip[:, ::-1], rim_strip)
    if plan["ends"]:
        turned = jnp.where(end_mask(plan, rim_strip.shape[1]), turned, jnp.zeros_like(turned))
    return turned


def orient_back(rim_strip, reverse, plan):
    masked = rim_strip
    if plan["ends"]:
        masked = jnp.where(end_mask(plan, rim_strip.shape[1]), masked, jnp.zeros_like(masked))
    return jnp.where(reverse[:, None, None], masked[:, ::-1], masked)


def select_rows(stack, index):
    onehot = (index[:, None] == jnp.arange(stack.shape[0])[None, :]).astype(stack.dtype)
    chosen = jnp.einsum("fk,k...->f...", onehot, stack, preferred_element_type=jnp.float32)
    return chosen.astype(stack.dtype)


def spread_rows(values, index, rows):
    if values.dtype == jnp.bfloat16:
        onehot = (jnp.arange(rows)[:, None] == index[None, :]).astype(jnp.bfloat16)
        return jnp.einsum("kf,f...->k...", onehot, values, preferred_element_type=jnp.float32)
    onehot = (index[:, None] == jnp.arange(rows)[None, :]).astype(jnp.float32)
    return jnp.einsum(
        "fk,f...->k...",
        onehot,
        values,
        precision=lax.Precision.HIGHEST,
        preferred_element_type=jnp.float32,
    )


def pick_links(lower_stack, upper_stack, plan):
    index_lower, remote_lower = (plan["lower"][0], plan["lower"][1])
    index_upper, remote_upper = (plan["upper"][0], plan["upper"][1])
    own_lower = select_rows(lower_stack, index_lower)
    own_upper = select_rows(upper_stack, index_upper)
    if plan["halves"] == 1:
        return (own_lower, own_upper)
    partner_lower, partner_upper = jnp.split(
        swap_rim(jnp.concatenate([lower_stack, upper_stack], axis=0), plan["half_bit"]), 2, axis=0
    )
    got_lower = select_rows(partner_lower, index_lower)
    got_upper = select_rows(partner_upper, index_upper)
    return (
        jnp.where(remote_lower[:, None, None], got_lower, own_lower),
        jnp.where(remote_upper[:, None, None], got_upper, own_upper),
    )


def pick_back(grad_lower, grad_upper, plan):
    index_lower, remote_lower = (plan["lower"][0], plan["lower"][1])
    index_upper, remote_upper = (plan["upper"][0], plan["upper"][1])
    rows = 4 * grad_lower.shape[0]
    if plan["halves"] == 1:
        return (spread_rows(grad_lower, index_lower, rows), spread_rows(grad_upper, index_upper, rows))
    stay_lower = jnp.where(remote_lower[:, None, None], 0.0, grad_lower)
    away_lower = jnp.where(remote_lower[:, None, None], grad_lower, 0.0)
    stay_upper = jnp.where(remote_upper[:, None, None], 0.0, grad_upper)
    away_upper = jnp.where(remote_upper[:, None, None], grad_upper, 0.0)
    away = jnp.concatenate(
        [spread_rows(away_lower, index_lower, rows), spread_rows(away_upper, index_upper, rows)], axis=0
    )
    back_lower, back_upper = jnp.split(swap_back(away, plan["half_bit"]), 2, axis=0)
    return (
        spread_rows(stay_lower, index_lower, rows) + back_lower,
        spread_rows(stay_upper, index_upper, rows) + back_upper,
    )


def cycled(value, plan, shift):
    count = lax.axis_size("tile")
    step_size, grid_side = (plan["step"], plan["grid_side"])
    pairs = []
    for source in range(count):
        position = source // step_size % grid_side
        moved = (position + shift) % grid_side
        pairs.append((source, source + (moved - position) * step_size))
    return lax.ppermute(value, "tile", pairs)


def mirror_masks(plan):
    mirror = sum(1 << bit_index for bit_index in plan["bits"])
    along = (plan["grid_side"] - 1) * plan["step"]
    return (mirror, mirror ^ along)


def xor_send(values, mask):
    count = lax.axis_size("tile")
    pairs = [(source, source ^ mask) for source in range(count)]
    joined = jnp.concatenate(values, axis=0)
    moved = lax.ppermute(shortened(joined), "tile", pairs).astype(joined.dtype)
    return jnp.split(moved, len(values), axis=0)


def shift_send(value, plan, shift):
    return cycled(shortened(value), plan, shift).astype(value.dtype)


def exchange(sends_list, plan):
    row_mask, both_mask = mirror_masks(plan)
    count = lax.axis_size("tile")
    received = [dict() for _ in sends_list]
    for key in ("up", "down", "row", "both"):
        pieces = [sends[key] for sends in sends_list]
        cuts = list(itertools.accumulate(piece.shape[1] for piece in pieces))[:-1]
        joined = jnp.concatenate([shortened(piece) for piece in pieces], axis=1)
        if key == "up":
            moved = cycled(joined, plan, 1)
        elif key == "down":
            moved = cycled(joined, plan, -1)
        else:
            mask = row_mask if key == "row" else both_mask
            moved = lax.ppermute(joined, "tile", [(source, source ^ mask) for source in range(count)])
        for got, piece, part in zip(received, pieces, jnp.split(moved, cuts, axis=1)):
            got[key] = part.astype(piece.dtype)
    return received


def forward_sends(lower_edge, upper_edge):
    both_edges = jnp.concatenate([lower_edge, upper_edge], axis=0)
    return {"up": upper_edge, "down": lower_edge, "row": both_edges, "both": both_edges}


def forward_finish(got, lower_edge, upper_edge, plan):
    from_lower, from_upper = (got["up"], got["down"])
    row_lower, row_upper = jnp.split(got["row"], 2, axis=0)
    both_lower, both_upper = jnp.split(got["both"], 2, axis=0)
    at_lower = plan["device_pos"] == 0
    at_upper = plan["device_pos"] == plan["grid_side"] - 1
    lower_stack = jnp.concatenate([from_lower, lower_edge, both_upper, row_lower], axis=0)
    upper_stack = jnp.concatenate([from_upper, upper_edge, both_lower, row_upper], axis=0)
    link_lower, link_upper = pick_links(lower_stack, upper_stack, plan)
    link_lower = orient(link_lower, plan["lower"][2], plan)
    link_upper = orient(link_upper, plan["upper"][2], plan)
    lower_rim = jnp.where(at_lower, link_lower, from_lower)
    upper_rim = jnp.where(at_upper, link_upper, from_upper)
    return (lower_rim, upper_rim)


def backward_sends(grad_lower, grad_upper, plan):
    at_lower = plan["device_pos"] == 0
    at_upper = plan["device_pos"] == plan["grid_side"] - 1
    near_lower = jnp.where(at_lower, 0.0, grad_lower)
    near_upper = jnp.where(at_upper, 0.0, grad_upper)
    face_count = grad_lower.shape[0]
    link_lower = orient_back(jnp.where(at_lower, grad_lower, 0.0), plan["lower"][2], plan)
    link_upper = orient_back(jnp.where(at_upper, grad_upper, 0.0), plan["upper"][2], plan)
    lower_stack, upper_stack = pick_back(link_lower, link_upper, plan)
    low = [lower_stack[k * face_count : (k + 1) * face_count] for k in range(4)]
    up = [upper_stack[k * face_count : (k + 1) * face_count] for k in range(4)]
    sends = {
        "down": near_lower + low[0],
        "up": near_upper + up[0],
        "row": jnp.concatenate([low[3], up[3]], axis=0),
        "both": jnp.concatenate([up[2], low[2]], axis=0),
    }
    return (sends, (low[1], up[1]))


def backward_finish(got, kept):
    row_lower, row_upper = jnp.split(got["row"], 2, axis=0)
    both_lower, both_upper = jnp.split(got["both"], 2, axis=0)
    grad_lower_edge = kept[0] + got["up"] + row_lower + both_lower
    grad_upper_edge = kept[1] + got["down"] + row_upper + both_upper
    return (grad_lower_edge, grad_upper_edge)


def add_ends(values, lower, upper, axis):
    first = lax.slice_in_dim(values, 0, 1, axis=axis)
    middle = lax.slice_in_dim(values, 1, values.shape[axis] - 1, axis=axis)
    last = lax.slice_in_dim(values, values.shape[axis] - 1, values.shape[axis], axis=axis)
    return jnp.concatenate(
        [first + jnp.expand_dims(lower, axis), middle, last + jnp.expand_dims(upper, axis)], axis=axis
    )


def pad_pair(tiles, grad, rim_plans):
    column_plan, row_plan = rim_plans
    back_plans = (dict(column_plan, ends=True), dict(row_plan, ends=False))
    padded, grad_tiles = (None, None)
    for stage in range(2):
        plan = rim_plans[stage]
        sends_list = []
        if tiles is not None:
            edges = (tiles[:, :, 0], tiles[:, :, -1]) if stage == 0 else (tiles[:, 0], tiles[:, -1])
            sends_list.append(forward_sends(*edges))
        if grad is not None:
            grad_edges = (grad[:, :, 0], grad[:, :, -1]) if stage == 0 else (grad[:, 0], grad[:, -1])
            grad_sends, kept = backward_sends(*grad_edges, back_plans[stage])
            sends_list.append(grad_sends)
        received = exchange(sends_list, plan)
        if tiles is not None:
            lower_rim, upper_rim = forward_finish(received[0], *edges, plan)
            tiles = jnp.concatenate(
                [jnp.expand_dims(lower_rim, 2 - stage), tiles, jnp.expand_dims(upper_rim, 2 - stage)],
                axis=2 - stage,
            )
        if grad is not None:
            lower_grad, upper_grad = backward_finish(received[-1], kept)
            inner = grad[:, :, 1:-1] if stage == 0 else grad[:, 1:-1]
            grad = add_ends(inner, lower_grad, upper_grad, 2 - stage)
    return (tiles, grad)


def convolve(padded, weight):
    channels = weight.shape[-1]
    kernel = weight.reshape(3, 3, weight.shape[1], channels)
    return lax.conv_general_dilated(
        padded,
        kernel,
        (1, 1),
        "VALID",
        dimension_numbers=("NHWC", "HWIO", "NHWC"),
        preferred_element_type=jnp.float32,
    )


def convolve_back(grad, weight):
    kernel = weight.reshape(3, 3, weight.shape[1], weight.shape[2])[::-1, ::-1]
    return lax.conv_general_dilated(
        grad,
        kernel,
        (1, 1),
        ((2, 2), (2, 2)),
        dimension_numbers=("NHWC", "HWOI", "NHWC"),
        preferred_element_type=jnp.float32,
    )


def weight_grad(padded, grad):
    summed = lax.conv_general_dilated(
        padded,
        grad,
        (1, 1),
        "VALID",
        dimension_numbers=("CHWN", "IHWO", "HWNC"),
        preferred_element_type=jnp.float32,
    )
    return summed.reshape((9,) + summed.shape[2:])


def local(fields, weight_one, weight_two, cotangent, face_links, face_order):
    local_tiles = fields[0]
    face_count = local_tiles.shape[0]
    extent = local_tiles.shape[1]
    devices = lax.axis_size("tile")
    grid_side = math.isqrt(devices * face_count // 12)
    halves = devices // (grid_side * grid_side)
    levels = grid_side.bit_length() - 1
    device = lax.axis_index("tile")
    my_half = device // (grid_side * grid_side)
    grid_row = device // grid_side % grid_side
    grid_col = device % grid_side
    column_plan = make_plan(
        face_order,
        face_links,
        my_half,
        halves,
        face_count,
        grid_side,
        1,
        list(range(levels, 2 * levels)),
        (2, 3),
        grid_col,
        grid_row,
        False,
        2 * levels,
    )
    row_plan = make_plan(
        face_order,
        face_links,
        my_half,
        halves,
        face_count,
        grid_side,
        grid_side,
        list(range(levels)),
        (0, 1),
        grid_row,
        grid_col,
        True,
        2 * levels,
    )
    rim_plans = (column_plan, row_plan)
    grad_out = cotangent[0]
    rim_two = convolve_back(grad_out, weight_two).astype(jnp.bfloat16)
    rim_two = lax.optimization_barrier(rim_two)
    padded_in, grad_hidden = pad_pair(local_tiles, rim_two, rim_plans)
    pre_act = convolve(padded_in, weight_one)
    hidden = jax.nn.gelu(pre_act, approximate=True).astype(jnp.bfloat16)
    padded_hidden = pad_pair(hidden, None, rim_plans)[0]
    second = convolve(padded_hidden, weight_two)
    block_output = (local_tiles.astype(jnp.float32) + second).astype(jnp.bfloat16)
    grad_scale = 1.0 / math.sqrt(lax.axis_size("dp") * 12 * (grid_side * extent) ** 2)
    local_two = weight_grad(padded_hidden, grad_out)
    gelu_pair = jax.vjp(partial(jax.nn.gelu, approximate=True), pre_act)
    grad_pre = gelu_pair[1](grad_hidden)[0].astype(jnp.bfloat16)
    local_one = weight_grad(padded_in, grad_pre)
    rim_one = convolve_back(grad_pre, weight_one).astype(jnp.bfloat16)
    rim_one, local_one, local_two = lax.optimization_barrier((rim_one, local_one, local_two))
    field_grad = (grad_out.astype(jnp.float32) + pad_pair(None, rim_one, rim_plans)[1]).astype(jnp.bfloat16)
    grad_one, grad_two = lax.psum((local_one, local_two), ("tile", "dp"))
    grad_one, grad_two = (grad_one * grad_scale, grad_two * grad_scale)
    return (block_output[None], field_grad[None], grad_one, grad_two)


def solution(mesh):
    in_specs = (
        P("dp", "tile", None, None, None),
        P(),
        P(),
        P("dp", "tile", None, None, None),
        P(),
        P(),
    )
    out_specs = (P("dp", "tile", None, None, None), P("dp", "tile", None, None, None), P(), P())
    return jax.shard_map(local, mesh=mesh, in_specs=in_specs, out_specs=out_specs, check_vma=False)
```
